32 devices in a mesh: fiber: 2 (over x), chan: 16 (over z, y, core).
Axes of the slice: x: 2, y: 2, z: 4, core: 2. Of those that a mesh axis runs over, the one named last changes fastest.
Arguments:
- recording: bfloat16 [1024, 16384], P('fiber', 'chan'), parts along dimension 0, may hold values from -6 to 6
- source_index: int32 [1024], P('fiber'), parts along dimension 0, may hold values from 0 to 511
- channel_mask: int32 [1024], P(('fiber', 'chan')), parts along dimension 0, may hold values 0 or 1
Outputs:
- correlations: bfloat16 [1024, 512, 256], P('fiber', 'chan'), parts along dimension 0
The draws below stay inside these ranges and needn't reach their ends.
There are 2 independent parts, one for each index of `fiber`. The reference program is written for one: setup_inputs(seed, part) draws one part's arguments, and reference() takes and returns one part's arrays. A program takes and returns all parts, laid end to end along the dimension named above; each array names one. Nothing has to cross between parts.
Inputs may be any that keep to these rules, and one draw needn't show every extreme that they name: `source_index`: indices of virtual-source channels of this fiber; they may repeat and may name bad channels. `channel_mask`: one flag for each channel.
All inputs are finite; a program needn't handle non-finite values. No bound on the sum of `channel_mask` on one device may be relied on, other than what follows from the above.
Results may differ from the reference program's by a relative error of at most 0.0092.
Values may be sent and summed in bfloat16 or wider, within the bound.
No kernel may reach another device: no remote copies, remote signals or barrier semaphores. Data moves between devices by JAX's collectives and lax.ppermute only.
A program may use at most 128 MiB of HBM per device.

```python
import math
import jax
import jax.numpy as jnp
from jax import lax

CH_DEV = 32
SEGS = 8
NSEG = 512
NF = 192
FBASE = 4
LAGS = 256
TAPS = 64
SOURCES = 512
CHANNELS = 512
NT = 4096
RAW = 16384
N_CHAN = 16


def set_ends(drawn, key, least, top_value):
    longest = drawn.shape.index(max(drawn.shape))
    spots = []
    for shift in (0, 1):
        where = [jax.random.randint(jax.random.fold_in(key, axis), (), 0, length) for axis, length in enumerate(drawn.shape)]
        where[longest] = (where[longest] + shift) % drawn.shape[longest]
        spots.append(tuple(where))
    return drawn.at[spots[0]].set(least).at[spots[1]].set(top_value)


def levels(stream_key, shape, shards, least, largest):
    loudness = 1.0
    for axis_at, blocks in shards:
        heights = jax.random.uniform(jax.random.fold_in(jax.random.fold_in(stream_key, 6), axis_at), (blocks,), jnp.float32, least / len(shards), largest / len(shards))
        loudness = loudness * jnp.repeat(jnp.exp(heights), shape[axis_at] // blocks).reshape((-1,) + (1,) * (len(shape) - 1 - axis_at))
    return loudness


def gaussian(stream_key, extent, scale, bound, split=(), kind=jnp.bfloat16):
    values = jax.random.normal(stream_key, extent, jnp.float32) * scale
    if len(split) > 0:
        values = levels(stream_key, extent, split, -0.22, 0.18) * values
    return jnp.clip(values, min=-bound, max=bound).astype(kind)


def setup_inputs(seed: int = 0, part: int = 0) -> dict:
    splits = jax.random.split(jax.random.key(seed), 4)
    part_keys = jax.random.split(jax.random.fold_in(splits[3], part), 4)
    recording = gaussian(part_keys[0], (CHANNELS, RAW), 1.0, 6.0, ((1, 16),))
    source_index = set_ends(jax.random.randint(part_keys[1], (SOURCES,), 0, CHANNELS), jax.random.fold_in(part_keys[1], 1), 0, CHANNELS - 1).astype(jnp.int32)
    channel_mask = set_ends((jax.random.randint(part_keys[2], (CHANNELS,), 0, 8) < 7).astype(jnp.int32), jax.random.fold_in(part_keys[2], 1), 0, 1)
    return {"recording": recording, "source_index": source_index, "channel_mask": channel_mask}


def lowpass_taps():
    offsets = jnp.arange(TAPS, dtype=jnp.float32) - (TAPS - 1) / 2.0
    cutoff = 0.1
    window = 0.5 - 0.5 * jnp.cos(2.0 * math.pi * (jnp.arange(TAPS, dtype=jnp.float32) + 0.5) / TAPS)
    kernel = 2.0 * cutoff * jnp.sinc(2.0 * cutoff * offsets) * window
    kernel = kernel / jnp.sum(kernel)
    return kernel[::-1].astype(jnp.bfloat16)

def decimate(padded, reversed_taps, out_length):
    summed = jnp.zeros((padded.shape[0], out_length), jnp.float32)
    for stride in range(TAPS // 4):
        window_rows = padded[:, 4 * stride:4 * stride + 4 * out_length].reshape(padded.shape[0], out_length, 4)
        weights = reversed_taps[4 * stride:4 * stride + 4]
        summed = summed + jnp.einsum('ctq,q->ct', window_rows.astype(jnp.float32), weights.astype(jnp.float32))
    return summed.astype(jnp.bfloat16)

def fourier_table():
    sample = jnp.arange(NSEG, dtype=jnp.int32)[:, None]
    frequency = FBASE + jnp.arange(NF, dtype=jnp.int32)[None, :]
    angles = 2.0 * math.pi * (sample * frequency % NSEG).astype(jnp.float32) / NSEG
    return jnp.concatenate([jnp.cos(angles), -jnp.sin(angles)], axis=1).astype(jnp.bfloat16)

def delay_table():
    frequency = FBASE + jnp.arange(NF, dtype=jnp.int32)[:, None]
    delays = jnp.arange(LAGS, dtype=jnp.int32)[None, :] - LAGS // 2
    angles = 2.0 * math.pi * (frequency * delays % NSEG).astype(jnp.float32) / NSEG
    return jnp.concatenate([jnp.cos(angles), -jnp.sin(angles)], axis=0).astype(jnp.bfloat16)

def whiten(spectrum):
    real_part = spectrum[:, :NF]
    imag_part = spectrum[:, NF:]
    power = real_part * real_part + imag_part * imag_part
    average = lax.optimization_barrier(jnp.mean(power, axis=1, keepdims=True))
    factor = lax.rsqrt(power + 0.1 * average + 1e-05)
    return jnp.concatenate([real_part * factor, imag_part * factor], axis=1).astype(jnp.bfloat16)

def correlate(chosen, receivers, delays):
    source_real = chosen[..., :NF].astype(jnp.float32)
    source_imag = chosen[..., NF:].astype(jnp.float32)
    recv_real = receivers[..., :NF].astype(jnp.float32)
    recv_imag = receivers[..., NF:].astype(jnp.float32)
    cross_real = jnp.einsum('swf,rwf->srf', source_real, recv_real) + jnp.einsum('swf,rwf->srf', source_imag, recv_imag)
    cross_imag = jnp.einsum('swf,rwf->srf', source_imag, recv_real) - jnp.einsum('swf,rwf->srf', source_real, recv_imag)
    cross = jnp.concatenate([cross_real, cross_imag], axis=2).astype(jnp.bfloat16)
    source_count = chosen.shape[0]
    recv_count = receivers.shape[0]
    lagged = jnp.dot(cross.reshape(source_count * recv_count, 2 * NF), delays, preferred_element_type=jnp.float32)
    lagged = lagged.reshape(source_count, recv_count, LAGS) * (1.0 / math.sqrt(SEGS * NF))
    return lagged.astype(jnp.bfloat16)

def reference(recording, source_index, channel_mask):
    padded = jnp.pad(recording, ((0, 0), (TAPS - 4, 0)))
    decimated = decimate(padded, lowpass_taps(), NT)
    spectrum = jnp.dot(decimated.reshape(CHANNELS * SEGS, NSEG), fourier_table(), preferred_element_type=jnp.float32)
    whitened = whiten(spectrum).reshape(CHANNELS, SEGS, 2 * NF)
    whitened = whitened * channel_mask.astype(jnp.bfloat16)[:, None, None]
    chosen = jnp.take(whitened, source_index.astype(jnp.int32), axis=0)
    delays = delay_table()
    blocks = whitened.reshape(N_CHAN, CH_DEV, SEGS, 2 * NF)

    def one_group(receivers):
        return correlate(chosen, receivers, delays)
    result = lax.map(one_group, blocks)
    return result.transpose(1, 0, 2, 3).reshape(SOURCES, CHANNELS, LAGS)
```

```python
import math

import jax
import jax.numpy as jnp
from jax import lax
from jax.sharding import PartitionSpec as P

SEGS = 8
NSEG = 512
NF = 192
FBASE = 4
LAGS = 256
TAPS = 64
SOURCES = 512


def from_behind(block, axis, distance):
    devices = range(lax.axis_size(axis))
    route = [(i - distance, i) for i in devices if i - distance in devices]
    return lax.ppermute(block, axis, route)


def lowpass_taps():
    offsets = jnp.arange(TAPS, dtype=jnp.float32) - (TAPS - 1) / 2.0
    cutoff = 0.1
    window = 0.5 - 0.5 * jnp.cos(2.0 * math.pi * (jnp.arange(TAPS, dtype=jnp.float32) + 0.5) / TAPS)
    kernel = 2.0 * cutoff * jnp.sinc(2.0 * cutoff * offsets) * window
    kernel = kernel / jnp.sum(kernel)
    return kernel[::-1].astype(jnp.bfloat16)


def band_matrix(reversed_taps, rows, out_length):
    index = lax.broadcasted_iota(jnp.int32, (rows, out_length), 0) - 4 * lax.broadcasted_iota(
        jnp.int32, (rows, out_length), 1
    )
    inside = (index >= 0) & (index < TAPS)
    picked = jnp.take(reversed_taps, jnp.clip(index, 0, TAPS - 1), axis=0)
    return jnp.where(inside, picked, jnp.zeros_like(picked))


def decimate(earlier, recording, reversed_taps, out_length):
    head = earlier.shape[1]
    band = band_matrix(reversed_taps, head + recording.shape[1], out_length)
    summed = jnp.dot(earlier, band[:head], preferred_element_type=jnp.float32)
    summed = summed + jnp.dot(recording, band[head:], preferred_element_type=jnp.float32)
    return summed.astype(jnp.bfloat16)


def fourier_table():
    sample = jnp.arange(NSEG, dtype=jnp.int32)[:, None]
    frequency = FBASE + jnp.arange(NF, dtype=jnp.int32)[None, :]
    angles = 2.0 * math.pi * (sample * frequency % NSEG).astype(jnp.float32) / NSEG
    return jnp.concatenate([jnp.cos(angles), -jnp.sin(angles)], axis=1).astype(jnp.bfloat16)


def delay_table():
    frequency = FBASE + jnp.arange(NF, dtype=jnp.int32)[:, None]
    delays = jnp.arange(LAGS, dtype=jnp.int32)[None, :] - LAGS // 2
    angles = 2.0 * math.pi * (frequency * delays % NSEG).astype(jnp.float32) / NSEG
    return jnp.concatenate([jnp.cos(angles), -jnp.sin(angles)], axis=0).astype(jnp.bfloat16)


def whiten(spectrum):
    real_part = spectrum[:, :NF]
    imag_part = spectrum[:, NF:]
    power = real_part * real_part + imag_part * imag_part
    average = jnp.mean(power, axis=1, keepdims=True)
    factor = lax.rsqrt(power + 0.1 * average + 1e-05)
    return jnp.concatenate([real_part * factor, imag_part * factor], axis=1).astype(jnp.bfloat16)


def correlate(chosen, receivers, delays):
    source_real = chosen[..., :NF]
    source_imag = chosen[..., NF:]
    recv_real = receivers[..., :NF]
    recv_imag = receivers[..., NF:]
    cross_real = jnp.einsum(
        "swf,rwf->srf", source_real, recv_real, preferred_element_type=jnp.float32
    )
    cross_real = cross_real + jnp.einsum(
        "swf,rwf->srf", source_imag, recv_imag, preferred_element_type=jnp.float32
    )
    cross_imag = jnp.einsum(
        "swf,rwf->srf", source_imag, recv_real, preferred_element_type=jnp.float32
    )
    cross_imag = cross_imag - jnp.einsum(
        "swf,rwf->srf", source_real, recv_imag, preferred_element_type=jnp.float32
    )
    cross = jnp.concatenate([cross_real, cross_imag], axis=2).astype(jnp.bfloat16)
    source_count = chosen.shape[0]
    recv_count = receivers.shape[0]
    lagged = jnp.dot(
        cross.reshape(source_count * recv_count, 2 * NF), delays, preferred_element_type=jnp.float32
    )
    lagged = lagged.reshape(source_count, recv_count, LAGS) * (1.0 / math.sqrt(SEGS * NF))
    return lagged.astype(jnp.bfloat16)


def body(recording, source_index, channel_mask):
    channels, raw_count = recording.shape
    devices = lax.axis_size("chan")
    per_device = channels // devices
    dec_length = raw_count // 4
    trailing = recording[:, raw_count - (TAPS - 4) :]
    earlier = from_behind(trailing, "chan", 1)
    decimated = decimate(earlier, recording, lowpass_taps(), dec_length)
    grouped = decimated.reshape(devices, per_device, dec_length)
    fourier = fourier_table()
    block = lax.all_to_all(grouped, "chan", split_axis=0, concat_axis=2, tiled=True)
    members = block.shape[1]
    segments = block.reshape(members * SEGS, NSEG)
    spectrum = jnp.dot(segments, fourier, preferred_element_type=jnp.float32)
    whitened = whiten(spectrum).reshape(members, SEGS, 2 * NF)
    whitened = whitened * channel_mask.astype(jnp.bfloat16)[:, None, None]
    shard_rows = lax.all_gather(whitened, "chan", axis=0, tiled=True)
    row_count = shard_rows.shape[0]
    chosen = jnp.take(shard_rows, jnp.clip(source_index, 0, row_count - 1), axis=0)
    result = correlate(chosen, whitened, delay_table())
    return result.reshape(SOURCES, per_device, LAGS)


def solution(mesh):
    placed = (P("fiber", "chan"), P("fiber"), P(("fiber", "chan")))
    return jax.shard_map(
        body, mesh=mesh, in_specs=placed, out_specs=P("fiber", "chan", None), check_vma=False
    )
```

```python
import math

import jax
import jax.numpy as jnp
import numpy as np
from jax import lax
from jax.experimental import pallas as pl
from jax.experimental.pallas import tpu as pltpu
from jax.sharding import PartitionSpec as P

SEGS = 8
NSEG = 512
NF = 192
FBASE = 4
LAGS = 256
TAPS = 64
SOURCES = 512


def from_behind(block, axis, distance):
    devices = range(lax.axis_size(axis))
    route = [(i - distance, i) for i in devices if i - distance in devices]
    return lax.ppermute(block, axis, route)


def lowpass_taps():
    offsets = jnp.arange(TAPS, dtype=jnp.float32) - (TAPS - 1) / 2.0
    cutoff = 0.1
    window = 0.5 - 0.5 * jnp.cos(2.0 * math.pi * (jnp.arange(TAPS, dtype=jnp.float32) + 0.5) / TAPS)
    kernel = 2.0 * cutoff * jnp.sinc(2.0 * cutoff * offsets) * window
    kernel = kernel / jnp.sum(kernel)
    return kernel[::-1].astype(jnp.bfloat16)


def band_matrix(rows, out_length):
    with jax.ensure_compile_time_eval():
        reversed_taps = np.asarray(lowpass_taps().astype(jnp.float32))
    index = np.arange(rows)[:, None] - 4 * np.arange(out_length)[None, :]
    inside = (index >= 0) & (index < TAPS)
    band = np.where(inside, reversed_taps[np.clip(index, 0, TAPS - 1)], 0.0)
    return jnp.asarray(band.astype(np.float32)).astype(jnp.bfloat16)


def decimate(earlier, recording, out_length):
    head = earlier.shape[1]
    band = band_matrix(head + recording.shape[1], out_length)
    summed = jnp.dot(earlier, band[:head], preferred_element_type=jnp.float32)
    summed = summed + jnp.dot(recording, band[head:], preferred_element_type=jnp.float32)
    return summed.astype(jnp.bfloat16)


def fourier_table():
    sample = jnp.arange(NSEG, dtype=jnp.int32)[:, None]
    frequency = FBASE + jnp.arange(NF, dtype=jnp.int32)[None, :]
    angles = 2.0 * math.pi * (sample * frequency % NSEG).astype(jnp.float32) / NSEG
    return jnp.concatenate([jnp.cos(angles), -jnp.sin(angles)], axis=1).astype(jnp.bfloat16)


def delay_table():
    frequency = FBASE + jnp.arange(NF, dtype=jnp.int32)[:, None]
    delays = jnp.arange(LAGS, dtype=jnp.int32)[None, :] - LAGS // 2
    angles = 2.0 * math.pi * (frequency * delays % NSEG).astype(jnp.float32) / NSEG
    return jnp.concatenate([jnp.cos(angles), -jnp.sin(angles)], axis=0).astype(jnp.bfloat16)


def whiten(spectrum):
    real_part = spectrum[:, :NF]
    imag_part = spectrum[:, NF:]
    power = real_part * real_part + imag_part * imag_part
    average = jnp.mean(power, axis=1, keepdims=True)
    factor = lax.rsqrt(power + 0.1 * average + 1e-05)
    return jnp.concatenate([real_part * factor, imag_part * factor], axis=1).astype(jnp.bfloat16)


def correlate_kernel(source_ref, plain_ref, swapped_ref, delays_ref, out_ref, cross_ref):
    block = source_ref.shape[0]
    receivers = plain_ref.shape[1]

    def one_source(s, carry):
        source = source_ref[s].astype(jnp.float32)
        direct = jnp.zeros((receivers, 2 * NF), jnp.float32)
        crossed = jnp.zeros((receivers, 2 * NF), jnp.float32)
        for w in range(SEGS):
            row = source[w : w + 1, :]
            direct = direct + row * plain_ref[w]
            crossed = crossed + row * swapped_ref[w]
        cross = direct - pltpu.roll(crossed, NF, 1)
        start = pl.multiple_of(s * receivers, receivers)
        cross_ref[pl.ds(start, receivers), :] = cross.astype(jnp.bfloat16)
        return carry

    lax.fori_loop(0, block, one_source, 0, unroll=True)
    lagged = jnp.dot(cross_ref[...], delays_ref[...], preferred_element_type=jnp.float32)
    lagged = lagged * (1.0 / math.sqrt(SEGS * NF))
    out_ref[...] = lagged.astype(jnp.bfloat16).reshape(out_ref.shape)


def correlate(chosen, receivers, delays, block=32):
    source_count = chosen.shape[0]
    recv_count = receivers.shape[0]
    spectra = receivers.astype(jnp.float32).transpose(1, 0, 2)
    real_part = spectra[..., :NF]
    imag_part = spectra[..., NF:]
    plain = jnp.concatenate([real_part, real_part], axis=-1)
    swapped = jnp.concatenate([imag_part, -imag_part], axis=-1)
    return pl.pallas_call(
        correlate_kernel,
        grid=(source_count // block,),
        in_specs=[
            pl.BlockSpec((block, SEGS, 2 * NF), lambda i: (i, 0, 0)),
            pl.BlockSpec((SEGS, recv_count, 2 * NF), lambda i: (0, 0, 0)),
            pl.BlockSpec((SEGS, recv_count, 2 * NF), lambda i: (0, 0, 0)),
            pl.BlockSpec((2 * NF, LAGS), lambda i: (0, 0)),
        ],
        out_specs=pl.BlockSpec((block, recv_count, LAGS), lambda i: (i, 0, 0)),
        out_shape=jax.ShapeDtypeStruct((source_count, recv_count, LAGS), jnp.bfloat16),
        scratch_shapes=[pltpu.VMEM((block * recv_count, 2 * NF), jnp.bfloat16)],
    )(chosen, plain, swapped, delays)


def body(recording, source_index, channel_mask):
    channels, raw_count = recording.shape
    devices = lax.axis_size("chan")
    per_device = channels // devices
    dec_length = raw_count // 4
    trailing = recording[:, raw_count - (TAPS - 4) :]
    earlier = from_behind(trailing, "chan", 1)
    decimated = decimate(earlier, recording, dec_length)
    grouped = decimated.reshape(devices, per_device, dec_length)
    fourier = fourier_table()
    block = lax.all_to_all(grouped, "chan", split_axis=0, concat_axis=2, tiled=True)
    members = block.shape[1]
    segments = block.reshape(members * SEGS, NSEG)
    spectrum = jnp.dot(segments, fourier, preferred_element_type=jnp.float32)
    whitened = whiten(spectrum).reshape(members, SEGS, 2 * NF)
    whitened = whitened * channel_mask.astype(jnp.bfloat16)[:, None, None]
    shard_rows = lax.all_gather(whitened, "chan", axis=0, tiled=True)
    row_count = shard_rows.shape[0]
    chosen = jnp.take(shard_rows, jnp.clip(source_index, 0, row_count - 1), axis=0, mode="clip")
    result = correlate(chosen, whitened, delay_table())
    return result.reshape(SOURCES, per_device, LAGS)


def solution(mesh):
    placed = (P("fiber", "chan"), P("fiber"), P(("fiber", "chan")))
    return jax.shard_map(
        body, mesh=mesh, in_specs=placed, out_specs=P("fiber", "chan", None), check_vma=False
    )
```

```python
import math

import jax
import jax.numpy as jnp
import numpy as np
from jax import lax
from jax.experimental import pallas as pl
from jax.experimental.pallas import tpu as pltpu
from jax.sharding import PartitionSpec as P

SEGS = 8
NSEG = 512
NF = 192
FBASE = 4
LAGS = 256
TAPS = 64
SOURCES = 512


def from_behind(block, axis, distance):
    devices = range(lax.axis_size(axis))
    route = [(i - distance, i) for i in devices if i - distance in devices]
    return lax.ppermute(block, axis, route)


def lowpass_taps():
    offsets = jnp.arange(TAPS, dtype=jnp.float32) - (TAPS - 1) / 2.0
    cutoff = 0.1
    window = 0.5 - 0.5 * jnp.cos(2.0 * math.pi * (jnp.arange(TAPS, dtype=jnp.float32) + 0.5) / TAPS)
    kernel = 2.0 * cutoff * jnp.sinc(2.0 * cutoff * offsets) * window
    kernel = kernel / jnp.sum(kernel)
    return kernel[::-1].astype(jnp.bfloat16)


def band_matrix(rows, out_length):
    with jax.ensure_compile_time_eval():
        reversed_taps = np.asarray(lowpass_taps().astype(jnp.float32))
    index = np.arange(rows)[:, None] - 4 * np.arange(out_length)[None, :]
    inside = (index >= 0) & (index < TAPS)
    band = np.where(inside, reversed_taps[np.clip(index, 0, TAPS - 1)], 0.0)
    return jnp.asarray(band.astype(np.float32)).astype(jnp.bfloat16)


def decimate(earlier, recording, out_length):
    head = earlier.shape[1]
    band = band_matrix(head + recording.shape[1], out_length)
    summed = jnp.dot(earlier, band[:head], preferred_element_type=jnp.float32)
    summed = summed + jnp.dot(recording, band[head:], preferred_element_type=jnp.float32)
    return summed.astype(jnp.bfloat16)


def fourier_table():
    sample = jnp.arange(NSEG, dtype=jnp.int32)[:, None]
    frequency = FBASE + jnp.arange(NF, dtype=jnp.int32)[None, :]
    angles = 2.0 * math.pi * (sample * frequency % NSEG).astype(jnp.float32) / NSEG
    return jnp.concatenate([jnp.cos(angles), -jnp.sin(angles)], axis=1).astype(jnp.bfloat16)


def delay_table():
    frequency = FBASE + jnp.arange(NF, dtype=jnp.int32)[:, None]
    delays = jnp.arange(LAGS, dtype=jnp.int32)[None, :] - LAGS // 2
    angles = 2.0 * math.pi * (frequency * delays % NSEG).astype(jnp.float32) / NSEG
    return jnp.concatenate([jnp.cos(angles), -jnp.sin(angles)], axis=0).astype(jnp.bfloat16)


def whiten(spectrum):
    real_part = spectrum[:, :NF]
    imag_part = spectrum[:, NF:]
    power = real_part * real_part + imag_part * imag_part
    average = jnp.mean(power, axis=1, keepdims=True)
    factor = lax.rsqrt(power + 0.1 * average + 1e-05)
    return jnp.concatenate([real_part * factor, imag_part * factor], axis=1).astype(jnp.bfloat16)


def correlate_kernel(source_ref, plain_ref, swapped_ref, delays_ref, out_ref, cross_ref):
    block = source_ref.shape[1]
    receivers = plain_ref.shape[1]

    def one_source(s, carry):
        direct = jnp.zeros((receivers, 2 * NF), jnp.float32)
        crossed = jnp.zeros((receivers, 2 * NF), jnp.float32)
        for w in range(SEGS):
            row = source_ref[w, pl.ds(s, 1), :].astype(jnp.float32)
            direct = direct + row * plain_ref[w]
            crossed = crossed + row * swapped_ref[w]
        cross = direct - pltpu.roll(crossed, NF, 1)
        start = pl.multiple_of(s * receivers, receivers)
        cross_ref[pl.ds(start, receivers), :] = cross.astype(jnp.bfloat16)
        return carry

    lax.fori_loop(0, block, one_source, 0, unroll=True)
    lagged = jnp.dot(cross_ref[...], delays_ref[...], preferred_element_type=jnp.float32)
    lagged = lagged * (1.0 / math.sqrt(SEGS * NF))
    out_ref[...] = lagged.astype(jnp.bfloat16).reshape(out_ref.shape)


def correlate(chosen, receivers, delays, block=32):
    source_count = chosen.shape[1]
    recv_count = receivers.shape[0]
    spectra = receivers.astype(jnp.float32).transpose(1, 0, 2)
    real_part = spectra[..., :NF]
    imag_part = spectra[..., NF:]
    plain = jnp.concatenate([real_part, real_part], axis=-1)
    swapped = jnp.concatenate([imag_part, -imag_part], axis=-1)
    return pl.pallas_call(
        correlate_kernel,
        grid=(source_count // block,),
        in_specs=[
            pl.BlockSpec((SEGS, block, 2 * NF), lambda i: (0, i, 0)),
            pl.BlockSpec((SEGS, recv_count, 2 * NF), lambda i: (0, 0, 0)),
            pl.BlockSpec((SEGS, recv_count, 2 * NF), lambda i: (0, 0, 0)),
            pl.BlockSpec((2 * NF, LAGS), lambda i: (0, 0)),
        ],
        out_specs=pl.BlockSpec((block, recv_count, LAGS), lambda i: (i, 0, 0)),
        out_shape=jax.ShapeDtypeStruct((source_count, recv_count, LAGS), jnp.bfloat16),
        scratch_shapes=[pltpu.VMEM((block * recv_count, 2 * NF), jnp.bfloat16)],
    )(chosen, plain, swapped, delays)


def body(recording, source_index, channel_mask):
    channels, raw_count = recording.shape
    devices = lax.axis_size("chan")
    per_device = channels // devices
    dec_length = raw_count // 4
    trailing = recording[:, raw_count - (TAPS - 4) :]
    earlier = from_behind(trailing, "chan", 1)
    decimated = decimate(earlier, recording, dec_length)
    grouped = decimated.reshape(devices, per_device, dec_length)
    fourier = fourier_table()
    block = lax.all_to_all(grouped, "chan", split_axis=0, concat_axis=2, tiled=True)
    members = block.shape[1]
    segments = block.reshape(members * SEGS, NSEG)
    spectrum = jnp.dot(segments, fourier, preferred_element_type=jnp.float32)
    whitened = whiten(spectrum).reshape(members, SEGS, 2 * NF)
    whitened = whitened * channel_mask.astype(jnp.bfloat16)[:, None, None]
    half = members // 2
    delays = delay_table()
    parts = []
    for rows in (whitened[:half], whitened[half:]):
        gathered = lax.all_gather(rows, "chan", axis=0, tiled=True)
        parts.append(correlate(gathered.transpose(1, 0, 2), whitened, delays))
    table = jnp.concatenate(parts, axis=0)
    channel = jnp.clip(source_index, 0, devices * members - 1)
    owner = channel // members
    local = channel % members
    position = jnp.where(
        local < half, owner * half + local, devices * half + owner * (members - half) + local - half
    )
    result = jnp.take(table, position, axis=0, mode="clip")
    return result.reshape(SOURCES, per_device, LAGS)


def solution(mesh):
    placed = (P("fiber", "chan"), P("fiber"), P(("fiber", "chan")))
    return jax.shard_map(
        body, mesh=mesh, in_specs=placed, out_specs=P("fiber", "chan", None), check_vma=False
    )
```

```python
import math

import jax
import jax.numpy as jnp
import numpy as np
from jax import lax
from jax.experimental import pallas as pl
from jax.experimental.pallas import tpu as pltpu
from jax.sharding import PartitionSpec as P

SEGS = 8
NSEG = 512
NF = 192
FBASE = 4
LAGS = 256
TAPS = 64
SOURCES = 512


def from_behind(block, axis, distance):
    devices = range(lax.axis_size(axis))
    route = [(i - distance, i) for i in devices if i - distance in devices]
    return lax.ppermute(block, axis, route)


def lowpass_taps():
    offsets = jnp.arange(TAPS, dtype=jnp.float32) - (TAPS - 1) / 2.0
    cutoff = 0.1
    window = 0.5 - 0.5 * jnp.cos(2.0 * math.pi * (jnp.arange(TAPS, dtype=jnp.float32) + 0.5) / TAPS)
    kernel = 2.0 * cutoff * jnp.sinc(2.0 * cutoff * offsets) * window
    kernel = kernel / jnp.sum(kernel)
    return kernel[::-1].astype(jnp.bfloat16)


def band_matrix(rows, out_length):
    with jax.ensure_compile_time_eval():
        reversed_taps = np.asarray(lowpass_taps().astype(jnp.float32))
    index = np.arange(rows)[:, None] - 4 * np.arange(out_length)[None, :]
    inside = (index >= 0) & (index < TAPS)
    band = np.where(inside, reversed_taps[np.clip(index, 0, TAPS - 1)], 0.0)
    return jnp.asarray(band.astype(np.float32)).astype(jnp.bfloat16)


def decimate(earlier, recording, out_length):
    head = earlier.shape[1]
    band = band_matrix(head + recording.shape[1], out_length)
    summed = jnp.dot(earlier, band[:head], preferred_element_type=jnp.float32)
    summed = summed + jnp.dot(recording, band[head:], preferred_element_type=jnp.float32)
    return summed.astype(jnp.bfloat16)


def fourier_table():
    sample = jnp.arange(NSEG, dtype=jnp.int32)[:, None]
    frequency = FBASE + jnp.arange(NF, dtype=jnp.int32)[None, :]
    angles = 2.0 * math.pi * (sample * frequency % NSEG).astype(jnp.float32) / NSEG
    return jnp.concatenate([jnp.cos(angles), -jnp.sin(angles)], axis=1).astype(jnp.bfloat16)


def delay_table():
    frequency = FBASE + jnp.arange(NF, dtype=jnp.int32)[:, None]
    delays = jnp.arange(LAGS, dtype=jnp.int32)[None, :] - LAGS // 2
    angles = 2.0 * math.pi * (frequency * delays % NSEG).astype(jnp.float32) / NSEG
    return jnp.concatenate([jnp.cos(angles), -jnp.sin(angles)], axis=0).astype(jnp.bfloat16)


def whiten(spectrum):
    real_part = spectrum[:, :NF]
    imag_part = spectrum[:, NF:]
    power = real_part * real_part + imag_part * imag_part
    average = jnp.mean(power, axis=1, keepdims=True)
    factor = lax.rsqrt(power + 0.1 * average + 1e-05)
    return jnp.concatenate([real_part * factor, imag_part * factor], axis=1).astype(jnp.bfloat16)


def correlate_kernel(source_ref, plain_ref, swapped_ref, delays_ref, out_ref, cross_ref):
    block = source_ref.shape[1]
    receivers = plain_ref.shape[1]

    def one_source(s, carry):
        direct = jnp.zeros((receivers, 2 * NF), jnp.float32)
        crossed = jnp.zeros((receivers, 2 * NF), jnp.float32)
        for w in range(SEGS):
            row = source_ref[w, pl.ds(s, 1), :].astype(jnp.float32)
            direct = direct + row * plain_ref[w]
            crossed = crossed + row * swapped_ref[w]
        cross = direct - pltpu.roll(crossed, NF, 1)
        start = pl.multiple_of(s * receivers, receivers)
        cross_ref[pl.ds(start, receivers), :] = cross.astype(jnp.bfloat16)
        return carry

    lax.fori_loop(0, block, one_source, 0, unroll=True)
    lagged = jnp.dot(cross_ref[...], delays_ref[...], preferred_element_type=jnp.float32)
    lagged = lagged * (1.0 / math.sqrt(SEGS * NF))
    out_ref[...] = lagged.astype(jnp.bfloat16).reshape(out_ref.shape)


def correlate(chosen, receivers, delays, block=32):
    source_count = chosen.shape[1]
    recv_count = receivers.shape[1]
    spectra = receivers.astype(jnp.float32)
    real_part = spectra[..., :NF]
    imag_part = spectra[..., NF:]
    plain = jnp.concatenate([real_part, real_part], axis=-1)
    swapped = jnp.concatenate([imag_part, -imag_part], axis=-1)
    return pl.pallas_call(
        correlate_kernel,
        grid=(source_count // block,),
        in_specs=[
            pl.BlockSpec((SEGS, block, 2 * NF), lambda i: (0, i, 0)),
            pl.BlockSpec((SEGS, recv_count, 2 * NF), lambda i: (0, 0, 0)),
            pl.BlockSpec((SEGS, recv_count, 2 * NF), lambda i: (0, 0, 0)),
            pl.BlockSpec((2 * NF, LAGS), lambda i: (0, 0)),
        ],
        out_specs=pl.BlockSpec((block, recv_count, LAGS), lambda i: (i, 0, 0)),
        out_shape=jax.ShapeDtypeStruct((source_count, recv_count, LAGS), jnp.bfloat16),
        scratch_shapes=[pltpu.VMEM((block * recv_count, 2 * NF), jnp.bfloat16)],
    )(chosen, plain, swapped, delays)


def body(recording, source_index, channel_mask):
    channels, raw_count = recording.shape
    devices = lax.axis_size("chan")
    me = lax.axis_index("chan")
    per_device = channels // devices
    dec_length = raw_count // 4
    sharing = devices // SEGS
    span = channels // sharing
    trailing = recording[:, raw_count - (TAPS - 4) :]
    earlier = from_behind(trailing, "chan", 1)
    decimated = decimate(earlier, recording, dec_length)
    slot = me % sharing
    rows = lax.dynamic_slice_in_dim(fourier_table(), slot * dec_length, dec_length, axis=0)
    partial = jnp.dot(decimated, rows, preferred_element_type=jnp.float32)
    pieces = partial.reshape(sharing, span, 2 * NF)
    spectrum = lax.dynamic_index_in_dim(pieces, slot, 0, keepdims=False)
    for step in range(1, sharing):
        route = [
            (group * sharing + i, group * sharing + (i + step) % sharing)
            for group in range(devices // sharing)
            for i in range(sharing)
        ]
        outgoing = lax.dynamic_index_in_dim(pieces, (slot + step) % sharing, 0, keepdims=False)
        spectrum = spectrum + lax.ppermute(outgoing, "chan", route)
    whitened = whiten(spectrum)
    flags = channel_mask.astype(jnp.bfloat16)
    flag_rows = jnp.zeros((16, 2 * NF), jnp.bfloat16).at[0, :per_device].set(flags)
    piece = jnp.concatenate([whitened, flag_rows], axis=0)
    gathered = lax.all_gather(piece, "chan", axis=0, tiled=False)
    table = gathered[:, :span].reshape(SEGS, channels, 2 * NF)
    flags_all = gathered[:, span, :per_device].reshape(channels)
    receivers = lax.dynamic_slice_in_dim(table, me * per_device, per_device, axis=1)
    receivers = receivers * flags[None, :, None]
    picked = jnp.clip(source_index, 0, channels - 1)
    chosen = jnp.take(table, picked, axis=1, mode="clip")
    chosen = chosen * jnp.take(flags_all, picked, mode="clip")[None, :, None]
    result = correlate(chosen, receivers, delay_table())
    return result.reshape(SOURCES, per_device, LAGS)


def solution(mesh):
    placed = (P("fiber", "chan"), P("fiber"), P(("fiber", "chan")))
    return jax.shard_map(
        body, mesh=mesh, in_specs=placed, out_specs=P("fiber", "chan", None), check_vma=False
    )
```

```python
import math

import jax
import jax.numpy as jnp
import numpy as np
from jax import lax
from jax.experimental import pallas as pl
from jax.experimental.pallas import tpu as pltpu
from jax.sharding import PartitionSpec as P

SEGS = 8
NSEG = 512
NF = 192
FBASE = 4
LAGS = 256
TAPS = 64
SOURCES = 512


def from_behind(block, axis, distance):
    devices = range(lax.axis_size(axis))
    route = [(i - distance, i) for i in devices if i - distance in devices]
    return lax.ppermute(block, axis, route)


def lowpass_taps():
    offsets = jnp.arange(TAPS, dtype=jnp.float32) - (TAPS - 1) / 2.0
    cutoff = 0.1
    window = 0.5 - 0.5 * jnp.cos(2.0 * math.pi * (jnp.arange(TAPS, dtype=jnp.float32) + 0.5) / TAPS)
    kernel = 2.0 * cutoff * jnp.sinc(2.0 * cutoff * offsets) * window
    kernel = kernel / jnp.sum(kernel)
    return kernel[::-1].astype(jnp.bfloat16)


def band_matrix(rows, out_length):
    with jax.ensure_compile_time_eval():
        reversed_taps = np.asarray(lowpass_taps().astype(jnp.float32))
    index = np.arange(rows)[:, None] - 4 * np.arange(out_length)[None, :]
    inside = (index >= 0) & (index < TAPS)
    band = np.where(inside, reversed_taps[np.clip(index, 0, TAPS - 1)], 0.0)
    return jnp.asarray(band.astype(np.float32)).astype(jnp.bfloat16)


def decimate(earlier, recording, out_length):
    head = earlier.shape[1]
    band = band_matrix(head + recording.shape[1], out_length)
    summed = jnp.dot(earlier, band[:head], preferred_element_type=jnp.float32)
    summed = summed + jnp.dot(recording, band[head:], preferred_element_type=jnp.float32)
    return summed.astype(jnp.bfloat16)


def fourier_table():
    sample = jnp.arange(NSEG, dtype=jnp.int32)[:, None]
    frequency = FBASE + jnp.arange(NF, dtype=jnp.int32)[None, :]
    angles = 2.0 * math.pi * (sample * frequency % NSEG).astype(jnp.float32) / NSEG
    return jnp.concatenate([jnp.cos(angles), -jnp.sin(angles)], axis=1).astype(jnp.bfloat16)


def delay_table():
    frequency = FBASE + jnp.arange(NF, dtype=jnp.int32)[:, None]
    delays = jnp.arange(LAGS, dtype=jnp.int32)[None, :] - LAGS // 2
    angles = 2.0 * math.pi * (frequency * delays % NSEG).astype(jnp.float32) / NSEG
    return jnp.concatenate([jnp.cos(angles), -jnp.sin(angles)], axis=0).astype(jnp.bfloat16)


def whiten(spectrum):
    real_part = spectrum[:, :NF]
    imag_part = spectrum[:, NF:]
    power = real_part * real_part + imag_part * imag_part
    average = jnp.mean(power, axis=1, keepdims=True)
    factor = lax.rsqrt(power + 0.1 * average + 1e-05)
    return jnp.concatenate([real_part * factor, imag_part * factor], axis=1).astype(jnp.bfloat16)


def correlate_kernel(flags_ref, source_ref, plain_ref, swapped_ref, delays_ref, out_ref, cross_ref):
    block = source_ref.shape[1]
    receivers = plain_ref.shape[1]

    def one_source(s, carry):
        direct = jnp.zeros((receivers, 2 * NF), jnp.float32)
        crossed = jnp.zeros((receivers, 2 * NF), jnp.float32)
        for w in range(SEGS):
            row = source_ref[w, pl.ds(s, 1), :].astype(jnp.float32)
            direct = direct + row * plain_ref[w]
            crossed = crossed + row * swapped_ref[w]
        flag = flags_ref[pl.program_id(0) * block + s].astype(jnp.float32)
        cross = (direct - pltpu.roll(crossed, NF, 1)) * flag
        start = pl.multiple_of(s * receivers, receivers)
        cross_ref[pl.ds(start, receivers), :] = cross.astype(jnp.bfloat16)
        return carry

    lax.fori_loop(0, block, one_source, 0, unroll=True)
    lagged = jnp.dot(cross_ref[...], delays_ref[...], preferred_element_type=jnp.float32)
    lagged = lagged * (1.0 / math.sqrt(SEGS * NF))
    out_ref[...] = lagged.astype(jnp.bfloat16).reshape(out_ref.shape)


def correlate(chosen, source_flags, receivers, delays, block=32):
    source_count = chosen.shape[1]
    recv_count = receivers.shape[1]
    spectra = receivers.astype(jnp.float32)
    real_part = spectra[..., :NF]
    imag_part = spectra[..., NF:]
    plain = jnp.concatenate([real_part, real_part], axis=-1)
    swapped = jnp.concatenate([imag_part, -imag_part], axis=-1)
    grid_spec = pltpu.PrefetchScalarGridSpec(
        num_scalar_prefetch=1,
        grid=(source_count // block,),
        in_specs=[
            pl.BlockSpec((SEGS, block, 2 * NF), lambda i, flags: (0, i, 0)),
            pl.BlockSpec((SEGS, recv_count, 2 * NF), lambda i, flags: (0, 0, 0)),
            pl.BlockSpec((SEGS, recv_count, 2 * NF), lambda i, flags: (0, 0, 0)),
            pl.BlockSpec((2 * NF, LAGS), lambda i, flags: (0, 0)),
        ],
        out_specs=pl.BlockSpec((block, recv_count, LAGS), lambda i, flags: (i, 0, 0)),
        scratch_shapes=[pltpu.VMEM((block * recv_count, 2 * NF), jnp.bfloat16)],
    )
    return pl.pallas_call(
        correlate_kernel,
        grid_spec=grid_spec,
        out_shape=jax.ShapeDtypeStruct((source_count, recv_count, LAGS), jnp.bfloat16),
    )(source_flags, chosen, plain, swapped, delays)


def body(recording, source_index, channel_mask):
    channels, raw_count = recording.shape
    devices = lax.axis_size("chan")
    me = lax.axis_index("chan")
    per_device = channels // devices
    dec_length = raw_count // 4
    sharing = devices // SEGS
    span = channels // sharing
    trailing = recording[:, raw_count - (TAPS - 4) :]
    earlier = from_behind(trailing, "chan", 1)
    decimated = decimate(earlier, recording, dec_length)
    slot = me % sharing
    rows = lax.dynamic_slice_in_dim(fourier_table(), slot * dec_length, dec_length, axis=0)
    partial = jnp.dot(decimated, rows, preferred_element_type=jnp.float32)
    pieces = partial.reshape(sharing, span, 2 * NF)
    spectrum = lax.dynamic_index_in_dim(pieces, slot, 0, keepdims=False)
    for step in range(1, sharing):
        route = [
            (group * sharing + i, group * sharing + (i + step) % sharing)
            for group in range(devices // sharing)
            for i in range(sharing)
        ]
        outgoing = lax.dynamic_index_in_dim(pieces, (slot + step) % sharing, 0, keepdims=False)
        spectrum = spectrum + lax.ppermute(outgoing, "chan", route)
    whitened = whiten(spectrum)
    flags = channel_mask.astype(jnp.bfloat16)
    flag_rows = jnp.zeros((16, 2 * NF), jnp.bfloat16).at[0, :per_device].set(flags)
    piece = jnp.concatenate([whitened, flag_rows], axis=0)
    gathered = lax.all_gather(piece, "chan", axis=0, tiled=True)
    height = piece.shape[0]
    segment_base = jnp.arange(SEGS, dtype=jnp.int32)[:, None] * (sharing * height)
    picked = jnp.clip(source_index, 0, channels - 1)
    source_rows = segment_base + (picked // span * height + picked % span)[None, :]
    chosen = jnp.take(gathered, source_rows, axis=0, mode="clip")
    flag_rows_at = jnp.arange(devices, dtype=jnp.int32) * height + span
    flags_all = jnp.take(gathered, flag_rows_at, axis=0, mode="clip")[:, :per_device]
    source_flags = jnp.take(flags_all.reshape(channels), picked, mode="clip")
    own = me * per_device + jnp.arange(per_device, dtype=jnp.int32)
    receiver_rows = segment_base + (own // span * height + own % span)[None, :]
    receivers = jnp.take(gathered, receiver_rows, axis=0, mode="clip")
    receivers = receivers * flags[None, :, None]
    result = correlate(chosen, source_flags.astype(jnp.int32), receivers, delay_table())
    return result.reshape(SOURCES, per_device, LAGS)


def solution(mesh):
    placed = (P("fiber", "chan"), P("fiber"), P(("fiber", "chan")))
    return jax.shard_map(
        body, mesh=mesh, in_specs=placed, out_specs=P("fiber", "chan", None), check_vma=False
    )
```

```python
import math

import jax
import jax.numpy as jnp
import numpy as np
from jax import lax
from jax.experimental import pallas as pl
from jax.experimental.pallas import tpu as pltpu
from jax.sharding import PartitionSpec as P

SEGS = 8
NSEG = 512
NF = 192
FBASE = 4
LAGS = 256
TAPS = 64
SOURCES = 512


def from_behind(block, axis, distance):
    devices = range(lax.axis_size(axis))
    route = [(i - distance, i) for i in devices if i - distance in devices]
    return lax.ppermute(block, axis, route)


def lowpass_taps():
    offsets = jnp.arange(TAPS, dtype=jnp.float32) - (TAPS - 1) / 2.0
    cutoff = 0.1
    window = 0.5 - 0.5 * jnp.cos(2.0 * math.pi * (jnp.arange(TAPS, dtype=jnp.float32) + 0.5) / TAPS)
    kernel = 2.0 * cutoff * jnp.sinc(2.0 * cutoff * offsets) * window
    kernel = kernel / jnp.sum(kernel)
    return kernel[::-1].astype(jnp.bfloat16)


def band_matrix(rows, out_length):
    with jax.ensure_compile_time_eval():
        reversed_taps = np.asarray(lowpass_taps().astype(jnp.float32))
    index = np.arange(rows)[:, None] - 4 * np.arange(out_length)[None, :]
    inside = (index >= 0) & (index < TAPS)
    band = np.where(inside, reversed_taps[np.clip(index, 0, TAPS - 1)], 0.0)
    return jnp.asarray(band.astype(np.float32)).astype(jnp.bfloat16)


def decimate(earlier, recording, out_length):
    head = earlier.shape[1]
    band = band_matrix(head + recording.shape[1], out_length)
    summed = jnp.dot(earlier, band[:head], preferred_element_type=jnp.float32)
    summed = summed + jnp.dot(recording, band[head:], preferred_element_type=jnp.float32)
    return summed.astype(jnp.bfloat16)


def fourier_table():
    sample = jnp.arange(NSEG, dtype=jnp.int32)[:, None]
    frequency = FBASE + jnp.arange(NF, dtype=jnp.int32)[None, :]
    angles = 2.0 * math.pi * (sample * frequency % NSEG).astype(jnp.float32) / NSEG
    return jnp.concatenate([jnp.cos(angles), -jnp.sin(angles)], axis=1).astype(jnp.bfloat16)


def delay_table():
    frequency = FBASE + jnp.arange(NF, dtype=jnp.int32)[:, None]
    delays = jnp.arange(LAGS, dtype=jnp.int32)[None, :] - LAGS // 2
    angles = 2.0 * math.pi * (frequency * delays % NSEG).astype(jnp.float32) / NSEG
    return jnp.concatenate([jnp.cos(angles), -jnp.sin(angles)], axis=0).astype(jnp.bfloat16)


def whiten(spectrum):
    real_part = spectrum[:, :NF]
    imag_part = spectrum[:, NF:]
    power = real_part * real_part + imag_part * imag_part
    average = jnp.mean(power, axis=1, keepdims=True)
    factor = lax.rsqrt(power + 0.1 * average + 1e-05)
    return jnp.concatenate([real_part * factor, imag_part * factor], axis=1).astype(jnp.bfloat16)


def correlate_kernel(flags_ref, source_ref, plain_ref, swapped_ref, delays_ref, out_ref, cross_ref):
    block = source_ref.shape[0]
    receivers = plain_ref.shape[1]

    def one_source(s, carry):
        source = source_ref[s].astype(jnp.float32)
        direct = jnp.zeros((receivers, 2 * NF), jnp.float32)
        crossed = jnp.zeros((receivers, 2 * NF), jnp.float32)
        for w in range(SEGS):
            row = source[w : w + 1, :]
            direct = direct + row * plain_ref[w]
            crossed = crossed + row * swapped_ref[w]
        flag = flags_ref[pl.program_id(0) * block + s].astype(jnp.float32)
        cross = (direct - pltpu.roll(crossed, NF, 1)) * flag
        start = pl.multiple_of(s * receivers, receivers)
        cross_ref[pl.ds(start, receivers), :] = cross.astype(jnp.bfloat16)
        return carry

    lax.fori_loop(0, block, one_source, 0, unroll=True)
    lagged = jnp.dot(cross_ref[...], delays_ref[...], preferred_element_type=jnp.float32)
    lagged = lagged * (1.0 / math.sqrt(SEGS * NF))
    out_ref[...] = lagged.astype(jnp.bfloat16).reshape(out_ref.shape)


def correlate(chosen, source_flags, receivers, delays, block=32):
    source_count = chosen.shape[0]
    recv_count = receivers.shape[1]
    spectra = receivers.astype(jnp.float32)
    real_part = spectra[..., :NF]
    imag_part = spectra[..., NF:]
    plain = jnp.concatenate([real_part, real_part], axis=-1)
    swapped = jnp.concatenate([imag_part, -imag_part], axis=-1)
    grid_spec = pltpu.PrefetchScalarGridSpec(
        num_scalar_prefetch=1,
        grid=(source_count // block,),
        in_specs=[
            pl.BlockSpec((block, SEGS, 2 * NF), lambda i, flags: (i, 0, 0)),
            pl.BlockSpec((SEGS, recv_count, 2 * NF), lambda i, flags: (0, 0, 0)),
            pl.BlockSpec((SEGS, recv_count, 2 * NF), lambda i, flags: (0, 0, 0)),
            pl.BlockSpec((2 * NF, LAGS), lambda i, flags: (0, 0)),
        ],
        out_specs=pl.BlockSpec((block, recv_count, LAGS), lambda i, flags: (i, 0, 0)),
        scratch_shapes=[pltpu.VMEM((block * recv_count, 2 * NF), jnp.bfloat16)],
    )
    return pl.pallas_call(
        correlate_kernel,
        grid_spec=grid_spec,
        out_shape=jax.ShapeDtypeStruct((source_count, recv_count, LAGS), jnp.bfloat16),
    )(source_flags, chosen, plain, swapped, delays)


def body(recording, source_index, channel_mask):
    channels, raw_count = recording.shape
    devices = lax.axis_size("chan")
    me = lax.axis_index("chan")
    per_device = channels // devices
    dec_length = raw_count // 4
    sharing = devices // SEGS
    span = channels // sharing
    trailing = recording[:, raw_count - (TAPS - 4) :]
    earlier = from_behind(trailing, "chan", 1)
    decimated = decimate(earlier, recording, dec_length)
    slot = me % sharing
    rows = lax.dynamic_slice_in_dim(fourier_table(), slot * dec_length, dec_length, axis=0)
    partial = jnp.dot(decimated, rows, preferred_element_type=jnp.float32)
    pieces = partial.reshape(sharing, span, 2 * NF)
    spectrum = lax.dynamic_index_in_dim(pieces, slot, 0, keepdims=False)
    for step in range(1, sharing):
        route = [
            (group * sharing + i, group * sharing + (i + step) % sharing)
            for group in range(devices // sharing)
            for i in range(sharing)
        ]
        outgoing = lax.dynamic_index_in_dim(pieces, (slot + step) % sharing, 0, keepdims=False)
        spectrum = spectrum + lax.ppermute(outgoing, "chan", route)
    whitened = whiten(spectrum)
    flags = channel_mask.astype(jnp.bfloat16)
    flag_rows = jnp.zeros((16, 2 * NF), jnp.bfloat16).at[0, :per_device].set(flags)
    piece = jnp.concatenate([whitened, flag_rows], axis=0)
    gathered = lax.all_gather(piece, "chan", axis=0, tiled=False)
    height = piece.shape[0]
    blocks = gathered.reshape(SEGS, sharing, height, 2 * NF)
    picked = jnp.clip(source_index, 0, channels - 1)
    chosen = blocks[:, picked // span, picked % span].transpose(1, 0, 2)
    flags_all = gathered[:, span, :per_device].reshape(channels).astype(jnp.int32)
    hits = picked[:, None] == jnp.arange(channels, dtype=jnp.int32)[None, :]
    source_flags = jnp.sum(jnp.where(hits, flags_all[None, :], 0), axis=1)
    first = me * per_device
    receivers = lax.dynamic_slice(
        blocks, (0, first // span, first % span, 0), (SEGS, 1, per_device, 2 * NF)
    ).reshape(SEGS, per_device, 2 * NF)
    receivers = receivers * flags[None, :, None]
    result = correlate(chosen, source_flags, receivers, delay_table())
    return result.reshape(SOURCES, per_device, LAGS)


def solution(mesh):
    placed = (P("fiber", "chan"), P("fiber"), P(("fiber", "chan")))
    return jax.shard_map(
        body, mesh=mesh, in_specs=placed, out_specs=P("fiber", "chan", None), check_vma=False
    )
```

```python
import math

import jax
import jax.numpy as jnp
import numpy as np
from jax import lax
from jax.experimental import pallas as pl
from jax.experimental.pallas import tpu as pltpu
from jax.sharding import PartitionSpec as P

SEGS = 8
NSEG = 512
NF = 192
FBASE = 4
LAGS = 256
TAPS = 64
SOURCES = 512


def from_behind(block, axis, distance):
    devices = range(lax.axis_size(axis))
    route = [(i - distance, i) for i in devices if i - distance in devices]
    return lax.ppermute(block, axis, route)


def lowpass_taps():
    offsets = jnp.arange(TAPS, dtype=jnp.float32) - (TAPS - 1) / 2.0
    cutoff = 0.1
    window = 0.5 - 0.5 * jnp.cos(2.0 * math.pi * (jnp.arange(TAPS, dtype=jnp.float32) + 0.5) / TAPS)
    kernel = 2.0 * cutoff * jnp.sinc(2.0 * cutoff * offsets) * window
    kernel = kernel / jnp.sum(kernel)
    return kernel[::-1].astype(jnp.bfloat16)


def band_matrix(rows, out_length):
    with jax.ensure_compile_time_eval():
        reversed_taps = np.asarray(lowpass_taps().astype(jnp.float32))
    index = np.arange(rows)[:, None] - 4 * np.arange(out_length)[None, :]
    inside = (index >= 0) & (index < TAPS)
    band = np.where(inside, reversed_taps[np.clip(index, 0, TAPS - 1)], 0.0)
    return jnp.asarray(band.astype(np.float32)).astype(jnp.bfloat16)


def decimate(earlier, recording, out_length):
    head = earlier.shape[1]
    band = band_matrix(head + recording.shape[1], out_length)
    summed = jnp.dot(earlier, band[:head], preferred_element_type=jnp.float32)
    summed = summed + jnp.dot(recording, band[head:], preferred_element_type=jnp.float32)
    return summed.astype(jnp.bfloat16)


def fourier_table():
    sample = jnp.arange(NSEG, dtype=jnp.int32)[:, None]
    frequency = FBASE + jnp.arange(NF, dtype=jnp.int32)[None, :]
    angles = 2.0 * math.pi * (sample * frequency % NSEG).astype(jnp.float32) / NSEG
    return jnp.concatenate([jnp.cos(angles), -jnp.sin(angles)], axis=1).astype(jnp.bfloat16)


def delay_table():
    frequency = FBASE + jnp.arange(NF, dtype=jnp.int32)[:, None]
    delays = jnp.arange(LAGS, dtype=jnp.int32)[None, :] - LAGS // 2
    angles = 2.0 * math.pi * (frequency * delays % NSEG).astype(jnp.float32) / NSEG
    return jnp.concatenate([jnp.cos(angles), -jnp.sin(angles)], axis=0).astype(jnp.bfloat16)


def whiten(spectrum):
    real_part = spectrum[:, :NF]
    imag_part = spectrum[:, NF:]
    power = real_part * real_part + imag_part * imag_part
    average = jnp.mean(power, axis=1, keepdims=True)
    factor = lax.rsqrt(power + 0.1 * average + 1e-05)
    return jnp.concatenate([real_part * factor, imag_part * factor], axis=1).astype(jnp.bfloat16)


def correlate_kernel(flags_ref, source_ref, recv_ref, delays_ref, out_ref, plain_ref, swapped_ref, cross_ref):
    block = source_ref.shape[0]
    receivers = recv_ref.shape[1]

    @pl.when(pl.program_id(0) == 0)
    def _():
        lower = lax.broadcasted_iota(jnp.int32, (receivers, 2 * NF), 1) < NF
        for w in range(SEGS):
            spectra = recv_ref[w].astype(jnp.float32)
            turned = pltpu.roll(spectra, NF, 1)
            plain_ref[w] = jnp.where(lower, spectra, turned)
            swapped_ref[w] = jnp.where(lower, turned, -spectra)

    def one_source(s, carry):
        source = source_ref[s].astype(jnp.float32)
        direct = jnp.zeros((receivers, 2 * NF), jnp.float32)
        crossed = jnp.zeros((receivers, 2 * NF), jnp.float32)
        for w in range(SEGS):
            row = source[w : w + 1, :]
            direct = direct + row * plain_ref[w]
            crossed = crossed + row * swapped_ref[w]
        flag = flags_ref[pl.program_id(0) * block + s].astype(jnp.float32)
        cross = (direct - pltpu.roll(crossed, NF, 1)) * flag
        start = pl.multiple_of(s * receivers, receivers)
        cross_ref[pl.ds(start, receivers), :] = cross.astype(jnp.bfloat16)
        return carry

    lax.fori_loop(0, block, one_source, 0, unroll=True)
    lagged = jnp.dot(cross_ref[...], delays_ref[...], preferred_element_type=jnp.float32)
    lagged = lagged * (1.0 / math.sqrt(SEGS * NF))
    out_ref[...] = lagged.astype(jnp.bfloat16).reshape(out_ref.shape)


def correlate(chosen, source_flags, receivers, delays, block=32):
    source_count = chosen.shape[0]
    recv_count = receivers.shape[1]
    grid_spec = pltpu.PrefetchScalarGridSpec(
        num_scalar_prefetch=1,
        grid=(source_count // block,),
        in_specs=[
            pl.BlockSpec((block, SEGS, 2 * NF), lambda i, flags: (i, 0, 0)),
            pl.BlockSpec((SEGS, recv_count, 2 * NF), lambda i, flags: (0, 0, 0)),
            pl.BlockSpec((2 * NF, LAGS), lambda i, flags: (0, 0)),
        ],
        out_specs=pl.BlockSpec((block, recv_count, LAGS), lambda i, flags: (i, 0, 0)),
        scratch_shapes=[
            pltpu.VMEM((SEGS, recv_count, 2 * NF), jnp.float32),
            pltpu.VMEM((SEGS, recv_count, 2 * NF), jnp.float32),
            pltpu.VMEM((block * recv_count, 2 * NF), jnp.bfloat16),
        ],
    )
    return pl.pallas_call(
        correlate_kernel,
        grid_spec=grid_spec,
        out_shape=jax.ShapeDtypeStruct((source_count, recv_count, LAGS), jnp.bfloat16),
        compiler_params=pltpu.CompilerParams(dimension_semantics=("arbitrary",)),
    )(source_flags, chosen, receivers, delays)


def body(recording, source_index, channel_mask):
    channels, raw_count = recording.shape
    devices = lax.axis_size("chan")
    me = lax.axis_index("chan")
    per_device = channels // devices
    dec_length = raw_count // 4
    sharing = devices // SEGS
    span = channels // sharing
    trailing = recording[:, raw_count - (TAPS - 4) :]
    earlier = from_behind(trailing, "chan", 1)
    decimated = decimate(earlier, recording, dec_length)
    slot = me % sharing
    rows = lax.dynamic_slice_in_dim(fourier_table(), slot * dec_length, dec_length, axis=0)
    partial = jnp.dot(decimated, rows, preferred_element_type=jnp.float32)
    pieces = partial.reshape(sharing, span, 2 * NF)
    spectrum = lax.dynamic_index_in_dim(pieces, slot, 0, keepdims=False)
    for step in range(1, sharing):
        route = [
            (group * sharing + i, group * sharing + (i + step) % sharing)
            for group in range(devices // sharing)
            for i in range(sharing)
        ]
        outgoing = lax.dynamic_index_in_dim(pieces, (slot + step) % sharing, 0, keepdims=False)
        spectrum = spectrum + lax.ppermute(outgoing, "chan", route)
    whitened = whiten(spectrum)
    flags = channel_mask.astype(jnp.bfloat16)
    flag_rows = jnp.zeros((16, 2 * NF), jnp.bfloat16).at[0, :per_device].set(flags)
    piece = jnp.concatenate([whitened, flag_rows], axis=0)
    gathered = lax.all_gather(piece, "chan", axis=0, tiled=False)
    height = piece.shape[0]
    blocks = gathered.reshape(SEGS, sharing, height, 2 * NF)
    picked = jnp.clip(source_index, 0, channels - 1)
    chosen = blocks[:, picked // span, picked % span].transpose(1, 0, 2)
    flags_all = gathered[:, span, :per_device].reshape(channels).astype(jnp.int32)
    hits = picked[:, None] == jnp.arange(channels, dtype=jnp.int32)[None, :]
    source_flags = jnp.sum(jnp.where(hits, flags_all[None, :], 0), axis=1)
    first = me * per_device
    receivers = lax.dynamic_slice(
        blocks, (0, first // span, first % span, 0), (SEGS, 1, per_device, 2 * NF)
    ).reshape(SEGS, per_device, 2 * NF)
    receivers = receivers * flags[None, :, None]
    result = correlate(chosen, source_flags, receivers, delay_table())
    return result.reshape(SOURCES, per_device, LAGS)


def solution(mesh):
    placed = (P("fiber", "chan"), P("fiber"), P(("fiber", "chan")))
    return jax.shard_map(
        body, mesh=mesh, in_specs=placed, out_specs=P("fiber", "chan", None), check_vma=False
    )
```

```python
import math

import jax
import jax.numpy as jnp
import numpy as np
from jax import lax
from jax.experimental import pallas as pl
from jax.experimental.pallas import tpu as pltpu
from jax.sharding import PartitionSpec as P

SEGS = 8
NSEG = 512
NF = 192
FBASE = 4
LAGS = 256
TAPS = 64
SOURCES = 512


def from_behind(block, axis, distance):
    devices = range(lax.axis_size(axis))
    route = [(i - distance, i) for i in devices if i - distance in devices]
    return lax.ppermute(block, axis, route)


def lowpass_taps():
    offsets = jnp.arange(TAPS, dtype=jnp.float32) - (TAPS - 1) / 2.0
    cutoff = 0.1
    window = 0.5 - 0.5 * jnp.cos(2.0 * math.pi * (jnp.arange(TAPS, dtype=jnp.float32) + 0.5) / TAPS)
    kernel = 2.0 * cutoff * jnp.sinc(2.0 * cutoff * offsets) * window
    kernel = kernel / jnp.sum(kernel)
    return kernel[::-1].astype(jnp.bfloat16)


def band_matrix(rows, out_length):
    with jax.ensure_compile_time_eval():
        reversed_taps = np.asarray(lowpass_taps().astype(jnp.float32))
    index = np.arange(rows)[:, None] - 4 * np.arange(out_length)[None, :]
    inside = (index >= 0) & (index < TAPS)
    band = np.where(inside, reversed_taps[np.clip(index, 0, TAPS - 1)], 0.0)
    return jnp.asarray(band.astype(np.float32)).astype(jnp.bfloat16)


def decimate(earlier, recording, out_length):
    head = earlier.shape[1]
    band = band_matrix(head + recording.shape[1], out_length)
    summed = jnp.dot(earlier, band[:head], preferred_element_type=jnp.float32)
    summed = summed + jnp.dot(recording, band[head:], preferred_element_type=jnp.float32)
    return summed.astype(jnp.bfloat16)


def fourier_table():
    with jax.ensure_compile_time_eval():
        sample = jnp.arange(NSEG, dtype=jnp.int32)[:, None]
        frequency = FBASE + jnp.arange(NF, dtype=jnp.int32)[None, :]
        angles = 2.0 * math.pi * (sample * frequency % NSEG).astype(jnp.float32) / NSEG
        table = jnp.concatenate([jnp.cos(angles), -jnp.sin(angles)], axis=1)
        table = np.asarray(table.astype(jnp.bfloat16).astype(jnp.float32))
    return jnp.asarray(table).astype(jnp.bfloat16)


def delay_table():
    with jax.ensure_compile_time_eval():
        frequency = FBASE + jnp.arange(NF, dtype=jnp.int32)[:, None]
        delays = jnp.arange(LAGS, dtype=jnp.int32)[None, :] - LAGS // 2
        angles = 2.0 * math.pi * (frequency * delays % NSEG).astype(jnp.float32) / NSEG
        table = jnp.concatenate([jnp.cos(angles), -jnp.sin(angles)], axis=0)
        table = np.asarray(table.astype(jnp.bfloat16).astype(jnp.float32))
    return jnp.asarray(table).astype(jnp.bfloat16)


def whiten(spectrum):
    real_part = spectrum[:, :NF]
    imag_part = spectrum[:, NF:]
    power = real_part * real_part + imag_part * imag_part
    average = jnp.mean(power, axis=1, keepdims=True)
    factor = lax.rsqrt(power + 0.1 * average + 1e-05)
    return jnp.concatenate([real_part * factor, imag_part * factor], axis=1).astype(jnp.bfloat16)


def correlate_kernel(flags_ref, source_ref, recv_ref, delays_ref, out_ref, plain_ref, swapped_ref, cross_ref):
    block = source_ref.shape[0]
    receivers = recv_ref.shape[1]

    @pl.when(pl.program_id(0) == 0)
    def _():
        lower = lax.broadcasted_iota(jnp.int32, (receivers, 2 * NF), 1) < NF
        for w in range(SEGS):
            spectra = recv_ref[w].astype(jnp.float32)
            turned = pltpu.roll(spectra, NF, 1)
            plain_ref[w] = jnp.where(lower, spectra, turned)
            swapped_ref[w] = jnp.where(lower, turned, -spectra)

    def one_source(s, carry):
        source = source_ref[s].astype(jnp.float32)
        direct = jnp.zeros((receivers, 2 * NF), jnp.float32)
        crossed = jnp.zeros((receivers, 2 * NF), jnp.float32)
        for w in range(SEGS):
            row = source[w : w + 1, :]
            direct = direct + row * plain_ref[w]
            crossed = crossed + row * swapped_ref[w]
        flag = flags_ref[pl.program_id(0) * block + s].astype(jnp.float32)
        cross = (direct - pltpu.roll(crossed, NF, 1)) * flag
        start = pl.multiple_of(s * receivers, receivers)
        cross_ref[pl.ds(start, receivers), :] = cross.astype(jnp.bfloat16)
        return carry

    lax.fori_loop(0, block, one_source, 0, unroll=True)
    lagged = jnp.dot(cross_ref[...], delays_ref[...], preferred_element_type=jnp.float32)
    lagged = lagged * (1.0 / math.sqrt(SEGS * NF))
    out_ref[...] = lagged.astype(jnp.bfloat16).reshape(out_ref.shape)


def correlate(chosen, source_flags, receivers, delays, block=32):
    source_count = chosen.shape[0]
    recv_count = receivers.shape[1]
    grid_spec = pltpu.PrefetchScalarGridSpec(
        num_scalar_prefetch=1,
        grid=(source_count // block,),
        in_specs=[
            pl.BlockSpec((block, SEGS, 2 * NF), lambda i, flags: (i, 0, 0)),
            pl.BlockSpec((SEGS, recv_count, 2 * NF), lambda i, flags: (0, 0, 0)),
            pl.BlockSpec((2 * NF, LAGS), lambda i, flags: (0, 0)),
        ],
        out_specs=pl.BlockSpec((block, recv_count, LAGS), lambda i, flags: (i, 0, 0)),
        scratch_shapes=[
            pltpu.VMEM((SEGS, recv_count, 2 * NF), jnp.float32),
            pltpu.VMEM((SEGS, recv_count, 2 * NF), jnp.float32),
            pltpu.VMEM((block * recv_count, 2 * NF), jnp.bfloat16),
        ],
    )
    return pl.pallas_call(
        correlate_kernel,
        grid_spec=grid_spec,
        out_shape=jax.ShapeDtypeStruct((source_count, recv_count, LAGS), jnp.bfloat16),
        compiler_params=pltpu.CompilerParams(dimension_semantics=("arbitrary",)),
    )(source_flags, chosen, receivers, delays)


def body(recording, source_index, channel_mask):
    channels, raw_count = recording.shape
    devices = lax.axis_size("chan")
    me = lax.axis_index("chan")
    per_device = channels // devices
    dec_length = raw_count // 4
    sharing = devices // SEGS
    span = channels // sharing
    trailing = recording[:, raw_count - (TAPS - 4) :]
    earlier = from_behind(trailing, "chan", 1)
    decimated = decimate(earlier, recording, dec_length)
    slot = me % sharing
    rows = lax.dynamic_slice_in_dim(fourier_table(), slot * dec_length, dec_length, axis=0)
    partial = jnp.dot(decimated, rows, preferred_element_type=jnp.float32)
    pieces = partial.reshape(sharing, span, 2 * NF)
    spectrum = lax.dynamic_index_in_dim(pieces, slot, 0, keepdims=False)
    for step in range(1, sharing):
        route = [
            (group * sharing + i, group * sharing + (i + step) % sharing)
            for group in range(devices // sharing)
            for i in range(sharing)
        ]
        outgoing = lax.dynamic_index_in_dim(pieces, (slot + step) % sharing, 0, keepdims=False)
        spectrum = spectrum + lax.ppermute(outgoing, "chan", route)
    whitened = whiten(spectrum)
    flags = channel_mask.astype(jnp.bfloat16)
    flag_rows = jnp.zeros((16, 2 * NF), jnp.bfloat16).at[0, :per_device].set(flags)
    piece = jnp.concatenate([whitened, flag_rows], axis=0)
    gathered = lax.all_gather(piece, "chan", axis=0, tiled=False)
    height = piece.shape[0]
    blocks = gathered.reshape(SEGS, sharing, height, 2 * NF)
    picked = jnp.clip(source_index, 0, channels - 1)
    chosen = blocks[:, picked // span, picked % span].transpose(1, 0, 2)
    flags_all = gathered[:, span, :per_device].reshape(channels).astype(jnp.int32)
    hits = picked[:, None] == jnp.arange(channels, dtype=jnp.int32)[None, :]
    source_flags = jnp.sum(jnp.where(hits, flags_all[None, :], 0), axis=1)
    first = me * per_device
    receivers = lax.dynamic_slice(
        blocks, (0, first // span, first % span, 0), (SEGS, 1, per_device, 2 * NF)
    ).reshape(SEGS, per_device, 2 * NF)
    receivers = receivers * flags[None, :, None]
    result = correlate(chosen, source_flags, receivers, delay_table())
    return result.reshape(SOURCES, per_device, LAGS)


def solution(mesh):
    placed = (P("fiber", "chan"), P("fiber"), P(("fiber", "chan")))
    return jax.shard_map(
        body, mesh=mesh, in_specs=placed, out_specs=P("fiber", "chan", None), check_vma=False
    )
```

```python
import math

import jax
import jax.numpy as jnp
import numpy as np
from jax import lax
from jax.experimental import pallas as pl
from jax.experimental.pallas import tpu as pltpu
from jax.sharding import PartitionSpec as P

SEGS = 8
NSEG = 512
NF = 192
FBASE = 4
LAGS = 256
TAPS = 64
SOURCES = 512


def from_behind(block, axis, distance):
    devices = range(lax.axis_size(axis))
    route = [(i - distance, i) for i in devices if i - distance in devices]
    return lax.ppermute(block, axis, route)


def lowpass_taps():
    offsets = jnp.arange(TAPS, dtype=jnp.float32) - (TAPS - 1) / 2.0
    cutoff = 0.1
    window = 0.5 - 0.5 * jnp.cos(2.0 * math.pi * (jnp.arange(TAPS, dtype=jnp.float32) + 0.5) / TAPS)
    kernel = 2.0 * cutoff * jnp.sinc(2.0 * cutoff * offsets) * window
    kernel = kernel / jnp.sum(kernel)
    return kernel[::-1].astype(jnp.bfloat16)


def band_matrix(rows, out_length):
    with jax.ensure_compile_time_eval():
        reversed_taps = np.asarray(lowpass_taps().astype(jnp.float32))
    index = np.arange(rows)[:, None] - 4 * np.arange(out_length)[None, :]
    inside = (index >= 0) & (index < TAPS)
    band = np.where(inside, reversed_taps[np.clip(index, 0, TAPS - 1)], 0.0)
    return jnp.asarray(band.astype(np.float32)).astype(jnp.bfloat16)


def decimate(earlier, recording, out_length):
    head = earlier.shape[1]
    band = band_matrix(head + recording.shape[1], out_length)
    summed = jnp.dot(earlier, band[:head], preferred_element_type=jnp.float32)
    summed = summed + jnp.dot(recording, band[head:], preferred_element_type=jnp.float32)
    return summed.astype(jnp.bfloat16)


def fourier_table():
    with jax.ensure_compile_time_eval():
        sample = jnp.arange(NSEG, dtype=jnp.int32)[:, None]
        frequency = FBASE + jnp.arange(NF, dtype=jnp.int32)[None, :]
        angles = 2.0 * math.pi * (sample * frequency % NSEG).astype(jnp.float32) / NSEG
        table = jnp.concatenate([jnp.cos(angles), -jnp.sin(angles)], axis=1)
        table = np.asarray(table.astype(jnp.bfloat16).astype(jnp.float32))
    return jnp.asarray(table).astype(jnp.bfloat16)


def delay_table():
    with jax.ensure_compile_time_eval():
        frequency = FBASE + jnp.arange(NF, dtype=jnp.int32)[:, None]
        delays = jnp.arange(LAGS, dtype=jnp.int32)[None, :] - LAGS // 2
        angles = 2.0 * math.pi * (frequency * delays % NSEG).astype(jnp.float32) / NSEG
        table = jnp.concatenate([jnp.cos(angles), -jnp.sin(angles)], axis=0)
        table = np.asarray(table.astype(jnp.bfloat16).astype(jnp.float32))
    return jnp.asarray(table).astype(jnp.bfloat16)


def whiten(spectrum):
    real_part = spectrum[:, :NF]
    imag_part = spectrum[:, NF:]
    power = real_part * real_part + imag_part * imag_part
    average = jnp.mean(power, axis=1, keepdims=True)
    factor = lax.rsqrt(power + 0.1 * average + 1e-05)
    return jnp.concatenate([real_part * factor, imag_part * factor], axis=1).astype(jnp.bfloat16)


def correlate_kernel(flags_ref, source_ref, recv_ref, delays_ref, out_ref, plain_ref, swapped_ref, *cross_refs):
    block = source_ref.shape[0]
    receivers = recv_ref.shape[1]
    share = block // len(cross_refs)

    @pl.when(pl.program_id(0) == 0)
    def _():
        lower = lax.broadcasted_iota(jnp.int32, (receivers, 2 * NF), 1) < NF
        for w in range(SEGS):
            spectra = recv_ref[w].astype(jnp.float32)
            turned = pltpu.roll(spectra, NF, 1)
            plain_ref[w] = jnp.where(lower, spectra, turned)
            swapped_ref[w] = jnp.where(lower, turned, -spectra)

    for part, cross_ref in enumerate(cross_refs):

        def one_source(s, carry):
            at = part * share + s
            source = source_ref[at].astype(jnp.float32)
            direct = jnp.zeros((receivers, 2 * NF), jnp.float32)
            crossed = jnp.zeros((receivers, 2 * NF), jnp.float32)
            for w in range(SEGS):
                row = source[w : w + 1, :]
                direct = direct + row * plain_ref[w]
                crossed = crossed + row * swapped_ref[w]
            flag = flags_ref[pl.program_id(0) * block + at].astype(jnp.float32)
            cross = (direct - pltpu.roll(crossed, NF, 1)) * flag
            start = pl.multiple_of(s * receivers, receivers)
            cross_ref[pl.ds(start, receivers), :] = cross.astype(jnp.bfloat16)
            return carry

        lax.fori_loop(0, share, one_source, 0, unroll=True)
        lagged = jnp.dot(cross_ref[...], delays_ref[...], preferred_element_type=jnp.float32)
        lagged = lagged * (1.0 / math.sqrt(SEGS * NF))
        out_ref[part * share : (part + 1) * share] = lagged.astype(jnp.bfloat16).reshape(
            share, receivers, LAGS
        )


def correlate(chosen, source_flags, receivers, delays, block=64, parts=2):
    source_count = chosen.shape[0]
    recv_count = receivers.shape[1]
    grid_spec = pltpu.PrefetchScalarGridSpec(
        num_scalar_prefetch=1,
        grid=(source_count // block,),
        in_specs=[
            pl.BlockSpec((block, SEGS, 2 * NF), lambda i, flags: (i, 0, 0)),
            pl.BlockSpec((SEGS, recv_count, 2 * NF), lambda i, flags: (0, 0, 0)),
            pl.BlockSpec((2 * NF, LAGS), lambda i, flags: (0, 0)),
        ],
        out_specs=pl.BlockSpec((block, recv_count, LAGS), lambda i, flags: (i, 0, 0)),
        scratch_shapes=[
            pltpu.VMEM((SEGS, recv_count, 2 * NF), jnp.float32),
            pltpu.VMEM((SEGS, recv_count, 2 * NF), jnp.float32),
        ]
        + [pltpu.VMEM((block // parts * recv_count, 2 * NF), jnp.bfloat16)] * parts,
    )
    return pl.pallas_call(
        correlate_kernel,
        grid_spec=grid_spec,
        out_shape=jax.ShapeDtypeStruct((source_count, recv_count, LAGS), jnp.bfloat16),
        compiler_params=pltpu.CompilerParams(dimension_semantics=("arbitrary",)),
    )(source_flags, chosen, receivers, delays)


def body(recording, source_index, channel_mask):
    channels, raw_count = recording.shape
    devices = lax.axis_size("chan")
    me = lax.axis_index("chan")
    per_device = channels // devices
    dec_length = raw_count // 4
    sharing = devices // SEGS
    span = channels // sharing
    trailing = recording[:, raw_count - (TAPS - 4) :]
    earlier = from_behind(trailing, "chan", 1)
    decimated = decimate(earlier, recording, dec_length)
    slot = me % sharing
    rows = lax.dynamic_slice_in_dim(fourier_table(), slot * dec_length, dec_length, axis=0)
    partial = jnp.dot(decimated, rows, preferred_element_type=jnp.float32)
    pieces = partial.reshape(sharing, span, 2 * NF)
    spectrum = lax.dynamic_index_in_dim(pieces, slot, 0, keepdims=False)
    for step in range(1, sharing):
        route = [
            (group * sharing + i, group * sharing + (i + step) % sharing)
            for group in range(devices // sharing)
            for i in range(sharing)
        ]
        outgoing = lax.dynamic_index_in_dim(pieces, (slot + step) % sharing, 0, keepdims=False)
        spectrum = spectrum + lax.ppermute(outgoing, "chan", route)
    whitened = whiten(spectrum)
    flags = channel_mask.astype(jnp.bfloat16)
    flag_rows = jnp.zeros((16, 2 * NF), jnp.bfloat16).at[0, :per_device].set(flags)
    piece = jnp.concatenate([whitened, flag_rows], axis=0)
    gathered = lax.all_gather(piece, "chan", axis=0, tiled=False)
    height = piece.shape[0]
    blocks = gathered.reshape(SEGS, sharing, height, 2 * NF)
    picked = jnp.clip(source_index, 0, channels - 1)
    chosen = blocks[:, picked // span, picked % span].transpose(1, 0, 2)
    flags_all = gathered[:, span, :per_device].reshape(channels).astype(jnp.int32)
    hits = picked[:, None] == jnp.arange(channels, dtype=jnp.int32)[None, :]
    source_flags = jnp.sum(jnp.where(hits, flags_all[None, :], 0), axis=1)
    first = me * per_device
    receivers = lax.dynamic_slice(
        blocks, (0, first // span, first % span, 0), (SEGS, 1, per_device, 2 * NF)
    ).reshape(SEGS, per_device, 2 * NF)
    receivers = receivers * flags[None, :, None]
    result = correlate(chosen, source_flags, receivers, delay_table())
    return result.reshape(SOURCES, per_device, LAGS)


def solution(mesh):
    placed = (P("fiber", "chan"), P("fiber"), P(("fiber", "chan")))
    return jax.shard_map(
        body, mesh=mesh, in_specs=placed, out_specs=P("fiber", "chan", None), check_vma=False
    )
```

```python
import math

import jax
import jax.numpy as jnp
import numpy as np
from jax import lax
from jax.experimental import pallas as pl
from jax.experimental.pallas import tpu as pltpu
from jax.sharding import PartitionSpec as P

SEGS = 8
NSEG = 512
NF = 192
FBASE = 4
LAGS = 256
TAPS = 64
SOURCES = 512


def from_behind(block, axis, distance):
    devices = range(lax.axis_size(axis))
    route = [(i - distance, i) for i in devices if i - distance in devices]
    return lax.ppermute(block, axis, route)


def lowpass_taps():
    offsets = jnp.arange(TAPS, dtype=jnp.float32) - (TAPS - 1) / 2.0
    cutoff = 0.1
    window = 0.5 - 0.5 * jnp.cos(2.0 * math.pi * (jnp.arange(TAPS, dtype=jnp.float32) + 0.5) / TAPS)
    kernel = 2.0 * cutoff * jnp.sinc(2.0 * cutoff * offsets) * window
    kernel = kernel / jnp.sum(kernel)
    return kernel[::-1].astype(jnp.bfloat16)


def band_matrix(rows, out_length):
    with jax.ensure_compile_time_eval():
        reversed_taps = np.asarray(lowpass_taps().astype(jnp.float32))
    index = np.arange(rows)[:, None] - 4 * np.arange(out_length)[None, :]
    inside = (index >= 0) & (index < TAPS)
    band = np.where(inside, reversed_taps[np.clip(index, 0, TAPS - 1)], 0.0)
    return jnp.asarray(band.astype(np.float32)).astype(jnp.bfloat16)


def decimate(earlier, recording, out_length):
    head = earlier.shape[1]
    band = band_matrix(head + recording.shape[1], out_length)
    summed = jnp.dot(earlier, band[:head], preferred_element_type=jnp.float32)
    summed = summed + jnp.dot(recording, band[head:], preferred_element_type=jnp.float32)
    return summed.astype(jnp.bfloat16)


def fourier_table():
    with jax.ensure_compile_time_eval():
        sample = jnp.arange(NSEG, dtype=jnp.int32)[:, None]
        frequency = FBASE + jnp.arange(NF, dtype=jnp.int32)[None, :]
        angles = 2.0 * math.pi * (sample * frequency % NSEG).astype(jnp.float32) / NSEG
        table = jnp.concatenate([jnp.cos(angles), -jnp.sin(angles)], axis=1)
        table = np.asarray(table.astype(jnp.bfloat16).astype(jnp.float32))
    return jnp.asarray(table).astype(jnp.bfloat16)


def delay_table():
    with jax.ensure_compile_time_eval():
        frequency = FBASE + jnp.arange(NF, dtype=jnp.int32)[:, None]
        delays = jnp.arange(LAGS, dtype=jnp.int32)[None, :] - LAGS // 2
        angles = 2.0 * math.pi * (frequency * delays % NSEG).astype(jnp.float32) / NSEG
        table = jnp.concatenate([jnp.cos(angles), -jnp.sin(angles)], axis=0)
        table = np.asarray(table.astype(jnp.bfloat16).astype(jnp.float32))
    return jnp.asarray(table).astype(jnp.bfloat16)


def whiten(spectrum):
    real_part = spectrum[:, :NF]
    imag_part = spectrum[:, NF:]
    power = real_part * real_part + imag_part * imag_part
    average = jnp.mean(power, axis=1, keepdims=True)
    factor = lax.rsqrt(power + 0.1 * average + 1e-05)
    return jnp.concatenate([real_part * factor, imag_part * factor], axis=1).astype(jnp.bfloat16)


def correlate_kernel(
    flags_ref, picked_ref, place_ref, source_ref, recv_ref, own_ref, delays_ref, out_ref,
    plain_ref, swapped_ref, *cross_refs,
):
    block = source_ref.shape[0]
    receivers = recv_ref.shape[2]
    share = block // len(cross_refs)

    @pl.when(pl.program_id(0) == 0)
    def _():
        lower = lax.broadcasted_iota(jnp.int32, (receivers, 2 * NF), 1) < NF
        own = own_ref[...]
        for w in range(SEGS):
            spectra = recv_ref[w, 0].astype(jnp.float32) * own
            turned = pltpu.roll(spectra, NF, 1)
            plain_ref[w] = jnp.where(lower, spectra, turned)
            swapped_ref[w] = jnp.where(lower, turned, -spectra)

    for part, cross_ref in enumerate(cross_refs):

        def one_source(s, carry):
            at = part * share + s
            source = source_ref[at].astype(jnp.float32)
            direct = jnp.zeros((receivers, 2 * NF), jnp.float32)
            crossed = jnp.zeros((receivers, 2 * NF), jnp.float32)
            for w in range(SEGS):
                row = source[w : w + 1, :]
                direct = direct + row * plain_ref[w]
                crossed = crossed + row * swapped_ref[w]
            flag = flags_ref[picked_ref[pl.program_id(0) * block + at]].astype(jnp.float32)
            cross = (direct - pltpu.roll(crossed, NF, 1)) * flag
            start = pl.multiple_of(s * receivers, receivers)
            cross_ref[pl.ds(start, receivers), :] = cross.astype(jnp.bfloat16)
            return carry

        lax.fori_loop(0, share, one_source, 0, unroll=True)
        lagged = jnp.dot(cross_ref[...], delays_ref[...], preferred_element_type=jnp.float32)
        lagged = lagged * (1.0 / math.sqrt(SEGS * NF))
        out_ref[part * share : (part + 1) * share] = lagged.astype(jnp.bfloat16).reshape(
            share, receivers, LAGS
        )


def correlate(chosen, flags_all, picked, place, blocks, own_flags, delays, block=64, parts=2):
    source_count = chosen.shape[0]
    recv_count = own_flags.shape[0]
    grid_spec = pltpu.PrefetchScalarGridSpec(
        num_scalar_prefetch=3,
        grid=(source_count // block,),
        in_specs=[
            pl.BlockSpec((block, SEGS, 2 * NF), lambda i, f, p, q: (i, 0, 0)),
            pl.BlockSpec((SEGS, 1, recv_count, 2 * NF), lambda i, f, p, q: (0, q[0], q[1], 0)),
            pl.BlockSpec((recv_count, 1), lambda i, f, p, q: (0, 0)),
            pl.BlockSpec((2 * NF, LAGS), lambda i, f, p, q: (0, 0)),
        ],
        out_specs=pl.BlockSpec((block, recv_count, LAGS), lambda i, f, p, q: (i, 0, 0)),
        scratch_shapes=[
            pltpu.VMEM((SEGS, recv_count, 2 * NF), jnp.float32),
            pltpu.VMEM((SEGS, recv_count, 2 * NF), jnp.float32),
        ]
        + [pltpu.VMEM((block // parts * recv_count, 2 * NF), jnp.bfloat16)] * parts,
    )
    return pl.pallas_call(
        correlate_kernel,
        grid_spec=grid_spec,
        out_shape=jax.ShapeDtypeStruct((source_count, recv_count, LAGS), jnp.bfloat16),
        compiler_params=pltpu.CompilerParams(dimension_semantics=("arbitrary",)),
    )(flags_all, picked, place, chosen, blocks, own_flags, delays)


def body(recording, source_index, channel_mask):
    channels, raw_count = recording.shape
    devices = lax.axis_size("chan")
    me = lax.axis_index("chan")
    per_device = channels // devices
    dec_length = raw_count // 4
    sharing = devices // SEGS
    span = channels // sharing
    trailing = recording[:, raw_count - (TAPS - 4) :]
    earlier = from_behind(trailing, "chan", 1)
    decimated = decimate(earlier, recording, dec_length)
    slot = me % sharing
    rows = lax.dynamic_slice_in_dim(fourier_table(), slot * dec_length, dec_length, axis=0)
    partial = jnp.dot(decimated, rows, preferred_element_type=jnp.float32)
    pieces = partial.reshape(sharing, span, 2 * NF)
    spectrum = lax.dynamic_index_in_dim(pieces, slot, 0, keepdims=False)
    for step in range(1, sharing):
        route = [
            (group * sharing + i, group * sharing + (i + step) % sharing)
            for group in range(devices // sharing)
            for i in range(sharing)
        ]
        outgoing = lax.dynamic_index_in_dim(pieces, (slot + step) % sharing, 0, keepdims=False)
        spectrum = spectrum + lax.ppermute(outgoing, "chan", route)
    whitened = whiten(spectrum)
    flags = channel_mask.astype(jnp.bfloat16)
    flag_rows = jnp.zeros((16, 2 * NF), jnp.bfloat16).at[0, :per_device].set(flags)
    piece = jnp.concatenate([whitened, flag_rows], axis=0)
    gathered = lax.all_gather(piece, "chan", axis=0, tiled=False)
    height = piece.shape[0]
    blocks = gathered.reshape(SEGS, sharing, height, 2 * NF)
    picked = jnp.clip(source_index, 0, channels - 1)
    chosen = blocks[:, picked // span, picked % span].transpose(1, 0, 2)
    flags_all = gathered[:, span, :per_device].reshape(channels).astype(jnp.int32)
    first = me * per_device
    place = jnp.stack([first // span, first % span // per_device]).astype(jnp.int32)
    own_flags = channel_mask.astype(jnp.float32)[:, None]
    result = correlate(chosen, flags_all, picked, place, blocks, own_flags, delay_table())
    return result.reshape(SOURCES, per_device, LAGS)


def solution(mesh):
    placed = (P("fiber", "chan"), P("fiber"), P(("fiber", "chan")))
    return jax.shard_map(
        body, mesh=mesh, in_specs=placed, out_specs=P("fiber", "chan", None), check_vma=False
    )
```

```python
import math

import jax
import jax.numpy as jnp
import numpy as np
from jax import lax
from jax.experimental import pallas as pl
from jax.experimental.pallas import tpu as pltpu
from jax.sharding import PartitionSpec as P

SEGS = 8
NSEG = 512
NF = 192
FBASE = 4
LAGS = 256
TAPS = 64
SOURCES = 512


def from_behind(block, axis, distance):
    devices = range(lax.axis_size(axis))
    route = [(i - distance, i) for i in devices if i - distance in devices]
    return lax.ppermute(block, axis, route)


def lowpass_taps():
    offsets = jnp.arange(TAPS, dtype=jnp.float32) - (TAPS - 1) / 2.0
    cutoff = 0.1
    window = 0.5 - 0.5 * jnp.cos(2.0 * math.pi * (jnp.arange(TAPS, dtype=jnp.float32) + 0.5) / TAPS)
    kernel = 2.0 * cutoff * jnp.sinc(2.0 * cutoff * offsets) * window
    kernel = kernel / jnp.sum(kernel)
    return kernel[::-1].astype(jnp.bfloat16)


def band_matrix(rows, out_length):
    with jax.ensure_compile_time_eval():
        reversed_taps = np.asarray(lowpass_taps().astype(jnp.float32))
    index = np.arange(rows)[:, None] - 4 * np.arange(out_length)[None, :]
    inside = (index >= 0) & (index < TAPS)
    band = np.where(inside, reversed_taps[np.clip(index, 0, TAPS - 1)], 0.0)
    return jnp.asarray(band.astype(np.float32)).astype(jnp.bfloat16)


def decimate(earlier, recording, out_length):
    head = earlier.shape[1]
    band = band_matrix(head + recording.shape[1], out_length)
    summed = jnp.dot(earlier, band[:head], preferred_element_type=jnp.float32)
    summed = summed + jnp.dot(recording, band[head:], preferred_element_type=jnp.float32)
    return summed.astype(jnp.bfloat16)


def fourier_table():
    with jax.ensure_compile_time_eval():
        sample = jnp.arange(NSEG, dtype=jnp.int32)[:, None]
        frequency = FBASE + jnp.arange(NF, dtype=jnp.int32)[None, :]
        angles = 2.0 * math.pi * (sample * frequency % NSEG).astype(jnp.float32) / NSEG
        table = jnp.concatenate([jnp.cos(angles), -jnp.sin(angles)], axis=1)
        table = np.asarray(table.astype(jnp.bfloat16).astype(jnp.float32))
    return jnp.asarray(table).astype(jnp.bfloat16)


def delay_table():
    with jax.ensure_compile_time_eval():
        frequency = FBASE + jnp.arange(NF, dtype=jnp.int32)[:, None]
        delays = jnp.arange(LAGS, dtype=jnp.int32)[None, :] - LAGS // 2
        angles = 2.0 * math.pi * (frequency * delays % NSEG).astype(jnp.float32) / NSEG
        table = jnp.concatenate([jnp.cos(angles), -jnp.sin(angles)], axis=0)
        table = np.asarray(table.astype(jnp.bfloat16).astype(jnp.float32))
    return jnp.asarray(table).astype(jnp.bfloat16)


def whiten(spectrum):
    real_part = spectrum[:, :NF]
    imag_part = spectrum[:, NF:]
    power = real_part * real_part + imag_part * imag_part
    average = jnp.mean(power, axis=1, keepdims=True)
    factor = lax.rsqrt(power + 0.1 * average + 1e-05)
    return jnp.concatenate([real_part * factor, imag_part * factor], axis=1).astype(jnp.bfloat16)


def correlate_kernel(
    flags_ref, picked_ref, rows_ref, place_ref, source_ref, recv_ref, own_ref, delays_ref, out_ref,
    plain_ref, swapped_ref, *cross_refs,
):
    block = out_ref.shape[0]
    receivers = recv_ref.shape[2]
    share = block // len(cross_refs)

    @pl.when(pl.program_id(0) == 0)
    def _():
        lower = lax.broadcasted_iota(jnp.int32, (receivers, 2 * NF), 1) < NF
        own = own_ref[...]
        for w in range(SEGS):
            spectra = recv_ref[w, 0].astype(jnp.float32) * own
            turned = pltpu.roll(spectra, NF, 1)
            plain_ref[w] = jnp.where(lower, spectra, turned)
            swapped_ref[w] = jnp.where(lower, turned, -spectra)

    for part, cross_ref in enumerate(cross_refs):

        def one_source(s, carry):
            at = part * share + s
            line = rows_ref[pl.program_id(0) * block + at]
            direct = jnp.zeros((receivers, 2 * NF), jnp.float32)
            crossed = jnp.zeros((receivers, 2 * NF), jnp.float32)
            for w in range(SEGS):
                row = source_ref[w, pl.ds(line, 1), :]
                direct = direct + row * plain_ref[w]
                crossed = crossed + row * swapped_ref[w]
            flag = flags_ref[picked_ref[pl.program_id(0) * block + at]].astype(jnp.float32)
            cross = (direct - pltpu.roll(crossed, NF, 1)) * flag
            start = pl.multiple_of(s * receivers, receivers)
            cross_ref[pl.ds(start, receivers), :] = cross.astype(jnp.bfloat16)
            return carry

        lax.fori_loop(0, share, one_source, 0, unroll=True)
        lagged = jnp.dot(cross_ref[...], delays_ref[...], preferred_element_type=jnp.float32)
        lagged = lagged * (1.0 / math.sqrt(SEGS * NF))
        out_ref[part * share : (part + 1) * share] = lagged.astype(jnp.bfloat16).reshape(
            share, receivers, LAGS
        )


def correlate(table, flags_all, picked, rows, place, blocks, own_flags, delays, block=64, parts=2):
    source_count = picked.shape[0]
    recv_count = own_flags.shape[0]
    grid_spec = pltpu.PrefetchScalarGridSpec(
        num_scalar_prefetch=4,
        grid=(source_count // block,),
        in_specs=[
            pl.BlockSpec(table.shape, lambda i, f, p, r, q: (0, 0, 0)),
            pl.BlockSpec((SEGS, 1, recv_count, 2 * NF), lambda i, f, p, r, q: (0, q[0], q[1], 0)),
            pl.BlockSpec((recv_count, 1), lambda i, f, p, r, q: (0, 0)),
            pl.BlockSpec((2 * NF, LAGS), lambda i, f, p, r, q: (0, 0)),
        ],
        out_specs=pl.BlockSpec((block, recv_count, LAGS), lambda i, f, p, r, q: (i, 0, 0)),
        scratch_shapes=[
            pltpu.VMEM((SEGS, recv_count, 2 * NF), jnp.float32),
            pltpu.VMEM((SEGS, recv_count, 2 * NF), jnp.float32),
        ]
        + [pltpu.VMEM((block // parts * recv_count, 2 * NF), jnp.bfloat16)] * parts,
    )
    return pl.pallas_call(
        correlate_kernel,
        grid_spec=grid_spec,
        out_shape=jax.ShapeDtypeStruct((source_count, recv_count, LAGS), jnp.bfloat16),
        compiler_params=pltpu.CompilerParams(
            dimension_semantics=("arbitrary",), vmem_limit_bytes=48 * 1024 * 1024
        ),
    )(flags_all, picked, rows, place, table, blocks, own_flags, delays)


def body(recording, source_index, channel_mask):
    channels, raw_count = recording.shape
    devices = lax.axis_size("chan")
    me = lax.axis_index("chan")
    per_device = channels // devices
    dec_length = raw_count // 4
    sharing = devices // SEGS
    span = channels // sharing
    trailing = recording[:, raw_count - (TAPS - 4) :]
    earlier = from_behind(trailing, "chan", 1)
    decimated = decimate(earlier, recording, dec_length)
    slot = me % sharing
    rows = lax.dynamic_slice_in_dim(fourier_table(), slot * dec_length, dec_length, axis=0)
    partial = jnp.dot(decimated, rows, preferred_element_type=jnp.float32)
    pieces = partial.reshape(sharing, span, 2 * NF)
    spectrum = lax.dynamic_index_in_dim(pieces, slot, 0, keepdims=False)
    for step in range(1, sharing):
        route = [
            (group * sharing + i, group * sharing + (i + step) % sharing)
            for group in range(devices // sharing)
            for i in range(sharing)
        ]
        outgoing = lax.dynamic_index_in_dim(pieces, (slot + step) % sharing, 0, keepdims=False)
        spectrum = spectrum + lax.ppermute(outgoing, "chan", route)
    whitened = whiten(spectrum)
    flags = channel_mask.astype(jnp.bfloat16)
    flag_rows = jnp.zeros((16, 2 * NF), jnp.bfloat16).at[0, :per_device].set(flags)
    piece = jnp.concatenate([whitened, flag_rows], axis=0)
    gathered = lax.all_gather(piece, "chan", axis=0, tiled=False)
    height = piece.shape[0]
    blocks = gathered.reshape(SEGS, sharing, height, 2 * NF)
    picked = jnp.clip(source_index, 0, channels - 1)
    rows = picked // span * height + picked % span
    table = blocks.reshape(SEGS, sharing * height, 2 * NF).astype(jnp.float32)
    flags_all = gathered[:, span, :per_device].reshape(channels).astype(jnp.int32)
    first = me * per_device
    place = jnp.stack([first // span, first % span // per_device]).astype(jnp.int32)
    own_flags = channel_mask.astype(jnp.float32)[:, None]
    result = correlate(table, flags_all, picked, rows, place, blocks, own_flags, delay_table())
    return result.reshape(SOURCES, per_device, LAGS)


def solution(mesh):
    placed = (P("fiber", "chan"), P("fiber"), P(("fiber", "chan")))
    return jax.shard_map(
        body, mesh=mesh, in_specs=placed, out_specs=P("fiber", "chan", None), check_vma=False
    )
```

```python
import math

import jax
import jax.numpy as jnp
import numpy as np
from jax import lax
from jax.experimental import pallas as pl
from jax.experimental.pallas import tpu as pltpu
from jax.sharding import PartitionSpec as P

SEGS = 8
NSEG = 512
NF = 192
FBASE = 4
LAGS = 256
TAPS = 64
SOURCES = 512


def from_behind(block, axis, distance):
    devices = range(lax.axis_size(axis))
    route = [(i - distance, i) for i in devices if i - distance in devices]
    return lax.ppermute(block, axis, route)


def lowpass_taps():
    offsets = jnp.arange(TAPS, dtype=jnp.float32) - (TAPS - 1) / 2.0
    cutoff = 0.1
    window = 0.5 - 0.5 * jnp.cos(2.0 * math.pi * (jnp.arange(TAPS, dtype=jnp.float32) + 0.5) / TAPS)
    kernel = 2.0 * cutoff * jnp.sinc(2.0 * cutoff * offsets) * window
    kernel = kernel / jnp.sum(kernel)
    return kernel[::-1].astype(jnp.bfloat16)


def band_matrix(rows, out_length):
    with jax.ensure_compile_time_eval():
        reversed_taps = np.asarray(lowpass_taps().astype(jnp.float32))
    index = np.arange(rows)[:, None] - 4 * np.arange(out_length)[None, :]
    inside = (index >= 0) & (index < TAPS)
    band = np.where(inside, reversed_taps[np.clip(index, 0, TAPS - 1)], 0.0)
    return jnp.asarray(band.astype(np.float32)).astype(jnp.bfloat16)


def decimate(earlier, recording, out_length):
    head = earlier.shape[1]
    band = band_matrix(head + recording.shape[1], out_length)
    summed = jnp.dot(earlier, band[:head], preferred_element_type=jnp.float32)
    summed = summed + jnp.dot(recording, band[head:], preferred_element_type=jnp.float32)
    return summed.astype(jnp.bfloat16)


def fourier_table():
    with jax.ensure_compile_time_eval():
        sample = jnp.arange(NSEG, dtype=jnp.int32)[:, None]
        frequency = FBASE + jnp.arange(NF, dtype=jnp.int32)[None, :]
        angles = 2.0 * math.pi * (sample * frequency % NSEG).astype(jnp.float32) / NSEG
        table = jnp.concatenate([jnp.cos(angles), -jnp.sin(angles)], axis=1)
        table = np.asarray(table.astype(jnp.bfloat16).astype(jnp.float32))
    return jnp.asarray(table).astype(jnp.bfloat16)


def delay_table():
    with jax.ensure_compile_time_eval():
        frequency = FBASE + jnp.arange(NF, dtype=jnp.int32)[:, None]
        delays = jnp.arange(LAGS, dtype=jnp.int32)[None, :] - LAGS // 2
        angles = 2.0 * math.pi * (frequency * delays % NSEG).astype(jnp.float32) / NSEG
        table = jnp.concatenate([jnp.cos(angles), -jnp.sin(angles)], axis=0)
        table = np.asarray(table.astype(jnp.bfloat16).astype(jnp.float32))
    return jnp.asarray(table).astype(jnp.bfloat16)


def whiten(spectrum):
    real_part = spectrum[:, :NF]
    imag_part = spectrum[:, NF:]
    power = real_part * real_part + imag_part * imag_part
    average = jnp.mean(power, axis=1, keepdims=True)
    factor = lax.rsqrt(power + 0.1 * average + 1e-05)
    return jnp.concatenate([real_part * factor, imag_part * factor], axis=1).astype(jnp.bfloat16)


def correlate_kernel(
    flags_ref, picked_ref, place_ref, source_ref, recv_ref, own_ref, delays_ref, out_ref,
    plain_ref, swapped_ref, *cross_refs,
):
    block = source_ref.shape[0]
    receivers = recv_ref.shape[2]
    share = block // len(cross_refs)

    @pl.when(pl.program_id(0) == 0)
    def _():
        lower = lax.broadcasted_iota(jnp.int32, (receivers, 2 * NF), 1) < NF
        own = own_ref[...]
        for w in range(SEGS):
            spectra = recv_ref[w, 0].astype(jnp.float32) * own
            turned = pltpu.roll(spectra, NF, 1)
            plain_ref[w] = jnp.where(lower, spectra, turned)
            swapped_ref[w] = jnp.where(lower, turned, -spectra)

    for part, cross_ref in enumerate(cross_refs):

        def one_source(s, carry):
            at = part * share + s
            source = source_ref[at].astype(jnp.float32)
            turned = pltpu.roll(source, NF, 1)
            cross = jnp.zeros((receivers, 2 * NF), jnp.float32)
            for w in range(SEGS):
                cross = cross + source[w : w + 1, :] * plain_ref[w]
                cross = cross + turned[w : w + 1, :] * swapped_ref[w]
            flag = flags_ref[picked_ref[pl.program_id(0) * block + at]].astype(jnp.float32)
            cross = cross * flag
            start = pl.multiple_of(s * receivers, receivers)
            cross_ref[pl.ds(start, receivers), :] = cross.astype(jnp.bfloat16)
            return carry

        lax.fori_loop(0, share, one_source, 0, unroll=True)
        lagged = jnp.dot(cross_ref[...], delays_ref[...], preferred_element_type=jnp.float32)
        lagged = lagged * (1.0 / math.sqrt(SEGS * NF))
        out_ref[part * share : (part + 1) * share] = lagged.astype(jnp.bfloat16).reshape(
            share, receivers, LAGS
        )


def correlate(chosen, flags_all, picked, place, blocks, own_flags, delays, block=64, parts=2):
    source_count = chosen.shape[0]
    recv_count = own_flags.shape[0]
    grid_spec = pltpu.PrefetchScalarGridSpec(
        num_scalar_prefetch=3,
        grid=(source_count // block,),
        in_specs=[
            pl.BlockSpec((block, SEGS, 2 * NF), lambda i, f, p, q: (i, 0, 0)),
            pl.BlockSpec((SEGS, 1, recv_count, 2 * NF), lambda i, f, p, q: (0, q[0], q[1], 0)),
            pl.BlockSpec((recv_count, 1), lambda i, f, p, q: (0, 0)),
            pl.BlockSpec((2 * NF, LAGS), lambda i, f, p, q: (0, 0)),
        ],
        out_specs=pl.BlockSpec((block, recv_count, LAGS), lambda i, f, p, q: (i, 0, 0)),
        scratch_shapes=[
            pltpu.VMEM((SEGS, recv_count, 2 * NF), jnp.float32),
            pltpu.VMEM((SEGS, recv_count, 2 * NF), jnp.float32),
        ]
        + [pltpu.VMEM((block // parts * recv_count, 2 * NF), jnp.bfloat16)] * parts,
    )
    return pl.pallas_call(
        correlate_kernel,
        grid_spec=grid_spec,
        out_shape=jax.ShapeDtypeStruct((source_count, recv_count, LAGS), jnp.bfloat16),
        compiler_params=pltpu.CompilerParams(dimension_semantics=("arbitrary",)),
    )(flags_all, picked, place, chosen, blocks, own_flags, delays)


def body(recording, source_index, channel_mask):
    channels, raw_count = recording.shape
    devices = lax.axis_size("chan")
    me = lax.axis_index("chan")
    per_device = channels // devices
    dec_length = raw_count // 4
    sharing = devices // SEGS
    span = channels // sharing
    trailing = recording[:, raw_count - (TAPS - 4) :]
    earlier = from_behind(trailing, "chan", 1)
    decimated = decimate(earlier, recording, dec_length)
    slot = me % sharing
    rows = lax.dynamic_slice_in_dim(fourier_table(), slot * dec_length, dec_length, axis=0)
    partial = jnp.dot(decimated, rows, preferred_element_type=jnp.float32)
    pieces = partial.reshape(sharing, span, 2 * NF)
    spectrum = lax.dynamic_index_in_dim(pieces, slot, 0, keepdims=False)
    for step in range(1, sharing):
        route = [
            (group * sharing + i, group * sharing + (i + step) % sharing)
            for group in range(devices // sharing)
            for i in range(sharing)
        ]
        outgoing = lax.dynamic_index_in_dim(pieces, (slot + step) % sharing, 0, keepdims=False)
        spectrum = spectrum + lax.ppermute(outgoing, "chan", route)
    whitened = whiten(spectrum)
    flags = channel_mask.astype(jnp.bfloat16)
    flag_rows = jnp.zeros((16, 2 * NF), jnp.bfloat16).at[0, :per_device].set(flags)
    piece = jnp.concatenate([whitened, flag_rows], axis=0)
    gathered = lax.all_gather(piece, "chan", axis=0, tiled=False)
    height = piece.shape[0]
    blocks = gathered.reshape(SEGS, sharing, height, 2 * NF)
    picked = jnp.clip(source_index, 0, channels - 1)
    chosen = blocks[:, picked // span, picked % span].transpose(1, 0, 2)
    flags_all = gathered[:, span, :per_device].reshape(channels).astype(jnp.int32)
    first = me * per_device
    place = jnp.stack([first // span, first % span // per_device]).astype(jnp.int32)
    own_flags = channel_mask.astype(jnp.float32)[:, None]
    result = correlate(chosen, flags_all, picked, place, blocks, own_flags, delay_table())
    return result.reshape(SOURCES, per_device, LAGS)


def solution(mesh):
    placed = (P("fiber", "chan"), P("fiber"), P(("fiber", "chan")))
    return jax.shard_map(
        body, mesh=mesh, in_specs=placed, out_specs=P("fiber", "chan", None), check_vma=False
    )
```

```python
import math

import jax
import jax.numpy as jnp
import numpy as np
from jax import lax
from jax.experimental import pallas as pl
from jax.experimental.pallas import tpu as pltpu
from jax.sharding import PartitionSpec as P

SEGS = 8
NSEG = 512
NF = 192
FBASE = 4
LAGS = 256
TAPS = 64
SOURCES = 512


def from_behind(block, axis, distance):
    devices = range(lax.axis_size(axis))
    route = [(i - distance, i) for i in devices if i - distance in devices]
    return lax.ppermute(block, axis, route)


def lowpass_taps():
    offsets = jnp.arange(TAPS, dtype=jnp.float32) - (TAPS - 1) / 2.0
    cutoff = 0.1
    window = 0.5 - 0.5 * jnp.cos(2.0 * math.pi * (jnp.arange(TAPS, dtype=jnp.float32) + 0.5) / TAPS)
    kernel = 2.0 * cutoff * jnp.sinc(2.0 * cutoff * offsets) * window
    kernel = kernel / jnp.sum(kernel)
    return kernel[::-1].astype(jnp.bfloat16)


def band_matrix(rows, out_length):
    with jax.ensure_compile_time_eval():
        reversed_taps = np.asarray(lowpass_taps().astype(jnp.float32))
    index = np.arange(rows)[:, None] - 4 * np.arange(out_length)[None, :]
    inside = (index >= 0) & (index < TAPS)
    band = np.where(inside, reversed_taps[np.clip(index, 0, TAPS - 1)], 0.0)
    return jnp.asarray(band.astype(np.float32)).astype(jnp.bfloat16)


def decimate(earlier, recording, out_length):
    head = earlier.shape[1]
    band = band_matrix(head + recording.shape[1], out_length)
    summed = jnp.dot(earlier, band[:head], preferred_element_type=jnp.float32)
    summed = summed + jnp.dot(recording, band[head:], preferred_element_type=jnp.float32)
    return summed.astype(jnp.bfloat16)


def fourier_table():
    with jax.ensure_compile_time_eval():
        sample = jnp.arange(NSEG, dtype=jnp.int32)[:, None]
        frequency = FBASE + jnp.arange(NF, dtype=jnp.int32)[None, :]
        angles = 2.0 * math.pi * (sample * frequency % NSEG).astype(jnp.float32) / NSEG
        table = jnp.concatenate([jnp.cos(angles), -jnp.sin(angles)], axis=1)
        table = np.asarray(table.astype(jnp.bfloat16).astype(jnp.float32))
    return jnp.asarray(table).astype(jnp.bfloat16)


def delay_table():
    with jax.ensure_compile_time_eval():
        frequency = FBASE + jnp.arange(NF, dtype=jnp.int32)[:, None]
        delays = jnp.arange(LAGS, dtype=jnp.int32)[None, :] - LAGS // 2
        angles = 2.0 * math.pi * (frequency * delays % NSEG).astype(jnp.float32) / NSEG
        table = jnp.concatenate([jnp.cos(angles), -jnp.sin(angles)], axis=0)
        table = np.asarray(table.astype(jnp.bfloat16).astype(jnp.float32))
    return jnp.asarray(table).astype(jnp.bfloat16)


def whiten(spectrum):
    real_part = spectrum[:, :NF]
    imag_part = spectrum[:, NF:]
    power = real_part * real_part + imag_part * imag_part
    average = jnp.mean(power, axis=1, keepdims=True)
    factor = lax.rsqrt(power + 0.1 * average + 1e-05)
    return jnp.concatenate([real_part * factor, imag_part * factor], axis=1).astype(jnp.bfloat16)


def correlate_kernel(
    flags_ref, picked_ref, place_ref, source_ref, recv_ref, own_ref, delays_ref, out_ref,
    plain_ref, swapped_ref, *cross_refs,
):
    block = source_ref.shape[0]
    receivers = recv_ref.shape[2]
    share = block // len(cross_refs)

    @pl.when(pl.program_id(0) == 0)
    def _():
        lower = lax.broadcasted_iota(jnp.int32, (receivers, 2 * NF), 1) < NF
        own = own_ref[...]
        for w in range(SEGS):
            spectra = recv_ref[w, 0].astype(jnp.float32) * own
            turned = pltpu.roll(spectra, NF, 1)
            plain_ref[w] = jnp.where(lower, spectra, turned)
            swapped_ref[w] = jnp.where(lower, turned, -spectra)

    for part, cross_ref in enumerate(cross_refs):

        def one_source(s, carry):
            at = part * share + s
            source = source_ref[at].astype(jnp.float32)
            direct = [jnp.zeros((receivers, 2 * NF), jnp.float32)] * 2
            crossed = [jnp.zeros((receivers, 2 * NF), jnp.float32)] * 2
            for w in range(SEGS):
                row = source[w : w + 1, :]
                direct[w % 2] = direct[w % 2] + row * plain_ref[w]
                crossed[w % 2] = crossed[w % 2] + row * swapped_ref[w]
            direct = direct[0] + direct[1]
            crossed = crossed[0] + crossed[1]
            flag = flags_ref[picked_ref[pl.program_id(0) * block + at]].astype(jnp.float32)
            cross = (direct - pltpu.roll(crossed, NF, 1)) * flag
            start = pl.multiple_of(s * receivers, receivers)
            cross_ref[pl.ds(start, receivers), :] = cross.astype(jnp.bfloat16)
            return carry

        lax.fori_loop(0, share, one_source, 0, unroll=True)
        lagged = jnp.dot(cross_ref[...], delays_ref[...], preferred_element_type=jnp.float32)
        lagged = lagged * (1.0 / math.sqrt(SEGS * NF))
        out_ref[part * share : (part + 1) * share] = lagged.astype(jnp.bfloat16).reshape(
            share, receivers, LAGS
        )


def correlate(chosen, flags_all, picked, place, blocks, own_flags, delays, block=64, parts=2):
    source_count = chosen.shape[0]
    recv_count = own_flags.shape[0]
    grid_spec = pltpu.PrefetchScalarGridSpec(
        num_scalar_prefetch=3,
        grid=(source_count // block,),
        in_specs=[
            pl.BlockSpec((block, SEGS, 2 * NF), lambda i, f, p, q: (i, 0, 0)),
            pl.BlockSpec((SEGS, 1, recv_count, 2 * NF), lambda i, f, p, q: (0, q[0], q[1], 0)),
            pl.BlockSpec((recv_count, 1), lambda i, f, p, q: (0, 0)),
            pl.BlockSpec((2 * NF, LAGS), lambda i, f, p, q: (0, 0)),
        ],
        out_specs=pl.BlockSpec((block, recv_count, LAGS), lambda i, f, p, q: (i, 0, 0)),
        scratch_shapes=[
            pltpu.VMEM((SEGS, recv_count, 2 * NF), jnp.float32),
            pltpu.VMEM((SEGS, recv_count, 2 * NF), jnp.float32),
        ]
        + [pltpu.VMEM((block // parts * recv_count, 2 * NF), jnp.bfloat16)] * parts,
    )
    return pl.pallas_call(
        correlate_kernel,
        grid_spec=grid_spec,
        out_shape=jax.ShapeDtypeStruct((source_count, recv_count, LAGS), jnp.bfloat16),
        compiler_params=pltpu.CompilerParams(dimension_semantics=("arbitrary",)),
    )(flags_all, picked, place, chosen, blocks, own_flags, delays)


def body(recording, source_index, channel_mask):
    channels, raw_count = recording.shape
    devices = lax.axis_size("chan")
    me = lax.axis_index("chan")
    per_device = channels // devices
    dec_length = raw_count // 4
    sharing = devices // SEGS
    span = channels // sharing
    trailing = recording[:, raw_count - (TAPS - 4) :]
    earlier = from_behind(trailing, "chan", 1)
    decimated = decimate(earlier, recording, dec_length)
    slot = me % sharing
    rows = lax.dynamic_slice_in_dim(fourier_table(), slot * dec_length, dec_length, axis=0)
    partial = jnp.dot(decimated, rows, preferred_element_type=jnp.float32)
    pieces = partial.reshape(sharing, span, 2 * NF)
    spectrum = lax.dynamic_index_in_dim(pieces, slot, 0, keepdims=False)
    for step in range(1, sharing):
        route = [
            (group * sharing + i, group * sharing + (i + step) % sharing)
            for group in range(devices // sharing)
            for i in range(sharing)
        ]
        outgoing = lax.dynamic_index_in_dim(pieces, (slot + step) % sharing, 0, keepdims=False)
        spectrum = spectrum + lax.ppermute(outgoing, "chan", route)
    whitened = whiten(spectrum)
    flags = channel_mask.astype(jnp.bfloat16)
    flag_rows = jnp.zeros((16, 2 * NF), jnp.bfloat16).at[0, :per_device].set(flags)
    piece = jnp.concatenate([whitened, flag_rows], axis=0)
    gathered = lax.all_gather(piece, "chan", axis=0, tiled=False)
    height = piece.shape[0]
    blocks = gathered.reshape(SEGS, sharing, height, 2 * NF)
    picked = jnp.clip(source_index, 0, channels - 1)
    chosen = blocks[:, picked // span, picked % span].transpose(1, 0, 2)
    flags_all = gathered[:, span, :per_device].reshape(channels).astype(jnp.int32)
    first = me * per_device
    place = jnp.stack([first // span, first % span // per_device]).astype(jnp.int32)
    own_flags = channel_mask.astype(jnp.float32)[:, None]
    result = correlate(chosen, flags_all, picked, place, blocks, own_flags, delay_table())
    return result.reshape(SOURCES, per_device, LAGS)


def solution(mesh):
    placed = (P("fiber", "chan"), P("fiber"), P(("fiber", "chan")))
    return jax.shard_map(
        body, mesh=mesh, in_specs=placed, out_specs=P("fiber", "chan", None), check_vma=False
    )
```

```python
import math

import jax
import jax.numpy as jnp
import numpy as np
from jax import lax
from jax.experimental import pallas as pl
from jax.experimental.pallas import tpu as pltpu
from jax.sharding import PartitionSpec as P

SEGS = 8
NSEG = 512
NF = 192
FBASE = 4
LAGS = 256
TAPS = 64
SOURCES = 512


def from_behind(block, axis, distance):
    devices = range(lax.axis_size(axis))
    route = [(i - distance, i) for i in devices if i - distance in devices]
    return lax.ppermute(block, axis, route)


def lowpass_taps():
    offsets = jnp.arange(TAPS, dtype=jnp.float32) - (TAPS - 1) / 2.0
    cutoff = 0.1
    window = 0.5 - 0.5 * jnp.cos(2.0 * math.pi * (jnp.arange(TAPS, dtype=jnp.float32) + 0.5) / TAPS)
    kernel = 2.0 * cutoff * jnp.sinc(2.0 * cutoff * offsets) * window
    kernel = kernel / jnp.sum(kernel)
    return kernel[::-1].astype(jnp.bfloat16)


def band_matrix(rows, out_length):
    with jax.ensure_compile_time_eval():
        reversed_taps = np.asarray(lowpass_taps().astype(jnp.float32))
    index = np.arange(rows)[:, None] - 4 * np.arange(out_length)[None, :]
    inside = (index >= 0) & (index < TAPS)
    band = np.where(inside, reversed_taps[np.clip(index, 0, TAPS - 1)], 0.0)
    return jnp.asarray(band.astype(np.float32)).astype(jnp.bfloat16)


def decimate(earlier, recording, out_length):
    head = earlier.shape[1]
    band = band_matrix(head + recording.shape[1], out_length)
    summed = jnp.dot(earlier, band[:head], preferred_element_type=jnp.float32)
    summed = summed + jnp.dot(recording, band[head:], preferred_element_type=jnp.float32)
    return summed.astype(jnp.bfloat16)


def fourier_table():
    with jax.ensure_compile_time_eval():
        sample = jnp.arange(NSEG, dtype=jnp.int32)[:, None]
        frequency = FBASE + jnp.arange(NF, dtype=jnp.int32)[None, :]
        angles = 2.0 * math.pi * (sample * frequency % NSEG).astype(jnp.float32) / NSEG
        table = jnp.concatenate([jnp.cos(angles), -jnp.sin(angles)], axis=1)
        table = np.asarray(table.astype(jnp.bfloat16).astype(jnp.float32))
    return jnp.asarray(table).astype(jnp.bfloat16)


def delay_table():
    with jax.ensure_compile_time_eval():
        frequency = FBASE + jnp.arange(NF, dtype=jnp.int32)[:, None]
        delays = jnp.arange(LAGS, dtype=jnp.int32)[None, :] - LAGS // 2
        angles = 2.0 * math.pi * (frequency * delays % NSEG).astype(jnp.float32) / NSEG
        table = jnp.concatenate([jnp.cos(angles), -jnp.sin(angles)], axis=0)
        table = np.asarray(table.astype(jnp.bfloat16).astype(jnp.float32))
    return jnp.asarray(table).astype(jnp.bfloat16)


def whiten(spectrum):
    real_part = spectrum[:, :NF]
    imag_part = spectrum[:, NF:]
    power = real_part * real_part + imag_part * imag_part
    average = jnp.mean(power, axis=1, keepdims=True)
    factor = lax.rsqrt(power + 0.1 * average + 1e-05)
    return jnp.concatenate([real_part * factor, imag_part * factor], axis=1).astype(jnp.bfloat16)


def correlate_kernel(
    flags_ref, picked_ref, place_ref, source_ref, recv_ref, own_ref, delays_ref, out_ref,
    plain_ref, swapped_ref, *cross_refs,
):
    block = source_ref.shape[1]
    receivers = recv_ref.shape[2]
    share = block // len(cross_refs)

    @pl.when(pl.program_id(0) == 0)
    def _():
        lower = lax.broadcasted_iota(jnp.int32, (receivers, 2 * NF), 1) < NF
        own = own_ref[...]
        for w in range(SEGS):
            spectra = recv_ref[w, 0].astype(jnp.float32) * own
            turned = pltpu.roll(spectra, NF, 1)
            plain_ref[w] = jnp.where(lower, spectra, turned)
            swapped_ref[w] = jnp.where(lower, turned, -spectra)

    for part, cross_ref in enumerate(cross_refs):

        def one_source(s, carry):
            at = part * share + s
            direct = jnp.zeros((receivers, 2 * NF), jnp.float32)
            crossed = jnp.zeros((receivers, 2 * NF), jnp.float32)
            for w in range(SEGS):
                row = source_ref[w, pl.ds(at, 1), :].astype(jnp.float32)
                direct = direct + row * plain_ref[w]
                crossed = crossed + row * swapped_ref[w]
            flag = flags_ref[picked_ref[pl.program_id(0) * block + at]].astype(jnp.float32)
            cross = (direct - pltpu.roll(crossed, NF, 1)) * flag
            start = pl.multiple_of(s * receivers, receivers)
            cross_ref[pl.ds(start, receivers), :] = cross.astype(jnp.bfloat16)
            return carry

        lax.fori_loop(0, share, one_source, 0, unroll=True)
        lagged = jnp.dot(cross_ref[...], delays_ref[...], preferred_element_type=jnp.float32)
        lagged = lagged * (1.0 / math.sqrt(SEGS * NF))
        out_ref[part * share : (part + 1) * share] = lagged.astype(jnp.bfloat16).reshape(
            share, receivers, LAGS
        )


def correlate(chosen, flags_all, picked, place, blocks, own_flags, delays, block=64, parts=2):
    source_count = chosen.shape[1]
    recv_count = own_flags.shape[0]
    grid_spec = pltpu.PrefetchScalarGridSpec(
        num_scalar_prefetch=3,
        grid=(source_count // block,),
        in_specs=[
            pl.BlockSpec((SEGS, block, 2 * NF), lambda i, f, p, q: (0, i, 0)),
            pl.BlockSpec((SEGS, 1, recv_count, 2 * NF), lambda i, f, p, q: (0, q[0], q[1], 0)),
            pl.BlockSpec((recv_count, 1), lambda i, f, p, q: (0, 0)),
            pl.BlockSpec((2 * NF, LAGS), lambda i, f, p, q: (0, 0)),
        ],
        out_specs=pl.BlockSpec((block, recv_count, LAGS), lambda i, f, p, q: (i, 0, 0)),
        scratch_shapes=[
            pltpu.VMEM((SEGS, recv_count, 2 * NF), jnp.float32),
            pltpu.VMEM((SEGS, recv_count, 2 * NF), jnp.float32),
        ]
        + [pltpu.VMEM((block // parts * recv_count, 2 * NF), jnp.bfloat16)] * parts,
    )
    return pl.pallas_call(
        correlate_kernel,
        grid_spec=grid_spec,
        out_shape=jax.ShapeDtypeStruct((source_count, recv_count, LAGS), jnp.bfloat16),
        compiler_params=pltpu.CompilerParams(dimension_semantics=("arbitrary",)),
    )(flags_all, picked, place, chosen, blocks, own_flags, delays)


def body(recording, source_index, channel_mask):
    channels, raw_count = recording.shape
    devices = lax.axis_size("chan")
    me = lax.axis_index("chan")
    per_device = channels // devices
    dec_length = raw_count // 4
    sharing = devices // SEGS
    span = channels // sharing
    trailing = recording[:, raw_count - (TAPS - 4) :]
    earlier = from_behind(trailing, "chan", 1)
    decimated = decimate(earlier, recording, dec_length)
    slot = me % sharing
    rows = lax.dynamic_slice_in_dim(fourier_table(), slot * dec_length, dec_length, axis=0)
    partial = jnp.dot(decimated, rows, preferred_element_type=jnp.float32)
    pieces = partial.reshape(sharing, span, 2 * NF)
    spectrum = lax.dynamic_index_in_dim(pieces, slot, 0, keepdims=False)
    for step in range(1, sharing):
        route = [
            (group * sharing + i, group * sharing + (i + step) % sharing)
            for group in range(devices // sharing)
            for i in range(sharing)
        ]
        outgoing = lax.dynamic_index_in_dim(pieces, (slot + step) % sharing, 0, keepdims=False)
        spectrum = spectrum + lax.ppermute(outgoing, "chan", route)
    whitened = whiten(spectrum)
    flags = channel_mask.astype(jnp.bfloat16)
    flag_rows = jnp.zeros((16, 2 * NF), jnp.bfloat16).at[0, :per_device].set(flags)
    piece = jnp.concatenate([whitened, flag_rows], axis=0)
    gathered = lax.all_gather(piece, "chan", axis=0, tiled=False)
    height = piece.shape[0]
    blocks = gathered.reshape(SEGS, sharing, height, 2 * NF)
    picked = jnp.clip(source_index, 0, channels - 1)
    table = gathered.reshape(SEGS, sharing * height, 2 * NF)
    line = picked // span * height + picked % span
    pick = (line[:, None] == jnp.arange(sharing * height, dtype=jnp.int32)[None, :]).astype(jnp.bfloat16)
    chosen = jnp.einsum("sc,wcj->wsj", pick, table, preferred_element_type=jnp.float32)
    chosen = chosen.astype(jnp.bfloat16)
    flags_all = gathered[:, span, :per_device].reshape(channels).astype(jnp.int32)
    first = me * per_device
    place = jnp.stack([first // span, first % span // per_device]).astype(jnp.int32)
    own_flags = channel_mask.astype(jnp.float32)[:, None]
    result = correlate(chosen, flags_all, picked, place, blocks, own_flags, delay_table())
    return result.reshape(SOURCES, per_device, LAGS)


def solution(mesh):
    placed = (P("fiber", "chan"), P("fiber"), P(("fiber", "chan")))
    return jax.shard_map(
        body, mesh=mesh, in_specs=placed, out_specs=P("fiber", "chan", None), check_vma=False
    )
```

```python
import math

import jax
import jax.numpy as jnp
import numpy as np
from jax import lax
from jax.experimental import pallas as pl
from jax.experimental.pallas import tpu as pltpu
from jax.sharding import PartitionSpec as P

SEGS = 8
NSEG = 512
NF = 192
FBASE = 4
LAGS = 256
TAPS = 64
SOURCES = 512


def from_behind(block, axis, distance):
    devices = range(lax.axis_size(axis))
    route = [(i - distance, i) for i in devices if i - distance in devices]
    return lax.ppermute(block, axis, route)


def lowpass_taps():
    offsets = jnp.arange(TAPS, dtype=jnp.float32) - (TAPS - 1) / 2.0
    cutoff = 0.1
    window = 0.5 - 0.5 * jnp.cos(2.0 * math.pi * (jnp.arange(TAPS, dtype=jnp.float32) + 0.5) / TAPS)
    kernel = 2.0 * cutoff * jnp.sinc(2.0 * cutoff * offsets) * window
    kernel = kernel / jnp.sum(kernel)
    return kernel[::-1].astype(jnp.bfloat16)


def band_matrix(rows, out_length):
    with jax.ensure_compile_time_eval():
        reversed_taps = np.asarray(lowpass_taps().astype(jnp.float32))
    index = np.arange(rows)[:, None] - 4 * np.arange(out_length)[None, :]
    inside = (index >= 0) & (index < TAPS)
    band = np.where(inside, reversed_taps[np.clip(index, 0, TAPS - 1)], 0.0)
    return jnp.asarray(band.astype(np.float32)).astype(jnp.bfloat16)


def decimate(earlier, recording, out_length):
    head = earlier.shape[1]
    band = band_matrix(head + recording.shape[1], out_length)
    summed = jnp.dot(earlier, band[:head], preferred_element_type=jnp.float32)
    summed = summed + jnp.dot(recording, band[head:], preferred_element_type=jnp.float32)
    return summed.astype(jnp.bfloat16)


def fourier_table():
    with jax.ensure_compile_time_eval():
        sample = jnp.arange(NSEG, dtype=jnp.int32)[:, None]
        frequency = FBASE + jnp.arange(NF, dtype=jnp.int32)[None, :]
        angles = 2.0 * math.pi * (sample * frequency % NSEG).astype(jnp.float32) / NSEG
        table = jnp.concatenate([jnp.cos(angles), -jnp.sin(angles)], axis=1)
        table = np.asarray(table.astype(jnp.bfloat16).astype(jnp.float32))
    return jnp.asarray(table).astype(jnp.bfloat16)


def delay_table():
    with jax.ensure_compile_time_eval():
        frequency = FBASE + jnp.arange(NF, dtype=jnp.int32)[:, None]
        delays = jnp.arange(LAGS, dtype=jnp.int32)[None, :] - LAGS // 2
        angles = 2.0 * math.pi * (frequency * delays % NSEG).astype(jnp.float32) / NSEG
        table = jnp.concatenate([jnp.cos(angles), -jnp.sin(angles)], axis=0)
        table = np.asarray(table.astype(jnp.bfloat16).astype(jnp.float32))
    return jnp.asarray(table).astype(jnp.bfloat16)


def whiten(spectrum):
    real_part = spectrum[:, :NF]
    imag_part = spectrum[:, NF:]
    power = real_part * real_part + imag_part * imag_part
    average = jnp.mean(power, axis=1, keepdims=True)
    factor = lax.rsqrt(power + 0.1 * average + 1e-05)
    return jnp.concatenate([real_part * factor, imag_part * factor], axis=1).astype(jnp.bfloat16)


def correlate_kernel(
    flags_ref, picked_ref, place_ref, lines_ref, table_ref, recv_ref, own_ref, delays_ref, out_ref,
    plain_ref, swapped_ref, source_ref, *cross_refs,
):
    block = out_ref.shape[0]
    receivers = recv_ref.shape[2]
    share = block // len(cross_refs)

    @pl.when(pl.program_id(0) == 0)
    def _():
        lower = lax.broadcasted_iota(jnp.int32, (receivers, 2 * NF), 1) < NF
        own = own_ref[...]
        for w in range(SEGS):
            spectra = recv_ref[w, 0].astype(jnp.float32) * own
            turned = pltpu.roll(spectra, NF, 1)
            plain_ref[w] = jnp.where(lower, spectra, turned)
            swapped_ref[w] = jnp.where(lower, turned, -spectra)

    height = table_ref.shape[1]
    wanted = lines_ref[...]
    pick = (wanted == lax.broadcasted_iota(jnp.int32, (block, height), 1)).astype(jnp.bfloat16)
    for w in range(SEGS):
        source_ref[w] = jnp.dot(pick, table_ref[w], preferred_element_type=jnp.float32)

    for part, cross_ref in enumerate(cross_refs):

        def one_source(s, carry):
            at = part * share + s
            direct = jnp.zeros((receivers, 2 * NF), jnp.float32)
            crossed = jnp.zeros((receivers, 2 * NF), jnp.float32)
            for w in range(SEGS):
                row = source_ref[w, pl.ds(at, 1), :]
                direct = direct + row * plain_ref[w]
                crossed = crossed + row * swapped_ref[w]
            flag = flags_ref[picked_ref[pl.program_id(0) * block + at]].astype(jnp.float32)
            cross = (direct - pltpu.roll(crossed, NF, 1)) * flag
            start = pl.multiple_of(s * receivers, receivers)
            cross_ref[pl.ds(start, receivers), :] = cross.astype(jnp.bfloat16)
            return carry

        lax.fori_loop(0, share, one_source, 0, unroll=True)
        lagged = jnp.dot(cross_ref[...], delays_ref[...], preferred_element_type=jnp.float32)
        lagged = lagged * (1.0 / math.sqrt(SEGS * NF))
        out_ref[part * share : (part + 1) * share] = lagged.astype(jnp.bfloat16).reshape(
            share, receivers, LAGS
        )


def correlate(table, lines, flags_all, picked, place, blocks, own_flags, delays, block=64, parts=2):
    source_count = picked.shape[0]
    recv_count = own_flags.shape[0]
    grid_spec = pltpu.PrefetchScalarGridSpec(
        num_scalar_prefetch=3,
        grid=(source_count // block,),
        in_specs=[
            pl.BlockSpec((block, 1), lambda i, f, p, q: (i, 0)),
            pl.BlockSpec(table.shape, lambda i, f, p, q: (0, 0, 0)),
            pl.BlockSpec((SEGS, 1, recv_count, 2 * NF), lambda i, f, p, q: (0, q[0], q[1], 0)),
            pl.BlockSpec((recv_count, 1), lambda i, f, p, q: (0, 0)),
            pl.BlockSpec((2 * NF, LAGS), lambda i, f, p, q: (0, 0)),
        ],
        out_specs=pl.BlockSpec((block, recv_count, LAGS), lambda i, f, p, q: (i, 0, 0)),
        scratch_shapes=[
            pltpu.VMEM((SEGS, recv_count, 2 * NF), jnp.float32),
            pltpu.VMEM((SEGS, recv_count, 2 * NF), jnp.float32),
            pltpu.VMEM((SEGS, block, 2 * NF), jnp.float32),
        ]
        + [pltpu.VMEM((block // parts * recv_count, 2 * NF), jnp.bfloat16)] * parts,
    )
    return pl.pallas_call(
        correlate_kernel,
        grid_spec=grid_spec,
        out_shape=jax.ShapeDtypeStruct((source_count, recv_count, LAGS), jnp.bfloat16),
        compiler_params=pltpu.CompilerParams(dimension_semantics=("arbitrary",)),
    )(flags_all, picked, place, lines, table, blocks, own_flags, delays)


def body(recording, source_index, channel_mask):
    channels, raw_count = recording.shape
    devices = lax.axis_size("chan")
    me = lax.axis_index("chan")
    per_device = channels // devices
    dec_length = raw_count // 4
    sharing = devices // SEGS
    span = channels // sharing
    trailing = recording[:, raw_count - (TAPS - 4) :]
    earlier = from_behind(trailing, "chan", 1)
    decimated = decimate(earlier, recording, dec_length)
    slot = me % sharing
    rows = lax.dynamic_slice_in_dim(fourier_table(), slot * dec_length, dec_length, axis=0)
    partial = jnp.dot(decimated, rows, preferred_element_type=jnp.float32)
    pieces = partial.reshape(sharing, span, 2 * NF)
    spectrum = lax.dynamic_index_in_dim(pieces, slot, 0, keepdims=False)
    for step in range(1, sharing):
        route = [
            (group * sharing + i, group * sharing + (i + step) % sharing)
            for group in range(devices // sharing)
            for i in range(sharing)
        ]
        outgoing = lax.dynamic_index_in_dim(pieces, (slot + step) % sharing, 0, keepdims=False)
        spectrum = spectrum + lax.ppermute(outgoing, "chan", route)
    whitened = whiten(spectrum)
    flags = channel_mask.astype(jnp.bfloat16)
    flag_rows = jnp.zeros((16, 2 * NF), jnp.bfloat16).at[0, :per_device].set(flags)
    piece = jnp.concatenate([whitened, flag_rows], axis=0)
    gathered = lax.all_gather(piece, "chan", axis=0, tiled=False)
    height = piece.shape[0]
    blocks = gathered.reshape(SEGS, sharing, height, 2 * NF)
    picked = jnp.clip(source_index, 0, channels - 1)
    table = gathered.reshape(SEGS, sharing * height, 2 * NF)
    line = picked // span * height + picked % span
    flags_all = gathered[:, span, :per_device].reshape(channels).astype(jnp.int32)
    first = me * per_device
    place = jnp.stack([first // span, first % span // per_device]).astype(jnp.int32)
    own_flags = channel_mask.astype(jnp.float32)[:, None]
    result = correlate(table, line[:, None], flags_all, picked, place, blocks, own_flags, delay_table())
    return result.reshape(SOURCES, per_device, LAGS)


def solution(mesh):
    placed = (P("fiber", "chan"), P("fiber"), P(("fiber", "chan")))
    return jax.shard_map(
        body, mesh=mesh, in_specs=placed, out_specs=P("fiber", "chan", None), check_vma=False
    )
```

```python
import math

import jax
import jax.numpy as jnp
import numpy as np
from jax import lax
from jax.experimental import pallas as pl
from jax.experimental.pallas import tpu as pltpu
from jax.sharding import PartitionSpec as P

SEGS = 8
NSEG = 512
NF = 192
FBASE = 4
LAGS = 256
TAPS = 64
SOURCES = 512


def from_behind(block, axis, distance):
    devices = range(lax.axis_size(axis))
    route = [(i - distance, i) for i in devices if i - distance in devices]
    return lax.ppermute(block, axis, route)


def lowpass_taps():
    offsets = jnp.arange(TAPS, dtype=jnp.float32) - (TAPS - 1) / 2.0
    cutoff = 0.1
    window = 0.5 - 0.5 * jnp.cos(2.0 * math.pi * (jnp.arange(TAPS, dtype=jnp.float32) + 0.5) / TAPS)
    kernel = 2.0 * cutoff * jnp.sinc(2.0 * cutoff * offsets) * window
    kernel = kernel / jnp.sum(kernel)
    return kernel[::-1].astype(jnp.bfloat16)


def band_matrix(rows, out_length):
    with jax.ensure_compile_time_eval():
        reversed_taps = np.asarray(lowpass_taps().astype(jnp.float32))
    index = np.arange(rows)[:, None] - 4 * np.arange(out_length)[None, :]
    inside = (index >= 0) & (index < TAPS)
    band = np.where(inside, reversed_taps[np.clip(index, 0, TAPS - 1)], 0.0)
    return jnp.asarray(band.astype(np.float32)).astype(jnp.bfloat16)


def decimate(earlier, recording, out_length):
    head = earlier.shape[1]
    band = band_matrix(head + recording.shape[1], out_length)
    summed = jnp.dot(earlier, band[:head], preferred_element_type=jnp.float32)
    summed = summed + jnp.dot(recording, band[head:], preferred_element_type=jnp.float32)
    return summed.astype(jnp.bfloat16)


def fourier_table():
    with jax.ensure_compile_time_eval():
        sample = jnp.arange(NSEG, dtype=jnp.int32)[:, None]
        frequency = FBASE + jnp.arange(NF, dtype=jnp.int32)[None, :]
        angles = 2.0 * math.pi * (sample * frequency % NSEG).astype(jnp.float32) / NSEG
        table = jnp.concatenate([jnp.cos(angles), -jnp.sin(angles)], axis=1)
        table = np.asarray(table.astype(jnp.bfloat16).astype(jnp.float32))
    return jnp.asarray(table).astype(jnp.bfloat16)


def delay_table():
    with jax.ensure_compile_time_eval():
        frequency = FBASE + jnp.arange(NF, dtype=jnp.int32)[:, None]
        delays = jnp.arange(LAGS, dtype=jnp.int32)[None, :] - LAGS // 2
        angles = 2.0 * math.pi * (frequency * delays % NSEG).astype(jnp.float32) / NSEG
        table = jnp.concatenate([jnp.cos(angles), -jnp.sin(angles)], axis=0)
        table = np.asarray(table.astype(jnp.bfloat16).astype(jnp.float32))
    return jnp.asarray(table).astype(jnp.bfloat16)


def whiten(spectrum):
    real_part = spectrum[:, :NF]
    imag_part = spectrum[:, NF:]
    power = real_part * real_part + imag_part * imag_part
    average = jnp.mean(power, axis=1, keepdims=True)
    factor = lax.rsqrt(power + 0.1 * average + 1e-05)
    return jnp.concatenate([real_part * factor, imag_part * factor], axis=1).astype(jnp.bfloat16)


def correlate_kernel(
    flags_ref, picked_ref, place_ref, lines_ref, table_ref, recv_ref, own_ref, delays_ref, out_ref,
    plain_ref, swapped_ref, source_ref, *cross_refs,
):
    block = out_ref.shape[0]
    receivers = recv_ref.shape[2]
    share = block // len(cross_refs)

    @pl.when(pl.program_id(0) == 0)
    def _():
        lower = lax.broadcasted_iota(jnp.int32, (receivers, 2 * NF), 1) < NF
        own = own_ref[...]
        for w in range(SEGS):
            spectra = recv_ref[w, 0].astype(jnp.float32) * own
            turned = pltpu.roll(spectra, NF, 1)
            plain_ref[w] = jnp.where(lower, spectra, turned)
            swapped_ref[w] = jnp.where(lower, turned, -spectra)

    height = table_ref.shape[1]
    wanted = lines_ref[...]
    pick = (wanted == lax.broadcasted_iota(jnp.int32, (block, height), 1)).astype(jnp.bfloat16)
    for part, cross_ref in enumerate(cross_refs):
        window = slice(part * share, (part + 1) * share)
        for w in range(SEGS):
            source_ref[w, window] = jnp.dot(
                pick[window], table_ref[w], preferred_element_type=jnp.float32
            )

        def one_source(s, carry):
            at = part * share + s
            direct = jnp.zeros((receivers, 2 * NF), jnp.float32)
            crossed = jnp.zeros((receivers, 2 * NF), jnp.float32)
            for w in range(SEGS):
                row = source_ref[w, pl.ds(at, 1), :]
                direct = direct + row * plain_ref[w]
                crossed = crossed + row * swapped_ref[w]
            flag = flags_ref[picked_ref[pl.program_id(0) * block + at]].astype(jnp.float32)
            cross = (direct - pltpu.roll(crossed, NF, 1)) * flag
            start = pl.multiple_of(s * receivers, receivers)
            cross_ref[pl.ds(start, receivers), :] = cross.astype(jnp.bfloat16)
            return carry

        lax.fori_loop(0, share, one_source, 0, unroll=True)
        lagged = jnp.dot(cross_ref[...], delays_ref[...], preferred_element_type=jnp.float32)
        lagged = lagged * (1.0 / math.sqrt(SEGS * NF))
        out_ref[part * share : (part + 1) * share] = lagged.astype(jnp.bfloat16).reshape(
            share, receivers, LAGS
        )


def correlate(table, lines, flags_all, picked, place, blocks, own_flags, delays, block=64, parts=2):
    source_count = picked.shape[0]
    recv_count = own_flags.shape[0]
    grid_spec = pltpu.PrefetchScalarGridSpec(
        num_scalar_prefetch=3,
        grid=(source_count // block,),
        in_specs=[
            pl.BlockSpec((block, 1), lambda i, f, p, q: (i, 0)),
            pl.BlockSpec(table.shape, lambda i, f, p, q: (0, 0, 0)),
            pl.BlockSpec((SEGS, 1, recv_count, 2 * NF), lambda i, f, p, q: (0, q[0], q[1], 0)),
            pl.BlockSpec((recv_count, 1), lambda i, f, p, q: (0, 0)),
            pl.BlockSpec((2 * NF, LAGS), lambda i, f, p, q: (0, 0)),
        ],
        out_specs=pl.BlockSpec((block, recv_count, LAGS), lambda i, f, p, q: (i, 0, 0)),
        scratch_shapes=[
            pltpu.VMEM((SEGS, recv_count, 2 * NF), jnp.float32),
            pltpu.VMEM((SEGS, recv_count, 2 * NF), jnp.float32),
            pltpu.VMEM((SEGS, block, 2 * NF), jnp.float32),
        ]
        + [pltpu.VMEM((block // parts * recv_count, 2 * NF), jnp.bfloat16)] * parts,
    )
    return pl.pallas_call(
        correlate_kernel,
        grid_spec=grid_spec,
        out_shape=jax.ShapeDtypeStruct((source_count, recv_count, LAGS), jnp.bfloat16),
        compiler_params=pltpu.CompilerParams(dimension_semantics=("arbitrary",)),
    )(flags_all, picked, place, lines, table, blocks, own_flags, delays)


def body(recording, source_index, channel_mask):
    channels, raw_count = recording.shape
    devices = lax.axis_size("chan")
    me = lax.axis_index("chan")
    per_device = channels // devices
    dec_length = raw_count // 4
    sharing = devices // SEGS
    span = channels // sharing
    trailing = recording[:, raw_count - (TAPS - 4) :]
    earlier = from_behind(trailing, "chan", 1)
    decimated = decimate(earlier, recording, dec_length)
    slot = me % sharing
    rows = lax.dynamic_slice_in_dim(fourier_table(), slot * dec_length, dec_length, axis=0)
    partial = jnp.dot(decimated, rows, preferred_element_type=jnp.float32)
    pieces = partial.reshape(sharing, span, 2 * NF)
    spectrum = lax.dynamic_index_in_dim(pieces, slot, 0, keepdims=False)
    for step in range(1, sharing):
        route = [
            (group * sharing + i, group * sharing + (i + step) % sharing)
            for group in range(devices // sharing)
            for i in range(sharing)
        ]
        outgoing = lax.dynamic_index_in_dim(pieces, (slot + step) % sharing, 0, keepdims=False)
        spectrum = spectrum + lax.ppermute(outgoing, "chan", route)
    whitened = whiten(spectrum)
    flags = channel_mask.astype(jnp.bfloat16)
    flag_rows = jnp.zeros((16, 2 * NF), jnp.bfloat16).at[0, :per_device].set(flags)
    piece = jnp.concatenate([whitened, flag_rows], axis=0)
    gathered = lax.all_gather(piece, "chan", axis=0, tiled=False)
    height = piece.shape[0]
    blocks = gathered.reshape(SEGS, sharing, height, 2 * NF)
    picked = jnp.clip(source_index, 0, channels - 1)
    table = gathered.reshape(SEGS, sharing * height, 2 * NF)
    line = picked // span * height + picked % span
    flags_all = gathered[:, span, :per_device].reshape(channels).astype(jnp.int32)
    first = me * per_device
    place = jnp.stack([first // span, first % span // per_device]).astype(jnp.int32)
    own_flags = channel_mask.astype(jnp.float32)[:, None]
    result = correlate(table, line[:, None], flags_all, picked, place, blocks, own_flags, delay_table())
    return result.reshape(SOURCES, per_device, LAGS)


def solution(mesh):
    placed = (P("fiber", "chan"), P("fiber"), P(("fiber", "chan")))
    return jax.shard_map(
        body, mesh=mesh, in_specs=placed, out_specs=P("fiber", "chan", None), check_vma=False
    )
```

```python
import math

import jax
import jax.numpy as jnp
import numpy as np
from jax import lax
from jax.experimental import pallas as pl
from jax.experimental.pallas import tpu as pltpu
from jax.sharding import PartitionSpec as P

SEGS = 8
NSEG = 512
NF = 192
FBASE = 4
LAGS = 256
TAPS = 64
SOURCES = 512


def from_behind(block, axis, distance):
    devices = range(lax.axis_size(axis))
    route = [(i - distance, i) for i in devices if i - distance in devices]
    return lax.ppermute(block, axis, route)


def lowpass_taps():
    offsets = jnp.arange(TAPS, dtype=jnp.float32) - (TAPS - 1) / 2.0
    cutoff = 0.1
    window = 0.5 - 0.5 * jnp.cos(2.0 * math.pi * (jnp.arange(TAPS, dtype=jnp.float32) + 0.5) / TAPS)
    kernel = 2.0 * cutoff * jnp.sinc(2.0 * cutoff * offsets) * window
    kernel = kernel / jnp.sum(kernel)
    return kernel[::-1].astype(jnp.bfloat16)


def band_matrix(rows, out_length):
    with jax.ensure_compile_time_eval():
        reversed_taps = np.asarray(lowpass_taps().astype(jnp.float32))
    index = np.arange(rows)[:, None] - 4 * np.arange(out_length)[None, :]
    inside = (index >= 0) & (index < TAPS)
    band = np.where(inside, reversed_taps[np.clip(index, 0, TAPS - 1)], 0.0)
    return jnp.asarray(band.astype(np.float32)).astype(jnp.bfloat16)


def decimate(earlier, recording, out_length):
    head = earlier.shape[1]
    band = band_matrix(head + recording.shape[1], out_length)
    summed = jnp.dot(earlier, band[:head], preferred_element_type=jnp.float32)
    summed = summed + jnp.dot(recording, band[head:], preferred_element_type=jnp.float32)
    return summed.astype(jnp.bfloat16)


def fourier_table():
    with jax.ensure_compile_time_eval():
        sample = jnp.arange(NSEG, dtype=jnp.int32)[:, None]
        frequency = FBASE + jnp.arange(NF, dtype=jnp.int32)[None, :]
        angles = 2.0 * math.pi * (sample * frequency % NSEG).astype(jnp.float32) / NSEG
        table = jnp.concatenate([jnp.cos(angles), -jnp.sin(angles)], axis=1)
        table = np.asarray(table.astype(jnp.bfloat16).astype(jnp.float32))
    return jnp.asarray(table).astype(jnp.bfloat16)


def delay_table():
    with jax.ensure_compile_time_eval():
        frequency = FBASE + jnp.arange(NF, dtype=jnp.int32)[:, None]
        delays = jnp.arange(LAGS, dtype=jnp.int32)[None, :] - LAGS // 2
        angles = 2.0 * math.pi * (frequency * delays % NSEG).astype(jnp.float32) / NSEG
        table = jnp.concatenate([jnp.cos(angles), -jnp.sin(angles)], axis=0)
        table = np.asarray(table.astype(jnp.bfloat16).astype(jnp.float32))
    return jnp.asarray(table).astype(jnp.bfloat16)


def whiten(spectrum):
    real_part = spectrum[:, :NF]
    imag_part = spectrum[:, NF:]
    power = real_part * real_part + imag_part * imag_part
    average = jnp.mean(power, axis=1, keepdims=True)
    factor = lax.rsqrt(power + 0.1 * average + 1e-05)
    return jnp.concatenate([real_part * factor, imag_part * factor], axis=1).astype(jnp.bfloat16)


def correlate_kernel(
    flags_ref, picked_ref, place_ref, lines_ref, table_ref, recv_ref, own_ref, delays_ref, out_ref,
    plain_ref, swapped_ref, source_ref, *cross_refs,
):
    block = out_ref.shape[0]
    receivers = recv_ref.shape[2]
    share = block // len(cross_refs)

    @pl.when(pl.program_id(0) == 0)
    def _():
        lower = lax.broadcasted_iota(jnp.int32, (receivers, 2 * NF), 1) < NF
        own = own_ref[...]
        for w in range(SEGS):
            spectra = recv_ref[w, 0].astype(jnp.float32) * own
            turned = pltpu.roll(spectra, NF, 1)
            plain_ref[w] = jnp.where(lower, spectra, turned)
            swapped_ref[w] = jnp.where(lower, turned, -spectra)

    height = table_ref.shape[1]
    step = pl.program_id(0)

    def select(at, slot):
        start = pl.multiple_of(at * block, block)
        wanted = lines_ref[pl.ds(start, block), :]
        pick = (wanted == lax.broadcasted_iota(jnp.int32, (block, height), 1)).astype(jnp.bfloat16)
        for w in range(SEGS):
            source_ref[slot, w] = jnp.dot(pick, table_ref[w], preferred_element_type=jnp.float32)

    @pl.when(step == 0)
    def _():
        select(0, 0)

    slot = step % 2
    select(jnp.minimum(step + 1, pl.num_programs(0) - 1), 1 - slot)

    for part, cross_ref in enumerate(cross_refs):

        def one_source(s, carry):
            at = part * share + s
            direct = jnp.zeros((receivers, 2 * NF), jnp.float32)
            crossed = jnp.zeros((receivers, 2 * NF), jnp.float32)
            for w in range(SEGS):
                row = source_ref[slot, w, pl.ds(at, 1), :]
                direct = direct + row * plain_ref[w]
                crossed = crossed + row * swapped_ref[w]
            flag = flags_ref[picked_ref[pl.program_id(0) * block + at]].astype(jnp.float32)
            cross = (direct - pltpu.roll(crossed, NF, 1)) * flag
            start = pl.multiple_of(s * receivers, receivers)
            cross_ref[pl.ds(start, receivers), :] = cross.astype(jnp.bfloat16)
            return carry

        lax.fori_loop(0, share, one_source, 0, unroll=True)
        lagged = jnp.dot(cross_ref[...], delays_ref[...], preferred_element_type=jnp.float32)
        lagged = lagged * (1.0 / math.sqrt(SEGS * NF))
        out_ref[part * share : (part + 1) * share] = lagged.astype(jnp.bfloat16).reshape(
            share, receivers, LAGS
        )


def correlate(table, lines, flags_all, picked, place, blocks, own_flags, delays, block=64, parts=2):
    source_count = picked.shape[0]
    recv_count = own_flags.shape[0]
    grid_spec = pltpu.PrefetchScalarGridSpec(
        num_scalar_prefetch=3,
        grid=(source_count // block,),
        in_specs=[
            pl.BlockSpec((source_count, 1), lambda i, f, p, q: (0, 0)),
            pl.BlockSpec(table.shape, lambda i, f, p, q: (0, 0, 0)),
            pl.BlockSpec((SEGS, 1, recv_count, 2 * NF), lambda i, f, p, q: (0, q[0], q[1], 0)),
            pl.BlockSpec((recv_count, 1), lambda i, f, p, q: (0, 0)),
            pl.BlockSpec((2 * NF, LAGS), lambda i, f, p, q: (0, 0)),
        ],
        out_specs=pl.BlockSpec((block, recv_count, LAGS), lambda i, f, p, q: (i, 0, 0)),
        scratch_shapes=[
            pltpu.VMEM((SEGS, recv_count, 2 * NF), jnp.float32),
            pltpu.VMEM((SEGS, recv_count, 2 * NF), jnp.float32),
            pltpu.VMEM((2, SEGS, block, 2 * NF), jnp.float32),
        ]
        + [pltpu.VMEM((block // parts * recv_count, 2 * NF), jnp.bfloat16)] * parts,
    )
    return pl.pallas_call(
        correlate_kernel,
        grid_spec=grid_spec,
        out_shape=jax.ShapeDtypeStruct((source_count, recv_count, LAGS), jnp.bfloat16),
        compiler_params=pltpu.CompilerParams(dimension_semantics=("arbitrary",)),
    )(flags_all, picked, place, lines, table, blocks, own_flags, delays)


def body(recording, source_index, channel_mask):
    channels, raw_count = recording.shape
    devices = lax.axis_size("chan")
    me = lax.axis_index("chan")
    per_device = channels // devices
    dec_length = raw_count // 4
    sharing = devices // SEGS
    span = channels // sharing
    trailing = recording[:, raw_count - (TAPS - 4) :]
    earlier = from_behind(trailing, "chan", 1)
    decimated = decimate(earlier, recording, dec_length)
    slot = me % sharing
    rows = lax.dynamic_slice_in_dim(fourier_table(), slot * dec_length, dec_length, axis=0)
    partial = jnp.dot(decimated, rows, preferred_element_type=jnp.float32)
    pieces = partial.reshape(sharing, span, 2 * NF)
    spectrum = lax.dynamic_index_in_dim(pieces, slot, 0, keepdims=False)
    for step in range(1, sharing):
        route = [
            (group * sharing + i, group * sharing + (i + step) % sharing)
            for group in range(devices // sharing)
            for i in range(sharing)
        ]
        outgoing = lax.dynamic_index_in_dim(pieces, (slot + step) % sharing, 0, keepdims=False)
        spectrum = spectrum + lax.ppermute(outgoing, "chan", route)
    whitened = whiten(spectrum)
    flags = channel_mask.astype(jnp.bfloat16)
    flag_rows = jnp.zeros((16, 2 * NF), jnp.bfloat16).at[0, :per_device].set(flags)
    piece = jnp.concatenate([whitened, flag_rows], axis=0)
    gathered = lax.all_gather(piece, "chan", axis=0, tiled=False)
    height = piece.shape[0]
    blocks = gathered.reshape(SEGS, sharing, height, 2 * NF)
    picked = jnp.clip(source_index, 0, channels - 1)
    table = gathered.reshape(SEGS, sharing * height, 2 * NF)
    line = picked // span * height + picked % span
    flags_all = gathered[:, span, :per_device].reshape(channels).astype(jnp.int32)
    first = me * per_device
    place = jnp.stack([first // span, first % span // per_device]).astype(jnp.int32)
    own_flags = channel_mask.astype(jnp.float32)[:, None]
    result = correlate(table, line[:, None], flags_all, picked, place, blocks, own_flags, delay_table())
    return result.reshape(SOURCES, per_device, LAGS)


def solution(mesh):
    placed = (P("fiber", "chan"), P("fiber"), P(("fiber", "chan")))
    return jax.shard_map(
        body, mesh=mesh, in_specs=placed, out_specs=P("fiber", "chan", None), check_vma=False
    )
```

```python
import math

import jax
import jax.numpy as jnp
import numpy as np
from jax import lax
from jax.experimental import pallas as pl
from jax.experimental.pallas import tpu as pltpu
from jax.sharding import PartitionSpec as P

SEGS = 8
NSEG = 512
NF = 192
FBASE = 4
LAGS = 256
TAPS = 64
SOURCES = 512


def from_behind(block, axis, distance):
    devices = range(lax.axis_size(axis))
    route = [(i - distance, i) for i in devices if i - distance in devices]
    return lax.ppermute(block, axis, route)


def lowpass_taps():
    offsets = jnp.arange(TAPS, dtype=jnp.float32) - (TAPS - 1) / 2.0
    cutoff = 0.1
    window = 0.5 - 0.5 * jnp.cos(2.0 * math.pi * (jnp.arange(TAPS, dtype=jnp.float32) + 0.5) / TAPS)
    kernel = 2.0 * cutoff * jnp.sinc(2.0 * cutoff * offsets) * window
    kernel = kernel / jnp.sum(kernel)
    return kernel[::-1].astype(jnp.bfloat16)


def band_matrix(rows, out_length):
    with jax.ensure_compile_time_eval():
        reversed_taps = np.asarray(lowpass_taps().astype(jnp.float32))
    index = np.arange(rows)[:, None] - 4 * np.arange(out_length)[None, :]
    inside = (index >= 0) & (index < TAPS)
    band = np.where(inside, reversed_taps[np.clip(index, 0, TAPS - 1)], 0.0)
    return jnp.asarray(band.astype(np.float32)).astype(jnp.bfloat16)


def decimate(earlier, recording, out_length):
    head = earlier.shape[1]
    band = band_matrix(head + recording.shape[1], out_length)
    summed = jnp.dot(earlier, band[:head], preferred_element_type=jnp.float32)
    summed = summed + jnp.dot(recording, band[head:], preferred_element_type=jnp.float32)
    return summed.astype(jnp.bfloat16)


def fourier_table():
    with jax.ensure_compile_time_eval():
        sample = jnp.arange(NSEG, dtype=jnp.int32)[:, None]
        frequency = FBASE + jnp.arange(NF, dtype=jnp.int32)[None, :]
        angles = 2.0 * math.pi * (sample * frequency % NSEG).astype(jnp.float32) / NSEG
        table = jnp.concatenate([jnp.cos(angles), -jnp.sin(angles)], axis=1)
        table = np.asarray(table.astype(jnp.bfloat16).astype(jnp.float32))
    return jnp.asarray(table).astype(jnp.bfloat16)


def delay_table():
    with jax.ensure_compile_time_eval():
        frequency = FBASE + jnp.arange(NF, dtype=jnp.int32)[:, None]
        delays = jnp.arange(LAGS, dtype=jnp.int32)[None, :] - LAGS // 2
        angles = 2.0 * math.pi * (frequency * delays % NSEG).astype(jnp.float32) / NSEG
        table = jnp.concatenate([jnp.cos(angles), -jnp.sin(angles)], axis=0)
        table = np.asarray(table.astype(jnp.bfloat16).astype(jnp.float32))
    return jnp.asarray(table).astype(jnp.bfloat16)


def whiten(spectrum):
    real_part = spectrum[:, :NF]
    imag_part = spectrum[:, NF:]
    power = real_part * real_part + imag_part * imag_part
    average = jnp.mean(power, axis=1, keepdims=True)
    factor = lax.rsqrt(power + 0.1 * average + 1e-05)
    return jnp.concatenate([real_part * factor, imag_part * factor], axis=1).astype(jnp.bfloat16)


def correlate_kernel(
    flags_ref, picked_ref, place_ref, lines_ref, table_ref, recv_ref, own_ref, delays_ref, out_ref,
    plain_ref, swapped_ref, source_ref, *cross_refs,
):
    block = out_ref.shape[0]
    receivers = recv_ref.shape[2]
    share = block // len(cross_refs)

    @pl.when(pl.program_id(0) == 0)
    def _():
        lower = lax.broadcasted_iota(jnp.int32, (receivers, 2 * NF), 1) < NF
        own = own_ref[...]
        for w in range(SEGS):
            spectra = recv_ref[w, 0].astype(jnp.float32) * own
            turned = pltpu.roll(spectra, NF, 1)
            plain_ref[w] = jnp.where(lower, spectra, turned)
            swapped_ref[w] = jnp.where(lower, turned, -spectra)

    height = table_ref.shape[1]
    step = pl.program_id(0)

    def select(at, slot):
        start = pl.multiple_of(at * block, block)
        wanted = lines_ref[pl.ds(start, block), :]
        pick = (wanted == lax.broadcasted_iota(jnp.int32, (block, height), 1)).astype(jnp.bfloat16)
        for w in range(SEGS):
            source_ref[slot, w] = jnp.dot(pick, table_ref[w], preferred_element_type=jnp.float32)

    @pl.when(step == 0)
    def _():
        select(0, 0)

    slot = step % 2
    select(jnp.minimum(step + 1, pl.num_programs(0) - 1), 1 - slot)

    for part, cross_ref in enumerate(cross_refs):

        def one_source(s, carry):
            at = part * share + s
            direct = jnp.zeros((receivers, 2 * NF), jnp.float32)
            crossed = jnp.zeros((receivers, 2 * NF), jnp.float32)
            for w in range(SEGS):
                row = source_ref[slot, w, pl.ds(at, 1), :]
                direct = direct + row * plain_ref[w]
                crossed = crossed + row * swapped_ref[w]
            flag = flags_ref[picked_ref[pl.program_id(0) * block + at]].astype(jnp.float32)
            cross = (direct - pltpu.roll(crossed, NF, 1)) * flag
            start = pl.multiple_of(s * receivers, receivers)
            cross_ref[pl.ds(start, receivers), :] = cross.astype(jnp.bfloat16)
            return carry

        lax.fori_loop(0, share, one_source, 0, unroll=True)
        lagged = jnp.dot(cross_ref[...], delays_ref[...], preferred_element_type=jnp.float32)
        lagged = lagged * (1.0 / math.sqrt(SEGS * NF))
        out_ref[part * share : (part + 1) * share] = lagged.astype(jnp.bfloat16).reshape(
            share, receivers, LAGS
        )


def correlate(table, lines, flags_all, picked, place, blocks, own_flags, delays, block=128, parts=2):
    source_count = picked.shape[0]
    recv_count = own_flags.shape[0]
    grid_spec = pltpu.PrefetchScalarGridSpec(
        num_scalar_prefetch=3,
        grid=(source_count // block,),
        in_specs=[
            pl.BlockSpec((source_count, 1), lambda i, f, p, q: (0, 0)),
            pl.BlockSpec(table.shape, lambda i, f, p, q: (0, 0, 0)),
            pl.BlockSpec((SEGS, 1, recv_count, 2 * NF), lambda i, f, p, q: (0, q[0], q[1], 0)),
            pl.BlockSpec((recv_count, 1), lambda i, f, p, q: (0, 0)),
            pl.BlockSpec((2 * NF, LAGS), lambda i, f, p, q: (0, 0)),
        ],
        out_specs=pl.BlockSpec((block, recv_count, LAGS), lambda i, f, p, q: (i, 0, 0)),
        scratch_shapes=[
            pltpu.VMEM((SEGS, recv_count, 2 * NF), jnp.float32),
            pltpu.VMEM((SEGS, recv_count, 2 * NF), jnp.float32),
            pltpu.VMEM((2, SEGS, block, 2 * NF), jnp.float32),
        ]
        + [pltpu.VMEM((block // parts * recv_count, 2 * NF), jnp.bfloat16)] * parts,
    )
    return pl.pallas_call(
        correlate_kernel,
        grid_spec=grid_spec,
        out_shape=jax.ShapeDtypeStruct((source_count, recv_count, LAGS), jnp.bfloat16),
        compiler_params=pltpu.CompilerParams(dimension_semantics=("arbitrary",)),
    )(flags_all, picked, place, lines, table, blocks, own_flags, delays)


def body(recording, source_index, channel_mask):
    channels, raw_count = recording.shape
    devices = lax.axis_size("chan")
    me = lax.axis_index("chan")
    per_device = channels // devices
    dec_length = raw_count // 4
    sharing = devices // SEGS
    span = channels // sharing
    trailing = recording[:, raw_count - (TAPS - 4) :]
    earlier = from_behind(trailing, "chan", 1)
    decimated = decimate(earlier, recording, dec_length)
    slot = me % sharing
    rows = lax.dynamic_slice_in_dim(fourier_table(), slot * dec_length, dec_length, axis=0)
    partial = jnp.dot(decimated, rows, preferred_element_type=jnp.float32)
    pieces = partial.reshape(sharing, span, 2 * NF)
    spectrum = lax.dynamic_index_in_dim(pieces, slot, 0, keepdims=False)
    for step in range(1, sharing):
        route = [
            (group * sharing + i, group * sharing + (i + step) % sharing)
            for group in range(devices // sharing)
            for i in range(sharing)
        ]
        outgoing = lax.dynamic_index_in_dim(pieces, (slot + step) % sharing, 0, keepdims=False)
        spectrum = spectrum + lax.ppermute(outgoing, "chan", route)
    whitened = whiten(spectrum)
    flags = channel_mask.astype(jnp.bfloat16)
    flag_rows = jnp.zeros((16, 2 * NF), jnp.bfloat16).at[0, :per_device].set(flags)
    piece = jnp.concatenate([whitened, flag_rows], axis=0)
    gathered = lax.all_gather(piece, "chan", axis=0, tiled=False)
    height = piece.shape[0]
    blocks = gathered.reshape(SEGS, sharing, height, 2 * NF)
    picked = jnp.clip(source_index, 0, channels - 1)
    table = gathered.reshape(SEGS, sharing * height, 2 * NF)
    line = picked // span * height + picked % span
    flags_all = gathered[:, span, :per_device].reshape(channels).astype(jnp.int32)
    first = me * per_device
    place = jnp.stack([first // span, first % span // per_device]).astype(jnp.int32)
    own_flags = channel_mask.astype(jnp.float32)[:, None]
    result = correlate(table, line[:, None], flags_all, picked, place, blocks, own_flags, delay_table())
    return result.reshape(SOURCES, per_device, LAGS)


def solution(mesh):
    placed = (P("fiber", "chan"), P("fiber"), P(("fiber", "chan")))
    return jax.shard_map(
        body, mesh=mesh, in_specs=placed, out_specs=P("fiber", "chan", None), check_vma=False
    )
```

```python
import math

import jax
import jax.numpy as jnp
import numpy as np
from jax import lax
from jax.experimental import pallas as pl
from jax.experimental.pallas import tpu as pltpu
from jax.sharding import PartitionSpec as P

SEGS = 8
NSEG = 512
NF = 192
FBASE = 4
LAGS = 256
TAPS = 64
SOURCES = 512


def from_behind(block, axis, distance):
    devices = range(lax.axis_size(axis))
    route = [(i - distance, i) for i in devices if i - distance in devices]
    return lax.ppermute(block, axis, route)


def lowpass_taps():
    offsets = jnp.arange(TAPS, dtype=jnp.float32) - (TAPS - 1) / 2.0
    cutoff = 0.1
    window = 0.5 - 0.5 * jnp.cos(2.0 * math.pi * (jnp.arange(TAPS, dtype=jnp.float32) + 0.5) / TAPS)
    kernel = 2.0 * cutoff * jnp.sinc(2.0 * cutoff * offsets) * window
    kernel = kernel / jnp.sum(kernel)
    return kernel[::-1].astype(jnp.bfloat16)


def band_matrix(rows, out_length):
    with jax.ensure_compile_time_eval():
        reversed_taps = np.asarray(lowpass_taps().astype(jnp.float32))
    index = np.arange(rows)[:, None] - 4 * np.arange(out_length)[None, :]
    inside = (index >= 0) & (index < TAPS)
    band = np.where(inside, reversed_taps[np.clip(index, 0, TAPS - 1)], 0.0)
    return jnp.asarray(band.astype(np.float32)).astype(jnp.bfloat16)


def decimate(earlier, recording, out_length):
    head = earlier.shape[1]
    band = band_matrix(head + recording.shape[1], out_length)
    summed = jnp.dot(earlier, band[:head], preferred_element_type=jnp.float32)
    summed = summed + jnp.dot(recording, band[head:], preferred_element_type=jnp.float32)
    return summed.astype(jnp.bfloat16)


def fourier_table():
    with jax.ensure_compile_time_eval():
        sample = jnp.arange(NSEG, dtype=jnp.int32)[:, None]
        frequency = FBASE + jnp.arange(NF, dtype=jnp.int32)[None, :]
        angles = 2.0 * math.pi * (sample * frequency % NSEG).astype(jnp.float32) / NSEG
        table = jnp.concatenate([jnp.cos(angles), -jnp.sin(angles)], axis=1)
        table = np.asarray(table.astype(jnp.bfloat16).astype(jnp.float32))
    return jnp.asarray(table).astype(jnp.bfloat16)


def delay_table():
    with jax.ensure_compile_time_eval():
        frequency = FBASE + jnp.arange(NF, dtype=jnp.int32)[:, None]
        delays = jnp.arange(LAGS, dtype=jnp.int32)[None, :] - LAGS // 2
        angles = 2.0 * math.pi * (frequency * delays % NSEG).astype(jnp.float32) / NSEG
        table = jnp.concatenate([jnp.cos(angles), -jnp.sin(angles)], axis=0)
        table = np.asarray(table.astype(jnp.bfloat16).astype(jnp.float32))
    return jnp.asarray(table).astype(jnp.bfloat16)


def whiten(spectrum):
    real_part = spectrum[:, :NF]
    imag_part = spectrum[:, NF:]
    power = real_part * real_part + imag_part * imag_part
    average = jnp.mean(power, axis=1, keepdims=True)
    factor = lax.rsqrt(power + 0.1 * average + 1e-05)
    return jnp.concatenate([real_part * factor, imag_part * factor], axis=1).astype(jnp.bfloat16)


def correlate_kernel(
    flags_ref, picked_ref, place_ref, lines_ref, table_ref, recv_ref, own_ref, delays_ref, out_ref,
    plain_ref, swapped_ref, source_ref, *cross_refs,
):
    block = out_ref.shape[0]
    receivers = recv_ref.shape[2]
    share = block // len(cross_refs)

    @pl.when(pl.program_id(0) == 0)
    def _():
        lower = lax.broadcasted_iota(jnp.int32, (receivers, 2 * NF), 1) < NF
        own = own_ref[...]
        for w in range(SEGS):
            spectra = recv_ref[w, 0].astype(jnp.float32) * own
            turned = pltpu.roll(spectra, NF, 1)
            plain_ref[w] = jnp.where(lower, spectra, turned)
            swapped_ref[w] = jnp.where(lower, turned, -spectra)

    height = table_ref.shape[1]
    step = pl.program_id(0)

    def select(at, slot):
        start = pl.multiple_of(at * block, block)
        wanted = lines_ref[pl.ds(start, block), :]
        pick = (wanted == lax.broadcasted_iota(jnp.int32, (block, height), 1)).astype(jnp.bfloat16)
        for w in range(SEGS):
            source_ref[slot, w] = jnp.dot(pick, table_ref[w], preferred_element_type=jnp.float32)

    @pl.when(step == 0)
    def _():
        select(0, 0)

    slot = step % 2
    select(jnp.minimum(step + 1, pl.num_programs(0) - 1), 1 - slot)

    for part, cross_ref in enumerate(cross_refs):

        def one_source(s, carry):
            at = part * share + s
            direct = jnp.zeros((receivers, 2 * NF), jnp.float32)
            crossed = jnp.zeros((receivers, 2 * NF), jnp.float32)
            for w in range(SEGS):
                row = source_ref[slot, w, pl.ds(at, 1), :]
                direct = direct + row * plain_ref[w]
                crossed = crossed + row * swapped_ref[w]
            flag = flags_ref[picked_ref[pl.program_id(0) * block + at]].astype(jnp.float32)
            cross = (direct - pltpu.roll(crossed, NF, 1)) * flag
            start = pl.multiple_of(s * receivers, receivers)
            cross_ref[pl.ds(start, receivers), :] = cross.astype(jnp.bfloat16)
            return carry

        lax.fori_loop(0, share, one_source, 0, unroll=True)
        lagged = jnp.dot(cross_ref[...], delays_ref[...], preferred_element_type=jnp.float32)
        lagged = lagged * (1.0 / math.sqrt(SEGS * NF))
        out_ref[part * share : (part + 1) * share] = lagged.astype(jnp.bfloat16).reshape(
            share, receivers, LAGS
        )


def correlate(table, lines, flags_all, picked, place, blocks, own_flags, delays, block=128, parts=4):
    source_count = picked.shape[0]
    recv_count = own_flags.shape[0]
    grid_spec = pltpu.PrefetchScalarGridSpec(
        num_scalar_prefetch=3,
        grid=(source_count // block,),
        in_specs=[
            pl.BlockSpec((source_count, 1), lambda i, f, p, q: (0, 0)),
            pl.BlockSpec(table.shape, lambda i, f, p, q: (0, 0, 0)),
            pl.BlockSpec((SEGS, 1, recv_count, 2 * NF), lambda i, f, p, q: (0, q[0], q[1], 0)),
            pl.BlockSpec((recv_count, 1), lambda i, f, p, q: (0, 0)),
            pl.BlockSpec((2 * NF, LAGS), lambda i, f, p, q: (0, 0)),
        ],
        out_specs=pl.BlockSpec((block, recv_count, LAGS), lambda i, f, p, q: (i, 0, 0)),
        scratch_shapes=[
            pltpu.VMEM((SEGS, recv_count, 2 * NF), jnp.float32),
            pltpu.VMEM((SEGS, recv_count, 2 * NF), jnp.float32),
            pltpu.VMEM((2, SEGS, block, 2 * NF), jnp.float32),
        ]
        + [pltpu.VMEM((block // parts * recv_count, 2 * NF), jnp.bfloat16)] * parts,
    )
    return pl.pallas_call(
        correlate_kernel,
        grid_spec=grid_spec,
        out_shape=jax.ShapeDtypeStruct((source_count, recv_count, LAGS), jnp.bfloat16),
        compiler_params=pltpu.CompilerParams(dimension_semantics=("arbitrary",)),
    )(flags_all, picked, place, lines, table, blocks, own_flags, delays)


def body(recording, source_index, channel_mask):
    channels, raw_count = recording.shape
    devices = lax.axis_size("chan")
    me = lax.axis_index("chan")
    per_device = channels // devices
    dec_length = raw_count // 4
    sharing = devices // SEGS
    span = channels // sharing
    trailing = recording[:, raw_count - (TAPS - 4) :]
    earlier = from_behind(trailing, "chan", 1)
    decimated = decimate(earlier, recording, dec_length)
    slot = me % sharing
    rows = lax.dynamic_slice_in_dim(fourier_table(), slot * dec_length, dec_length, axis=0)
    partial = jnp.dot(decimated, rows, preferred_element_type=jnp.float32)
    pieces = partial.reshape(sharing, span, 2 * NF)
    spectrum = lax.dynamic_index_in_dim(pieces, slot, 0, keepdims=False)
    for step in range(1, sharing):
        route = [
            (group * sharing + i, group * sharing + (i + step) % sharing)
            for group in range(devices // sharing)
            for i in range(sharing)
        ]
        outgoing = lax.dynamic_index_in_dim(pieces, (slot + step) % sharing, 0, keepdims=False)
        spectrum = spectrum + lax.ppermute(outgoing, "chan", route)
    whitened = whiten(spectrum)
    flags = channel_mask.astype(jnp.bfloat16)
    flag_rows = jnp.zeros((16, 2 * NF), jnp.bfloat16).at[0, :per_device].set(flags)
    piece = jnp.concatenate([whitened, flag_rows], axis=0)
    gathered = lax.all_gather(piece, "chan", axis=0, tiled=False)
    height = piece.shape[0]
    blocks = gathered.reshape(SEGS, sharing, height, 2 * NF)
    picked = jnp.clip(source_index, 0, channels - 1)
    table = gathered.reshape(SEGS, sharing * height, 2 * NF)
    line = picked // span * height + picked % span
    flags_all = gathered[:, span, :per_device].reshape(channels).astype(jnp.int32)
    first = me * per_device
    place = jnp.stack([first // span, first % span // per_device]).astype(jnp.int32)
    own_flags = channel_mask.astype(jnp.float32)[:, None]
    result = correlate(table, line[:, None], flags_all, picked, place, blocks, own_flags, delay_table())
    return result.reshape(SOURCES, per_device, LAGS)


def solution(mesh):
    placed = (P("fiber", "chan"), P("fiber"), P(("fiber", "chan")))
    return jax.shard_map(
        body, mesh=mesh, in_specs=placed, out_specs=P("fiber", "chan", None), check_vma=False
    )
```

```python
import math

import jax
import jax.numpy as jnp
import numpy as np
from jax import lax
from jax.experimental import pallas as pl
from jax.experimental.pallas import tpu as pltpu
from jax.sharding import PartitionSpec as P

SEGS = 8
NSEG = 512
NF = 192
FBASE = 4
LAGS = 256
TAPS = 64
SOURCES = 512


def from_behind(block, axis, distance):
    devices = range(lax.axis_size(axis))
    route = [(i - distance, i) for i in devices if i - distance in devices]
    return lax.ppermute(block, axis, route)


def lowpass_taps():
    offsets = jnp.arange(TAPS, dtype=jnp.float32) - (TAPS - 1) / 2.0
    cutoff = 0.1
    window = 0.5 - 0.5 * jnp.cos(2.0 * math.pi * (jnp.arange(TAPS, dtype=jnp.float32) + 0.5) / TAPS)
    kernel = 2.0 * cutoff * jnp.sinc(2.0 * cutoff * offsets) * window
    kernel = kernel / jnp.sum(kernel)
    return kernel[::-1].astype(jnp.bfloat16)


def band_matrix(rows, out_length):
    with jax.ensure_compile_time_eval():
        reversed_taps = np.asarray(lowpass_taps().astype(jnp.float32))
    index = np.arange(rows)[:, None] - 4 * np.arange(out_length)[None, :]
    inside = (index >= 0) & (index < TAPS)
    band = np.where(inside, reversed_taps[np.clip(index, 0, TAPS - 1)], 0.0)
    return jnp.asarray(band.astype(np.float32)).astype(jnp.bfloat16)


def decimate(earlier, recording, out_length):
    head = earlier.shape[1]
    band = band_matrix(head + recording.shape[1], out_length)
    summed = jnp.dot(earlier, band[:head], preferred_element_type=jnp.float32)
    summed = summed + jnp.dot(recording, band[head:], preferred_element_type=jnp.float32)
    return summed.astype(jnp.bfloat16)


def fourier_table():
    with jax.ensure_compile_time_eval():
        sample = jnp.arange(NSEG, dtype=jnp.int32)[:, None]
        frequency = FBASE + jnp.arange(NF, dtype=jnp.int32)[None, :]
        angles = 2.0 * math.pi * (sample * frequency % NSEG).astype(jnp.float32) / NSEG
        table = jnp.concatenate([jnp.cos(angles), -jnp.sin(angles)], axis=1)
        table = np.asarray(table.astype(jnp.bfloat16).astype(jnp.float32))
    return jnp.asarray(table).astype(jnp.bfloat16)


def delay_table():
    with jax.ensure_compile_time_eval():
        frequency = FBASE + jnp.arange(NF, dtype=jnp.int32)[:, None]
        delays = jnp.arange(LAGS, dtype=jnp.int32)[None, :] - LAGS // 2
        angles = 2.0 * math.pi * (frequency * delays % NSEG).astype(jnp.float32) / NSEG
        table = jnp.concatenate([jnp.cos(angles), -jnp.sin(angles)], axis=0)
        table = np.asarray(table.astype(jnp.bfloat16).astype(jnp.float32))
    return jnp.asarray(table).astype(jnp.bfloat16)


def whiten(spectrum):
    real_part = spectrum[:, :NF]
    imag_part = spectrum[:, NF:]
    power = real_part * real_part + imag_part * imag_part
    average = jnp.mean(power, axis=1, keepdims=True)
    factor = lax.rsqrt(power + 0.1 * average + 1e-05)
    return jnp.concatenate([real_part * factor, imag_part * factor], axis=1).astype(jnp.bfloat16)


def correlate_kernel(
    flags_ref, picked_ref, place_ref, lines_ref, table_ref, recv_ref, own_ref, delays_ref, out_ref,
    plain_ref, swapped_ref, source_ref, *cross_refs,
):
    block = out_ref.shape[0]
    receivers = recv_ref.shape[2]
    share = block // len(cross_refs)

    @pl.when(pl.program_id(0) == 0)
    def _():
        lower = lax.broadcasted_iota(jnp.int32, (receivers, 2 * NF), 1) < NF
        own = own_ref[...]
        for w in range(SEGS):
            spectra = recv_ref[w, 0].astype(jnp.float32) * own
            turned = pltpu.roll(spectra, NF, 1)
            plain_ref[w] = jnp.where(lower, spectra, turned)
            swapped_ref[w] = jnp.where(lower, turned, -spectra)

    height = table_ref.shape[1]
    step = pl.program_id(0)

    def select(at, slot):
        start = pl.multiple_of(at * block, block)
        wanted = lines_ref[pl.ds(start, block), :]
        pick = (wanted == lax.broadcasted_iota(jnp.int32, (block, height), 1)).astype(jnp.bfloat16)
        for w in range(SEGS):
            source_ref[slot, w] = jnp.dot(pick, table_ref[w], preferred_element_type=jnp.float32)

    @pl.when(step == 0)
    def _():
        select(0, 0)

    slot = step % 2
    select(jnp.minimum(step + 1, pl.num_programs(0) - 1), 1 - slot)

    for part, cross_ref in enumerate(cross_refs):

        def one_source(s, carry):
            at = part * share + s
            direct = jnp.zeros((receivers, 2 * NF), jnp.float32)
            crossed = jnp.zeros((receivers, 2 * NF), jnp.float32)
            for w in range(SEGS):
                row = source_ref[slot, w, pl.ds(at, 1), :]
                direct = direct + row * plain_ref[w]
                crossed = crossed + row * swapped_ref[w]
            flag = flags_ref[picked_ref[pl.program_id(0) * block + at]].astype(jnp.float32)
            cross = (direct - pltpu.roll(crossed, NF, 1)) * flag
            start = pl.multiple_of(s * receivers, receivers)
            cross_ref[pl.ds(start, receivers), :] = cross.astype(jnp.bfloat16)
            return carry

        lax.fori_loop(0, share, one_source, 0, unroll=True)
        lagged = jnp.dot(cross_ref[...], delays_ref[...], preferred_element_type=jnp.float32)
        lagged = lagged * (1.0 / math.sqrt(SEGS * NF))
        out_ref[part * share : (part + 1) * share] = lagged.astype(jnp.bfloat16).reshape(
            share, receivers, LAGS
        )


def correlate(table, lines, flags_all, picked, place, blocks, own_flags, delays, block=128, parts=8):
    source_count = picked.shape[0]
    recv_count = own_flags.shape[0]
    grid_spec = pltpu.PrefetchScalarGridSpec(
        num_scalar_prefetch=3,
        grid=(source_count // block,),
        in_specs=[
            pl.BlockSpec((source_count, 1), lambda i, f, p, q: (0, 0)),
            pl.BlockSpec(table.shape, lambda i, f, p, q: (0, 0, 0)),
            pl.BlockSpec((SEGS, 1, recv_count, 2 * NF), lambda i, f, p, q: (0, q[0], q[1], 0)),
            pl.BlockSpec((recv_count, 1), lambda i, f, p, q: (0, 0)),
            pl.BlockSpec((2 * NF, LAGS), lambda i, f, p, q: (0, 0)),
        ],
        out_specs=pl.BlockSpec((block, recv_count, LAGS), lambda i, f, p, q: (i, 0, 0)),
        scratch_shapes=[
            pltpu.VMEM((SEGS, recv_count, 2 * NF), jnp.float32),
            pltpu.VMEM((SEGS, recv_count, 2 * NF), jnp.float32),
            pltpu.VMEM((2, SEGS, block, 2 * NF), jnp.float32),
        ]
        + [pltpu.VMEM((block // parts * recv_count, 2 * NF), jnp.bfloat16)] * parts,
    )
    return pl.pallas_call(
        correlate_kernel,
        grid_spec=grid_spec,
        out_shape=jax.ShapeDtypeStruct((source_count, recv_count, LAGS), jnp.bfloat16),
        compiler_params=pltpu.CompilerParams(dimension_semantics=("arbitrary",)),
    )(flags_all, picked, place, lines, table, blocks, own_flags, delays)


def body(recording, source_index, channel_mask):
    channels, raw_count = recording.shape
    devices = lax.axis_size("chan")
    me = lax.axis_index("chan")
    per_device = channels // devices
    dec_length = raw_count // 4
    sharing = devices // SEGS
    span = channels // sharing
    trailing = recording[:, raw_count - (TAPS - 4) :]
    earlier = from_behind(trailing, "chan", 1)
    decimated = decimate(earlier, recording, dec_length)
    slot = me % sharing
    rows = lax.dynamic_slice_in_dim(fourier_table(), slot * dec_length, dec_length, axis=0)
    partial = jnp.dot(decimated, rows, preferred_element_type=jnp.float32)
    pieces = partial.reshape(sharing, span, 2 * NF)
    spectrum = lax.dynamic_index_in_dim(pieces, slot, 0, keepdims=False)
    for step in range(1, sharing):
        route = [
            (group * sharing + i, group * sharing + (i + step) % sharing)
            for group in range(devices // sharing)
            for i in range(sharing)
        ]
        outgoing = lax.dynamic_index_in_dim(pieces, (slot + step) % sharing, 0, keepdims=False)
        spectrum = spectrum + lax.ppermute(outgoing, "chan", route)
    whitened = whiten(spectrum)
    flags = channel_mask.astype(jnp.bfloat16)
    flag_rows = jnp.zeros((16, 2 * NF), jnp.bfloat16).at[0, :per_device].set(flags)
    piece = jnp.concatenate([whitened, flag_rows], axis=0)
    gathered = lax.all_gather(piece, "chan", axis=0, tiled=False)
    height = piece.shape[0]
    blocks = gathered.reshape(SEGS, sharing, height, 2 * NF)
    picked = jnp.clip(source_index, 0, channels - 1)
    table = gathered.reshape(SEGS, sharing * height, 2 * NF)
    line = picked // span * height + picked % span
    flags_all = gathered[:, span, :per_device].reshape(channels).astype(jnp.int32)
    first = me * per_device
    place = jnp.stack([first // span, first % span // per_device]).astype(jnp.int32)
    own_flags = channel_mask.astype(jnp.float32)[:, None]
    result = correlate(table, line[:, None], flags_all, picked, place, blocks, own_flags, delay_table())
    return result.reshape(SOURCES, per_device, LAGS)


def solution(mesh):
    placed = (P("fiber", "chan"), P("fiber"), P(("fiber", "chan")))
    return jax.shard_map(
        body, mesh=mesh, in_specs=placed, out_specs=P("fiber", "chan", None), check_vma=False
    )
```

```python
import math

import jax
import jax.numpy as jnp
import numpy as np
from jax import lax
from jax.experimental import pallas as pl
from jax.experimental.pallas import tpu as pltpu
from jax.sharding import PartitionSpec as P

SEGS = 8
NSEG = 512
NF = 192
FBASE = 4
LAGS = 256
TAPS = 64
SOURCES = 512


def from_behind(block, axis, distance):
    devices = range(lax.axis_size(axis))
    route = [(i - distance, i) for i in devices if i - distance in devices]
    return lax.ppermute(block, axis, route)


def lowpass_taps():
    offsets = jnp.arange(TAPS, dtype=jnp.float32) - (TAPS - 1) / 2.0
    cutoff = 0.1
    window = 0.5 - 0.5 * jnp.cos(2.0 * math.pi * (jnp.arange(TAPS, dtype=jnp.float32) + 0.5) / TAPS)
    kernel = 2.0 * cutoff * jnp.sinc(2.0 * cutoff * offsets) * window
    kernel = kernel / jnp.sum(kernel)
    return kernel[::-1].astype(jnp.bfloat16)


def band_matrix(rows, out_length):
    with jax.ensure_compile_time_eval():
        reversed_taps = np.asarray(lowpass_taps().astype(jnp.float32))
    index = np.arange(rows)[:, None] - 4 * np.arange(out_length)[None, :]
    inside = (index >= 0) & (index < TAPS)
    band = np.where(inside, reversed_taps[np.clip(index, 0, TAPS - 1)], 0.0)
    return jnp.asarray(band.astype(np.float32)).astype(jnp.bfloat16)


def decimate(earlier, recording, out_length):
    head = earlier.shape[1]
    band = band_matrix(head + recording.shape[1], out_length)
    summed = jnp.dot(earlier, band[:head], preferred_element_type=jnp.float32)
    summed = summed + jnp.dot(recording, band[head:], preferred_element_type=jnp.float32)
    return summed.astype(jnp.bfloat16)


def fourier_table():
    with jax.ensure_compile_time_eval():
        sample = jnp.arange(NSEG, dtype=jnp.int32)[:, None]
        frequency = FBASE + jnp.arange(NF, dtype=jnp.int32)[None, :]
        angles = 2.0 * math.pi * (sample * frequency % NSEG).astype(jnp.float32) / NSEG
        table = jnp.concatenate([jnp.cos(angles), -jnp.sin(angles)], axis=1)
        table = np.asarray(table.astype(jnp.bfloat16).astype(jnp.float32))
    return jnp.asarray(table).astype(jnp.bfloat16)


def delay_table():
    with jax.ensure_compile_time_eval():
        frequency = FBASE + jnp.arange(NF, dtype=jnp.int32)[:, None]
        delays = jnp.arange(LAGS, dtype=jnp.int32)[None, :] - LAGS // 2
        angles = 2.0 * math.pi * (frequency * delays % NSEG).astype(jnp.float32) / NSEG
        table = jnp.concatenate([jnp.cos(angles), -jnp.sin(angles)], axis=0)
        table = np.asarray(table.astype(jnp.bfloat16).astype(jnp.float32))
    return jnp.asarray(table).astype(jnp.bfloat16)


def whiten(spectrum):
    real_part = spectrum[:, :NF]
    imag_part = spectrum[:, NF:]
    power = real_part * real_part + imag_part * imag_part
    average = jnp.mean(power, axis=1, keepdims=True)
    factor = lax.rsqrt(power + 0.1 * average + 1e-05)
    return jnp.concatenate([real_part * factor, imag_part * factor], axis=1).astype(jnp.bfloat16)


def correlate_kernel(
    flags_ref, picked_ref, place_ref, lines_ref, table_ref, recv_ref, own_ref, delays_ref, out_ref,
    plain_ref, swapped_ref, source_ref, *cross_refs,
):
    block = out_ref.shape[0]
    receivers = recv_ref.shape[2]
    share = block // len(cross_refs)

    @pl.when(pl.program_id(0) == 0)
    def _():
        lower = lax.broadcasted_iota(jnp.int32, (receivers, 2 * NF), 1) < NF
        own = own_ref[...]
        for w in range(SEGS):
            spectra = recv_ref[w, 0].astype(jnp.float32) * own
            turned = pltpu.roll(spectra, NF, 1)
            plain_ref[w] = jnp.where(lower, spectra, turned)
            swapped_ref[w] = jnp.where(lower, turned, -spectra)

    height = table_ref.shape[1]
    step = pl.program_id(0)

    def select(at, slot):
        start = pl.multiple_of(at * block, block)
        wanted = lines_ref[pl.ds(start, block), :]
        pick = (wanted == lax.broadcasted_iota(jnp.int32, (block, height), 1)).astype(jnp.bfloat16)
        for w in range(SEGS):
            source_ref[slot, w] = jnp.dot(pick, table_ref[w], preferred_element_type=jnp.float32)

    @pl.when(step == 0)
    def _():
        select(0, 0)

    slot = step % 2
    select(jnp.minimum(step + 1, pl.num_programs(0) - 1), 1 - slot)

    for part, cross_ref in enumerate(cross_refs):

        def one_source(s, carry):
            at = part * share + s
            direct = jnp.zeros((receivers, 2 * NF), jnp.float32)
            crossed = jnp.zeros((receivers, 2 * NF), jnp.float32)
            for w in range(SEGS):
                row = source_ref[slot, w, pl.ds(at, 1), :]
                direct = direct + row * plain_ref[w]
                crossed = crossed + row * swapped_ref[w]
            flag = flags_ref[picked_ref[pl.program_id(0) * block + at]].astype(jnp.float32)
            cross = (direct - pltpu.roll(crossed, NF, 1)) * flag
            start = pl.multiple_of(s * receivers, receivers)
            cross_ref[pl.ds(start, receivers), :] = cross.astype(jnp.bfloat16)
            return carry

        lax.fori_loop(0, share, one_source, 0, unroll=True)
        lagged = jnp.dot(cross_ref[...], delays_ref[...], preferred_element_type=jnp.float32)
        lagged = lagged * (1.0 / math.sqrt(SEGS * NF))
        out_ref[part * share : (part + 1) * share] = lagged.astype(jnp.bfloat16).reshape(
            share, receivers, LAGS
        )


def correlate(table, lines, flags_all, picked, place, blocks, own_flags, delays, block=128, parts=16):
    source_count = picked.shape[0]
    recv_count = own_flags.shape[0]
    grid_spec = pltpu.PrefetchScalarGridSpec(
        num_scalar_prefetch=3,
        grid=(source_count // block,),
        in_specs=[
            pl.BlockSpec((source_count, 1), lambda i, f, p, q: (0, 0)),
            pl.BlockSpec(table.shape, lambda i, f, p, q: (0, 0, 0)),
            pl.BlockSpec((SEGS, 1, recv_count, 2 * NF), lambda i, f, p, q: (0, q[0], q[1], 0)),
            pl.BlockSpec((recv_count, 1), lambda i, f, p, q: (0, 0)),
            pl.BlockSpec((2 * NF, LAGS), lambda i, f, p, q: (0, 0)),
        ],
        out_specs=pl.BlockSpec((block, recv_count, LAGS), lambda i, f, p, q: (i, 0, 0)),
        scratch_shapes=[
            pltpu.VMEM((SEGS, recv_count, 2 * NF), jnp.float32),
            pltpu.VMEM((SEGS, recv_count, 2 * NF), jnp.float32),
            pltpu.VMEM((2, SEGS, block, 2 * NF), jnp.float32),
        ]
        + [pltpu.VMEM((block // parts * recv_count, 2 * NF), jnp.bfloat16)] * parts,
    )
    return pl.pallas_call(
        correlate_kernel,
        grid_spec=grid_spec,
        out_shape=jax.ShapeDtypeStruct((source_count, recv_count, LAGS), jnp.bfloat16),
        compiler_params=pltpu.CompilerParams(dimension_semantics=("arbitrary",)),
    )(flags_all, picked, place, lines, table, blocks, own_flags, delays)


def body(recording, source_index, channel_mask):
    channels, raw_count = recording.shape
    devices = lax.axis_size("chan")
    me = lax.axis_index("chan")
    per_device = channels // devices
    dec_length = raw_count // 4
    sharing = devices // SEGS
    span = channels // sharing
    trailing = recording[:, raw_count - (TAPS - 4) :]
    earlier = from_behind(trailing, "chan", 1)
    decimated = decimate(earlier, recording, dec_length)
    slot = me % sharing
    rows = lax.dynamic_slice_in_dim(fourier_table(), slot * dec_length, dec_length, axis=0)
    partial = jnp.dot(decimated, rows, preferred_element_type=jnp.float32)
    pieces = partial.reshape(sharing, span, 2 * NF)
    spectrum = lax.dynamic_index_in_dim(pieces, slot, 0, keepdims=False)
    for step in range(1, sharing):
        route = [
            (group * sharing + i, group * sharing + (i + step) % sharing)
            for group in range(devices // sharing)
            for i in range(sharing)
        ]
        outgoing = lax.dynamic_index_in_dim(pieces, (slot + step) % sharing, 0, keepdims=False)
        spectrum = spectrum + lax.ppermute(outgoing, "chan", route)
    whitened = whiten(spectrum)
    flags = channel_mask.astype(jnp.bfloat16)
    flag_rows = jnp.zeros((16, 2 * NF), jnp.bfloat16).at[0, :per_device].set(flags)
    piece = jnp.concatenate([whitened, flag_rows], axis=0)
    gathered = lax.all_gather(piece, "chan", axis=0, tiled=False)
    height = piece.shape[0]
    blocks = gathered.reshape(SEGS, sharing, height, 2 * NF)
    picked = jnp.clip(source_index, 0, channels - 1)
    table = gathered.reshape(SEGS, sharing * height, 2 * NF)
    line = picked // span * height + picked % span
    flags_all = gathered[:, span, :per_device].reshape(channels).astype(jnp.int32)
    first = me * per_device
    place = jnp.stack([first // span, first % span // per_device]).astype(jnp.int32)
    own_flags = channel_mask.astype(jnp.float32)[:, None]
    result = correlate(table, line[:, None], flags_all, picked, place, blocks, own_flags, delay_table())
    return result.reshape(SOURCES, per_device, LAGS)


def solution(mesh):
    placed = (P("fiber", "chan"), P("fiber"), P(("fiber", "chan")))
    return jax.shard_map(
        body, mesh=mesh, in_specs=placed, out_specs=P("fiber", "chan", None), check_vma=False
    )
```

```python
import math

import jax
import jax.numpy as jnp
import numpy as np
from jax import lax
from jax.experimental import pallas as pl
from jax.experimental.pallas import tpu as pltpu
from jax.sharding import PartitionSpec as P

SEGS = 8
NSEG = 512
NF = 192
FBASE = 4
LAGS = 256
TAPS = 64
SOURCES = 512


def from_behind(block, axis, distance):
    devices = range(lax.axis_size(axis))
    route = [(i - distance, i) for i in devices if i - distance in devices]
    return lax.ppermute(block, axis, route)


def lowpass_taps():
    offsets = jnp.arange(TAPS, dtype=jnp.float32) - (TAPS - 1) / 2.0
    cutoff = 0.1
    window = 0.5 - 0.5 * jnp.cos(2.0 * math.pi * (jnp.arange(TAPS, dtype=jnp.float32) + 0.5) / TAPS)
    kernel = 2.0 * cutoff * jnp.sinc(2.0 * cutoff * offsets) * window
    kernel = kernel / jnp.sum(kernel)
    return kernel[::-1].astype(jnp.bfloat16)


def band_matrix(rows, out_length):
    with jax.ensure_compile_time_eval():
        reversed_taps = np.asarray(lowpass_taps().astype(jnp.float32))
    index = np.arange(rows)[:, None] - 4 * np.arange(out_length)[None, :]
    inside = (index >= 0) & (index < TAPS)
    band = np.where(inside, reversed_taps[np.clip(index, 0, TAPS - 1)], 0.0)
    return jnp.asarray(band.astype(np.float32)).astype(jnp.bfloat16)


def decimate(earlier, recording, out_length):
    head = earlier.shape[1]
    band = band_matrix(head + recording.shape[1], out_length)
    summed = jnp.dot(earlier, band[:head], preferred_element_type=jnp.float32)
    summed = summed + jnp.dot(recording, band[head:], preferred_element_type=jnp.float32)
    return summed.astype(jnp.bfloat16)


def fourier_table():
    with jax.ensure_compile_time_eval():
        sample = jnp.arange(NSEG, dtype=jnp.int32)[:, None]
        frequency = FBASE + jnp.arange(NF, dtype=jnp.int32)[None, :]
        angles = 2.0 * math.pi * (sample * frequency % NSEG).astype(jnp.float32) / NSEG
        table = jnp.concatenate([jnp.cos(angles), -jnp.sin(angles)], axis=1)
        table = np.asarray(table.astype(jnp.bfloat16).astype(jnp.float32))
    return jnp.asarray(table).astype(jnp.bfloat16)


def delay_table():
    with jax.ensure_compile_time_eval():
        frequency = FBASE + jnp.arange(NF, dtype=jnp.int32)[:, None]
        delays = jnp.arange(LAGS, dtype=jnp.int32)[None, :] - LAGS // 2
        angles = 2.0 * math.pi * (frequency * delays % NSEG).astype(jnp.float32) / NSEG
        table = jnp.concatenate([jnp.cos(angles), -jnp.sin(angles)], axis=0)
        table = np.asarray(table.astype(jnp.bfloat16).astype(jnp.float32))
    return jnp.asarray(table).astype(jnp.bfloat16)


def whiten(spectrum):
    real_part = spectrum[:, :NF]
    imag_part = spectrum[:, NF:]
    power = real_part * real_part + imag_part * imag_part
    average = jnp.mean(power, axis=1, keepdims=True)
    factor = lax.rsqrt(power + 0.1 * average + 1e-05)
    return jnp.concatenate([real_part * factor, imag_part * factor], axis=1).astype(jnp.bfloat16)


def correlate_kernel(
    flags_ref, picked_ref, place_ref, lines_ref, table_ref, recv_ref, own_ref, delays_ref, out_ref,
    plain_ref, swapped_ref, source_ref, *cross_refs,
):
    block = out_ref.shape[0]
    receivers = recv_ref.shape[2]
    share = block // len(cross_refs)

    @pl.when(pl.program_id(0) == 0)
    def _():
        lower = lax.broadcasted_iota(jnp.int32, (receivers, 2 * NF), 1) < NF
        own = own_ref[...]
        for w in range(SEGS):
            spectra = recv_ref[w, 0].astype(jnp.float32) * own
            turned = pltpu.roll(spectra, NF, 1)
            plain_ref[w] = jnp.where(lower, spectra, turned)
            swapped_ref[w] = jnp.where(lower, turned, -spectra)

    height = table_ref.shape[1]
    step = pl.program_id(0)

    def select(at, slot):
        start = pl.multiple_of(at * block, block)
        wanted = lines_ref[pl.ds(start, block), :]
        pick = (wanted == lax.broadcasted_iota(jnp.int32, (block, height), 1)).astype(jnp.bfloat16)
        for w in range(SEGS):
            source_ref[slot, w] = jnp.dot(pick, table_ref[w], preferred_element_type=jnp.float32)

    @pl.when(step == 0)
    def _():
        select(0, 0)

    slot = step % 2
    select(jnp.minimum(step + 1, pl.num_programs(0) - 1), 1 - slot)

    for part, cross_ref in enumerate(cross_refs):

        def one_source(s, carry):
            at = part * share + s
            direct = jnp.zeros((receivers, 2 * NF), jnp.float32)
            crossed = jnp.zeros((receivers, 2 * NF), jnp.float32)
            for w in range(SEGS):
                row = source_ref[slot, w, pl.ds(at, 1), :]
                direct = direct + row * plain_ref[w]
                crossed = crossed + row * swapped_ref[w]
            flag = flags_ref[picked_ref[pl.program_id(0) * block + at]].astype(jnp.float32)
            cross = (direct - pltpu.roll(crossed, NF, 1)) * flag
            start = pl.multiple_of(s * receivers, receivers)
            cross_ref[pl.ds(start, receivers), :] = cross.astype(jnp.bfloat16)
            return carry

        lax.fori_loop(0, share, one_source, 0, unroll=True)
        lagged = jnp.dot(cross_ref[...], delays_ref[...], preferred_element_type=jnp.float32)
        lagged = lagged * (1.0 / math.sqrt(SEGS * NF))
        out_ref[part * share : (part + 1) * share] = lagged.astype(jnp.bfloat16).reshape(
            share, receivers, LAGS
        )


def correlate(table, lines, flags_all, picked, place, blocks, own_flags, delays, block=128, parts=32):
    source_count = picked.shape[0]
    recv_count = own_flags.shape[0]
    grid_spec = pltpu.PrefetchScalarGridSpec(
        num_scalar_prefetch=3,
        grid=(source_count // block,),
        in_specs=[
            pl.BlockSpec((source_count, 1), lambda i, f, p, q: (0, 0)),
            pl.BlockSpec(table.shape, lambda i, f, p, q: (0, 0, 0)),
            pl.BlockSpec((SEGS, 1, recv_count, 2 * NF), lambda i, f, p, q: (0, q[0], q[1], 0)),
            pl.BlockSpec((recv_count, 1), lambda i, f, p, q: (0, 0)),
            pl.BlockSpec((2 * NF, LAGS), lambda i, f, p, q: (0, 0)),
        ],
        out_specs=pl.BlockSpec((block, recv_count, LAGS), lambda i, f, p, q: (i, 0, 0)),
        scratch_shapes=[
            pltpu.VMEM((SEGS, recv_count, 2 * NF), jnp.float32),
            pltpu.VMEM((SEGS, recv_count, 2 * NF), jnp.float32),
            pltpu.VMEM((2, SEGS, block, 2 * NF), jnp.float32),
        ]
        + [pltpu.VMEM((block // parts * recv_count, 2 * NF), jnp.bfloat16)] * parts,
    )
    return pl.pallas_call(
        correlate_kernel,
        grid_spec=grid_spec,
        out_shape=jax.ShapeDtypeStruct((source_count, recv_count, LAGS), jnp.bfloat16),
        compiler_params=pltpu.CompilerParams(dimension_semantics=("arbitrary",)),
    )(flags_all, picked, place, lines, table, blocks, own_flags, delays)


def body(recording, source_index, channel_mask):
    channels, raw_count = recording.shape
    devices = lax.axis_size("chan")
    me = lax.axis_index("chan")
    per_device = channels // devices
    dec_length = raw_count // 4
    sharing = devices // SEGS
    span = channels // sharing
    trailing = recording[:, raw_count - (TAPS - 4) :]
    earlier = from_behind(trailing, "chan", 1)
    decimated = decimate(earlier, recording, dec_length)
    slot = me % sharing
    rows = lax.dynamic_slice_in_dim(fourier_table(), slot * dec_length, dec_length, axis=0)
    partial = jnp.dot(decimated, rows, preferred_element_type=jnp.float32)
    pieces = partial.reshape(sharing, span, 2 * NF)
    spectrum = lax.dynamic_index_in_dim(pieces, slot, 0, keepdims=False)
    for step in range(1, sharing):
        route = [
            (group * sharing + i, group * sharing + (i + step) % sharing)
            for group in range(devices // sharing)
            for i in range(sharing)
        ]
        outgoing = lax.dynamic_index_in_dim(pieces, (slot + step) % sharing, 0, keepdims=False)
        spectrum = spectrum + lax.ppermute(outgoing, "chan", route)
    whitened = whiten(spectrum)
    flags = channel_mask.astype(jnp.bfloat16)
    flag_rows = jnp.zeros((16, 2 * NF), jnp.bfloat16).at[0, :per_device].set(flags)
    piece = jnp.concatenate([whitened, flag_rows], axis=0)
    gathered = lax.all_gather(piece, "chan", axis=0, tiled=False)
    height = piece.shape[0]
    blocks = gathered.reshape(SEGS, sharing, height, 2 * NF)
    picked = jnp.clip(source_index, 0, channels - 1)
    table = gathered.reshape(SEGS, sharing * height, 2 * NF)
    line = picked // span * height + picked % span
    flags_all = gathered[:, span, :per_device].reshape(channels).astype(jnp.int32)
    first = me * per_device
    place = jnp.stack([first // span, first % span // per_device]).astype(jnp.int32)
    own_flags = channel_mask.astype(jnp.float32)[:, None]
    result = correlate(table, line[:, None], flags_all, picked, place, blocks, own_flags, delay_table())
    return result.reshape(SOURCES, per_device, LAGS)


def solution(mesh):
    placed = (P("fiber", "chan"), P("fiber"), P(("fiber", "chan")))
    return jax.shard_map(
        body, mesh=mesh, in_specs=placed, out_specs=P("fiber", "chan", None), check_vma=False
    )
```
